32 devices in a mesh: groups: 2 (over x), ctx: 16 (over z, y, core).
Axes of the slice: x: 2, y: 2, z: 4, core: 2. Of those that a mesh axis runs over, the one named last changes fastest.
Arguments:
- query_proj: bfloat16 [4096, 4096], P(('groups', 'ctx')), parts along dimension 0, may hold values from -6 to 6
- key_proj: bfloat16 [4096, 4096], P(('groups', 'ctx')), parts along dimension 0, may hold values from -6 to 6
- value_proj: bfloat16 [4096, 4096], P(('groups', 'ctx')), parts along dimension 0, may hold values from -6 to 6
- out_grad: bfloat16 [4096, 4096], P(('groups', 'ctx')), parts along dimension 0, may hold values from -6 to 6
- decay_rate: float32 [256, 16], replicated, may hold values from 0 to 0.034, as said below
- residue: float32 [256, 16], replicated, may hold values from -0.3 to 0.3
- group_of: int32 [4096], replicated, may hold values from 0 to 255, as said below
Outputs:
- hyena_out: bfloat16 [4096, 4096], P(('groups', 'ctx')), parts along dimension 0
- query_grad: bfloat16 [4096, 4096], P(('groups', 'ctx')), parts along dimension 0
- key_grad: bfloat16 [4096, 4096], P(('groups', 'ctx')), parts along dimension 0
- value_grad: bfloat16 [4096, 4096], P(('groups', 'ctx')), parts along dimension 0
- filter_update: float32 [512, 16], P('groups'), parts along dimension 0
The draws below stay inside these ranges and needn't reach their ends.
There are 2 independent parts, one for each index of `groups`. The reference program is written for one: setup_inputs(seed, part) draws one part's arguments, and reference() takes and returns one part's arrays. A program takes and returns all parts, laid end to end along the dimension named above; an argument that names none is the same for every part. Nothing has to cross between parts.
Inputs may be any that keep to these rules, and one draw needn't show every extreme that they name: `group_of`: each of the 256 filter groups holds exactly 16 channels. `decay_rate`: positive rates.
All inputs are finite; a program needn't handle non-finite values.
Results may differ from the reference program's by a relative error of at most 0.005.
Values sent between devices are 32-bit elements; how exact they have to be, the bound alone decides.
No kernel may reach another device: no remote copies, remote signals or barrier semaphores. Data moves between devices by JAX's collectives and lax.ppermute only.
A program may use at most 192 MiB of HBM per device.

```python
import jax
import jax.numpy as jnp
from jax import lax

D = 4096
CPG = 16
S = 16
G = 256
SEQ = 2048


def rates_from(key):
    base = jax.random.fold_in(key, 11)
    first, second, third = jax.random.split(base, 3)
    slow_low = jnp.log(0.2 / SEQ)
    slow_high = jnp.log(2.0 / SEQ)
    fast_high = jnp.log(1.0 / 30.0)
    share = 0.5
    picked = jax.random.uniform(first, (G, S), jnp.float32) < share
    slow_rate = jnp.exp(jax.random.uniform(second, (G, S), jnp.float32, slow_low, slow_high))
    fast_rate = jnp.exp(jax.random.uniform(third, (G, S), jnp.float32, slow_high, fast_high))
    return jnp.where(picked, slow_rate, fast_rate).astype(jnp.float32)


def draw_decay_rate(key, part):
    return rates_from(key)


def draw_residue(key, part):
    rates = rates_from(key)
    noise = jnp.clip(jax.random.normal(jax.random.fold_in(key, 12), (G, S), jnp.float32), -4.0, 4.0)
    return (noise * jnp.sqrt(1.0 - jnp.exp(-2.0 * rates)) * 0.25).astype(jnp.float32)


def draw_group_of(key, part):
    shuffled = jax.random.permutation(jax.random.fold_in(key, 13), D)
    return (shuffled // CPG).astype(jnp.int32)


def levels(key, dims, pieces, low, top_value):
    loudness, own = 1.0, jax.random.fold_in(key, 6)
    for position, blocks in pieces:
        heights = jnp.exp(jax.random.uniform(jax.random.fold_in(own, position), (blocks,), jnp.float32, low / len(pieces), top_value / len(pieces)))
        loudness = loudness * jnp.repeat(heights, dims[position] // blocks).reshape([-1 if axis == position else 1 for axis in range(len(dims))])
    return loudness


def bell_draw(stream_key, dims, scale, reach, shards=(), kind=jnp.bfloat16):
    loudness = levels(stream_key, dims, shards, -0.22, 0.18) if shards else 1.0
    drawn = jax.random.normal(stream_key, dims, jnp.float32) * scale * loudness
    return jnp.minimum(jnp.maximum(drawn, -reach), reach).astype(kind)


def setup_inputs(seed: int = 0, part: int = 0) -> dict:
    splits = jax.random.split(jax.random.key(seed), 8)
    part_keys = jax.random.split(jax.random.fold_in(splits[7], part), 8)
    return {
        "query_proj": bell_draw(part_keys[0], (SEQ, D), 1.0, 6.0, ((0, 16),)),
        "key_proj": bell_draw(part_keys[1], (SEQ, D), 1.0, 6.0, ((0, 16),)),
        "value_proj": bell_draw(part_keys[2], (SEQ, D), 1.0, 6.0, ((0, 16),)),
        "out_grad": bell_draw(part_keys[3], (SEQ, D), 1.0, 6.0, ((0, 16),)),
        "decay_rate": draw_decay_rate(jax.random.fold_in(splits[7], 71), part),
        "residue": draw_residue(jax.random.fold_in(splits[7], 71), part),
        "group_of": draw_group_of(jax.random.fold_in(splits[7], 71), part),
    }


def reference(query_proj, key_proj, value_proj, out_grad, decay_rate, residue, group_of):
    high = lax.Precision.HIGHEST
    query_f = query_proj.astype(jnp.float32)
    key_f = key_proj.astype(jnp.float32)
    value_f = value_proj.astype(jnp.float32)
    grad_f = out_grad.astype(jnp.float32)
    mixed = (key_f * value_f).astype(jnp.bfloat16)
    mixed = lax.optimization_barrier(mixed).astype(jnp.float32)
    upstream = grad_f * query_f
    member = (group_of[:, None] == jnp.arange(G, dtype=jnp.int32)[None, :]).astype(jnp.float32)
    rate_channel = jnp.dot(member, decay_rate, precision=high)
    residue_channel = jnp.dot(member, residue, precision=high)
    factor = jnp.exp(-rate_channel)
    empty = jnp.zeros(rate_channel.shape, jnp.float32)

    def forward_step(carry, inputs):
        state, total = carry
        mixed_row, upstream_row = inputs
        state = factor * state + mixed_row[:, None]
        total = total + upstream_row[:, None] * state
        return ((state, total), lax.optimization_barrier(jnp.sum(residue_channel * state, axis=1)))
    (final_state, total), filtered = lax.scan(forward_step, (empty, empty), (mixed, upstream))

    def backward_step(state, upstream_row):
        state = factor * state + upstream_row[:, None]
        return (state, lax.optimization_barrier(jnp.sum(residue_channel * state, axis=1)))
    final_adjoint, mixed_grad = lax.scan(backward_step, empty, upstream, reverse=True)
    filter_grad = jnp.dot(member.T, total, precision=high)
    filter_update = filter_grad / jnp.sqrt(jnp.mean(filter_grad * filter_grad) + 1e-06)
    hyena_out = (query_f * filtered).astype(jnp.bfloat16)
    query_grad = (grad_f * filtered).astype(jnp.bfloat16)
    key_grad = (mixed_grad * value_f).astype(jnp.bfloat16)
    value_grad = (mixed_grad * key_f).astype(jnp.bfloat16)
    return (hyena_out, query_grad, key_grad, value_grad, filter_update)
```

```python
import jax
import jax.numpy as jnp
from jax import lax
from jax.experimental import pallas as pl
from jax.experimental.pallas import tpu as pltpu
from jax.sharding import PartitionSpec as P

BLOCK = 1024
SUB = 256
ROWS = 8


def carry_kernel(q_ref, k_ref, v_ref, g_ref, p_ref, xend_ref, head_ref, mix_ref, up_ref):
    f32 = jnp.float32
    mix_ref[...] = (k_ref[...].astype(f32) * v_ref[...].astype(f32)).astype(jnp.bfloat16).astype(f32)
    up_ref[...] = g_ref[...].astype(f32) * q_ref[...].astype(f32)
    rows, width = mix_ref.shape
    chunks = rows // ROWS
    for h in range(width // SUB):
        cols = pl.ds(h * SUB, SUB)
        p = p_ref[:, cols]

        def body(c, carry):
            x, a = carry
            fb = pl.multiple_of(c * ROWS, ROWS)
            bb = pl.multiple_of((chunks - 1 - c) * ROWS, ROWS)
            mt = mix_ref[pl.ds(fb, ROWS), cols]
            ub = up_ref[pl.ds(bb, ROWS), cols]
            for j in range(ROWS):
                x = p * x + mt[j : j + 1, :]
                jb = ROWS - 1 - j
                a = p * a + ub[jb : jb + 1, :]
            return x, a

        zero = jnp.zeros(p.shape, f32)
        x, a = lax.fori_loop(0, chunks, body, (zero, zero))
        xend_ref[:, cols] = x
        head_ref[:, cols] = a


def main_kernel(
    q_ref, k_ref, v_ref, g_ref, p_ref, r_ref, s_ref, b_ref,
    ho_ref, qg_ref, kg_ref, vg_ref, tot_ref,
    mix_ref, up_ref, filt_ref, mg_ref,
):
    f32 = jnp.float32
    mix_ref[...] = (k_ref[...].astype(f32) * v_ref[...].astype(f32)).astype(jnp.bfloat16).astype(f32)
    up_ref[...] = g_ref[...].astype(f32) * q_ref[...].astype(f32)
    rows, width = mix_ref.shape
    chunks = rows // ROWS
    for h in range(width // SUB):
        cols = pl.ds(h * SUB, SUB)
        p = p_ref[:, cols]
        r = r_ref[:, cols]

        def body(c, carry):
            x, tot, a = carry
            fb = pl.multiple_of(c * ROWS, ROWS)
            bb = pl.multiple_of((chunks - 1 - c) * ROWS, ROWS)
            mt = mix_ref[pl.ds(fb, ROWS), cols]
            ut = up_ref[pl.ds(fb, ROWS), cols]
            ub = up_ref[pl.ds(bb, ROWS), cols]
            for j in range(ROWS):
                x = p * x + mt[j : j + 1, :]
                tot = tot + ut[j : j + 1, :] * x
                filt_ref[pl.ds(fb + j, 1), cols] = jnp.sum(r * x, axis=0, keepdims=True)
                jb = ROWS - 1 - j
                a = p * a + ub[jb : jb + 1, :]
                mg_ref[pl.ds(bb + jb, 1), cols] = jnp.sum(r * a, axis=0, keepdims=True)
            return x, tot, a

        zero = jnp.zeros(p.shape, f32)
        _, tot, _ = lax.fori_loop(0, chunks, body, (s_ref[:, cols], zero, b_ref[:, cols]))
        tot_ref[:, cols] = tot
    filt = filt_ref[...]
    mg = mg_ref[...]
    ho_ref[...] = (q_ref[...].astype(f32) * filt).astype(jnp.bfloat16)
    qg_ref[...] = (g_ref[...].astype(f32) * filt).astype(jnp.bfloat16)
    kg_ref[...] = (mg * v_ref[...].astype(f32)).astype(jnp.bfloat16)
    vg_ref[...] = (mg * k_ref[...].astype(f32)).astype(jnp.bfloat16)


def local_carries(query_proj, key_proj, value_proj, out_grad, factor):
    rows, width = query_proj.shape
    modes = factor.shape[0]
    big = pl.BlockSpec((rows, BLOCK), lambda i: (0, i))
    small = pl.BlockSpec((modes, BLOCK), lambda i: (0, i))
    return pl.pallas_call(
        carry_kernel,
        grid=(width // BLOCK,),
        in_specs=[big, big, big, big, small],
        out_specs=[small, small],
        out_shape=[jax.ShapeDtypeStruct((modes, width), jnp.float32)] * 2,
        scratch_shapes=[pltpu.VMEM((rows, BLOCK), jnp.float32)] * 2,
    )(query_proj, key_proj, value_proj, out_grad, factor)


def full_scans(query_proj, key_proj, value_proj, out_grad, factor, weight, state_in, adjoint_in):
    rows, width = query_proj.shape
    modes = factor.shape[0]
    big = pl.BlockSpec((rows, BLOCK), lambda i: (0, i))
    small = pl.BlockSpec((modes, BLOCK), lambda i: (0, i))
    out_big = jax.ShapeDtypeStruct((rows, width), jnp.bfloat16)
    return pl.pallas_call(
        main_kernel,
        grid=(width // BLOCK,),
        in_specs=[big, big, big, big, small, small, small, small],
        out_specs=[big, big, big, big, small],
        out_shape=[out_big] * 4 + [jax.ShapeDtypeStruct((modes, width), jnp.float32)],
        scratch_shapes=[pltpu.VMEM((rows, BLOCK), jnp.float32)] * 4,
    )(query_proj, key_proj, value_proj, out_grad, factor, weight, state_in, adjoint_in)


def make_on_device(count):
    def on_device(query_proj, key_proj, value_proj, out_grad, decay_rate, residue, group_of):
        high = lax.Precision.HIGHEST
        rows = query_proj.shape[0]
        group_count = decay_rate.shape[0]
        rate = jnp.take(decay_rate, group_of, axis=0).T
        weight = jnp.take(residue, group_of, axis=0).T
        factor = jnp.exp(-rate)
        end_state, head_adjoint = local_carries(query_proj, key_proj, value_proj, out_grad, factor)

        def span(blocks):
            return jnp.exp(-rate * float(rows * blocks))

        fwd_all = end_state
        bwd_all = head_adjoint
        state_in = jnp.zeros_like(end_state)
        adjoint_in = jnp.zeros_like(head_adjoint)
        shift = 1
        while shift < count:
            ahead = [(i, i + shift) for i in range(count - shift)]
            behind = [(i + shift, i) for i in range(count - shift)]
            got_fwd = lax.ppermute(fwd_all, "ctx", ahead)
            got_bwd = lax.ppermute(bwd_all, "ctx", behind)
            inner = span(shift - 1)
            outer = span(shift)
            state_in = state_in + inner * got_fwd
            adjoint_in = adjoint_in + inner * got_bwd
            fwd_all = fwd_all + outer * got_fwd
            bwd_all = bwd_all + outer * got_bwd
            shift *= 2

        hyena_out, query_grad, key_grad, value_grad, total = full_scans(
            query_proj, key_proj, value_proj, out_grad, factor, weight, state_in, adjoint_in
        )
        member = (group_of[:, None] == jnp.arange(group_count, dtype=jnp.int32)[None, :]).astype(
            jnp.float32
        )
        local_grad = jnp.dot(total, member, precision=high)
        filter_grad = lax.psum(local_grad, "ctx").T
        filter_update = filter_grad / jnp.sqrt(jnp.mean(filter_grad * filter_grad) + 1e-06)
        return (hyena_out, query_grad, key_grad, value_grad, filter_update)

    return on_device


def solution(mesh):
    placed = (
        P(("groups", "ctx"), None),
        P(("groups", "ctx"), None),
        P(("groups", "ctx"), None),
        P(("groups", "ctx"), None),
        P(),
        P(),
        P(),
    )
    return jax.shard_map(
        make_on_device(mesh.shape["ctx"]),
        mesh=mesh,
        in_specs=placed,
        out_specs=(
            P(("groups", "ctx"), None),
            P(("groups", "ctx"), None),
            P(("groups", "ctx"), None),
            P(("groups", "ctx"), None),
            P("groups", None),
        ),
        check_vma=False,
    )
```

```python
import jax
import jax.numpy as jnp
from jax import lax
from jax.experimental import pallas as pl
from jax.experimental.pallas import tpu as pltpu
from jax.sharding import PartitionSpec as P

BLOCK = 1024
SUB = 256
ROWS = 8


def carry_kernel(q_ref, k_ref, v_ref, g_ref, p_ref, xend_ref, head_ref, tot_ref, mix_ref, up_ref):
    f32 = jnp.float32
    mix_ref[...] = (k_ref[...].astype(f32) * v_ref[...].astype(f32)).astype(jnp.bfloat16).astype(f32)
    up_ref[...] = g_ref[...].astype(f32) * q_ref[...].astype(f32)
    rows, width = mix_ref.shape
    chunks = rows // ROWS
    for h in range(width // SUB):
        cols = pl.ds(h * SUB, SUB)
        p = p_ref[:, cols]

        def body(c, carry):
            x, tot, a = carry
            fb = pl.multiple_of(c * ROWS, ROWS)
            bb = pl.multiple_of((chunks - 1 - c) * ROWS, ROWS)
            mt = mix_ref[pl.ds(fb, ROWS), cols]
            ut = up_ref[pl.ds(fb, ROWS), cols]
            ub = up_ref[pl.ds(bb, ROWS), cols]
            for j in range(ROWS):
                x = p * x + mt[j : j + 1, :]
                tot = tot + ut[j : j + 1, :] * x
                jb = ROWS - 1 - j
                a = p * a + ub[jb : jb + 1, :]
            return x, tot, a

        zero = jnp.zeros(p.shape, f32)
        x, tot, a = lax.fori_loop(0, chunks, body, (zero, zero, zero))
        xend_ref[:, cols] = x
        head_ref[:, cols] = a
        tot_ref[:, cols] = tot


def main_kernel(
    q_ref, k_ref, v_ref, g_ref, p_ref, r_ref, s_ref, b_ref,
    ho_ref, qg_ref, kg_ref, vg_ref,
    mix_ref, up_ref, filt_ref, mg_ref,
):
    f32 = jnp.float32
    mix_ref[...] = (k_ref[...].astype(f32) * v_ref[...].astype(f32)).astype(jnp.bfloat16).astype(f32)
    up_ref[...] = g_ref[...].astype(f32) * q_ref[...].astype(f32)
    rows, width = mix_ref.shape
    chunks = rows // ROWS
    for h in range(width // SUB):
        cols = pl.ds(h * SUB, SUB)
        p = p_ref[:, cols]
        r = r_ref[:, cols]

        def body(c, carry):
            x, a = carry
            fb = pl.multiple_of(c * ROWS, ROWS)
            bb = pl.multiple_of((chunks - 1 - c) * ROWS, ROWS)
            mt = mix_ref[pl.ds(fb, ROWS), cols]
            ub = up_ref[pl.ds(bb, ROWS), cols]
            for j in range(ROWS):
                x = p * x + mt[j : j + 1, :]
                filt_ref[pl.ds(fb + j, 1), cols] = jnp.sum(r * x, axis=0, keepdims=True)
                jb = ROWS - 1 - j
                a = p * a + ub[jb : jb + 1, :]
                mg_ref[pl.ds(bb + jb, 1), cols] = jnp.sum(r * a, axis=0, keepdims=True)
            return x, a

        lax.fori_loop(0, chunks, body, (s_ref[:, cols], b_ref[:, cols]))
    filt = filt_ref[...]
    mg = mg_ref[...]
    ho_ref[...] = (q_ref[...].astype(f32) * filt).astype(jnp.bfloat16)
    qg_ref[...] = (g_ref[...].astype(f32) * filt).astype(jnp.bfloat16)
    kg_ref[...] = (mg * v_ref[...].astype(f32)).astype(jnp.bfloat16)
    vg_ref[...] = (mg * k_ref[...].astype(f32)).astype(jnp.bfloat16)


def local_carries(query_proj, key_proj, value_proj, out_grad, factor):
    rows, width = query_proj.shape
    modes = factor.shape[0]
    big = pl.BlockSpec((rows, BLOCK), lambda i: (0, i))
    small = pl.BlockSpec((modes, BLOCK), lambda i: (0, i))
    return pl.pallas_call(
        carry_kernel,
        grid=(width // BLOCK,),
        in_specs=[big, big, big, big, small],
        out_specs=[small, small, small],
        out_shape=[jax.ShapeDtypeStruct((modes, width), jnp.float32)] * 3,
        scratch_shapes=[pltpu.VMEM((rows, BLOCK), jnp.float32)] * 2,
    )(query_proj, key_proj, value_proj, out_grad, factor)


def full_scans(query_proj, key_proj, value_proj, out_grad, factor, weight, state_in, adjoint_in):
    rows, width = query_proj.shape
    modes = factor.shape[0]
    big = pl.BlockSpec((rows, BLOCK), lambda i: (0, i))
    small = pl.BlockSpec((modes, BLOCK), lambda i: (0, i))
    out_big = jax.ShapeDtypeStruct((rows, width), jnp.bfloat16)
    return pl.pallas_call(
        main_kernel,
        grid=(width // BLOCK,),
        in_specs=[big, big, big, big, small, small, small, small],
        out_specs=[big, big, big, big],
        out_shape=[out_big] * 4,
        scratch_shapes=[pltpu.VMEM((rows, BLOCK), jnp.float32)] * 4,
    )(query_proj, key_proj, value_proj, out_grad, factor, weight, state_in, adjoint_in)


def make_on_device(count):
    def on_device(query_proj, key_proj, value_proj, out_grad, decay_rate, residue, group_of):
        high = lax.Precision.HIGHEST
        rows = query_proj.shape[0]
        group_count = decay_rate.shape[0]
        member = (group_of[None, :] == jnp.arange(group_count, dtype=jnp.int32)[:, None]).astype(
            jnp.float32
        )
        rate = jnp.dot(decay_rate.T, member, precision=high)
        weight = jnp.dot(residue.T, member, precision=high)
        factor = jnp.exp(-rate)
        end_state, head_adjoint, local_total = local_carries(
            query_proj, key_proj, value_proj, out_grad, factor
        )

        def span(blocks):
            return jnp.exp(-rate * float(rows * blocks))

        fwd_all = end_state
        bwd_all = head_adjoint
        state_in = jnp.zeros_like(end_state)
        adjoint_in = jnp.zeros_like(head_adjoint)
        shift = 1
        while shift < count:
            ahead = [(i, i + shift) for i in range(count - shift)]
            behind = [(i + shift, i) for i in range(count - shift)]
            got_fwd = lax.ppermute(fwd_all, "ctx", ahead)
            got_bwd = lax.ppermute(bwd_all, "ctx", behind)
            got_fwd, got_bwd = lax.optimization_barrier((got_fwd, got_bwd))
            inner = span(shift - 1)
            outer = span(shift)
            state_in = state_in + inner * got_fwd
            adjoint_in = adjoint_in + inner * got_bwd
            fwd_all = fwd_all + outer * got_fwd
            bwd_all = bwd_all + outer * got_bwd
            shift *= 2

        total = local_total + state_in * factor * head_adjoint
        local_grad = jnp.dot(total, member.T, precision=high)
        gathered = lax.all_gather(local_grad, "ctx")
        hyena_out, query_grad, key_grad, value_grad = full_scans(
            query_proj, key_proj, value_proj, out_grad, factor, weight, state_in, adjoint_in
        )
        filter_grad = jnp.sum(gathered, axis=0).T
        filter_update = filter_grad / jnp.sqrt(jnp.mean(filter_grad * filter_grad) + 1e-06)
        return (hyena_out, query_grad, key_grad, value_grad, filter_update)

    return on_device


def solution(mesh):
    placed = (
        P(("groups", "ctx"), None),
        P(("groups", "ctx"), None),
        P(("groups", "ctx"), None),
        P(("groups", "ctx"), None),
        P(),
        P(),
        P(),
    )
    return jax.shard_map(
        make_on_device(mesh.shape["ctx"]),
        mesh=mesh,
        in_specs=placed,
        out_specs=(
            P(("groups", "ctx"), None),
            P(("groups", "ctx"), None),
            P(("groups", "ctx"), None),
            P(("groups", "ctx"), None),
            P("groups", None),
        ),
        check_vma=False,
    )
```

```python
import jax
import jax.numpy as jnp
from jax import lax
from jax.experimental import pallas as pl
from jax.experimental.pallas import tpu as pltpu
from jax.sharding import PartitionSpec as P

BLOCK = 1024
SUB = 256
ROWS = 8


def carry_kernel(q_ref, k_ref, v_ref, g_ref, p_ref, xend_ref, head_ref, tot_ref, mix_ref, up_ref):
    f32 = jnp.float32
    mix_ref[...] = (k_ref[...].astype(f32) * v_ref[...].astype(f32)).astype(jnp.bfloat16).astype(f32)
    up_ref[...] = g_ref[...].astype(f32) * q_ref[...].astype(f32)
    rows, width = mix_ref.shape
    chunks = rows // ROWS
    for h in range(width // SUB):
        cols = pl.ds(h * SUB, SUB)
        p = p_ref[:, cols]

        def body(c, carry):
            x, tot, a = carry
            fb = pl.multiple_of(c * ROWS, ROWS)
            bb = pl.multiple_of((chunks - 1 - c) * ROWS, ROWS)
            mt = mix_ref[pl.ds(fb, ROWS), cols]
            ut = up_ref[pl.ds(fb, ROWS), cols]
            ub = up_ref[pl.ds(bb, ROWS), cols]
            for j in range(ROWS):
                x = p * x + mt[j : j + 1, :]
                tot = tot + ut[j : j + 1, :] * x
                jb = ROWS - 1 - j
                a = p * a + ub[jb : jb + 1, :]
            return x, tot, a

        zero = jnp.zeros(p.shape, f32)
        x, tot, a = lax.fori_loop(0, chunks, body, (zero, zero, zero))
        xend_ref[:, cols] = x
        head_ref[:, cols] = a
        tot_ref[:, cols] = tot


def main_kernel(
    q_ref, k_ref, v_ref, g_ref, p_ref, r_ref, s_ref, b_ref,
    ho_ref, qg_ref, kg_ref, vg_ref,
    mix_ref, up_ref, filt_ref, mg_ref,
):
    f32 = jnp.float32
    mix_ref[...] = (k_ref[...].astype(f32) * v_ref[...].astype(f32)).astype(jnp.bfloat16).astype(f32)
    up_ref[...] = g_ref[...].astype(f32) * q_ref[...].astype(f32)
    rows, width = mix_ref.shape
    chunks = rows // ROWS
    for h in range(width // SUB):
        cols = pl.ds(h * SUB, SUB)
        p = p_ref[:, cols]
        r = r_ref[:, cols]

        def body(c, carry):
            x, a = carry
            fb = pl.multiple_of(c * ROWS, ROWS)
            bb = pl.multiple_of((chunks - 1 - c) * ROWS, ROWS)
            mt = mix_ref[pl.ds(fb, ROWS), cols]
            ub = up_ref[pl.ds(bb, ROWS), cols]
            for j in range(ROWS):
                x = p * x + mt[j : j + 1, :]
                filt_ref[pl.ds(fb + j, 1), cols] = jnp.sum(r * x, axis=0, keepdims=True)
                jb = ROWS - 1 - j
                a = p * a + ub[jb : jb + 1, :]
                mg_ref[pl.ds(bb + jb, 1), cols] = jnp.sum(r * a, axis=0, keepdims=True)
            return x, a

        lax.fori_loop(0, chunks, body, (s_ref[:, cols], b_ref[:, cols]))
    filt = filt_ref[...]
    mg = mg_ref[...]
    ho_ref[...] = (q_ref[...].astype(f32) * filt).astype(jnp.bfloat16)
    qg_ref[...] = (g_ref[...].astype(f32) * filt).astype(jnp.bfloat16)
    kg_ref[...] = (mg * v_ref[...].astype(f32)).astype(jnp.bfloat16)
    vg_ref[...] = (mg * k_ref[...].astype(f32)).astype(jnp.bfloat16)


def local_carries(query_proj, key_proj, value_proj, out_grad, factor):
    rows, width = query_proj.shape
    modes = factor.shape[0]
    big = pl.BlockSpec((rows, BLOCK), lambda i: (0, i))
    small = pl.BlockSpec((modes, BLOCK), lambda i: (0, i))
    return pl.pallas_call(
        carry_kernel,
        grid=(width // BLOCK,),
        in_specs=[big, big, big, big, small],
        out_specs=[small, small, small],
        out_shape=[jax.ShapeDtypeStruct((modes, width), jnp.float32)] * 3,
        scratch_shapes=[pltpu.VMEM((rows, BLOCK), jnp.float32)] * 2,
    )(query_proj, key_proj, value_proj, out_grad, factor)


def full_scans(query_proj, key_proj, value_proj, out_grad, factor, weight, state_in, adjoint_in):
    rows, width = query_proj.shape
    modes = factor.shape[0]
    big = pl.BlockSpec((rows, BLOCK), lambda i: (0, i))
    small = pl.BlockSpec((modes, BLOCK), lambda i: (0, i))
    out_big = jax.ShapeDtypeStruct((rows, width), jnp.bfloat16)
    return pl.pallas_call(
        main_kernel,
        grid=(width // BLOCK,),
        in_specs=[big, big, big, big, small, small, small, small],
        out_specs=[big, big, big, big],
        out_shape=[out_big] * 4,
        scratch_shapes=[pltpu.VMEM((rows, BLOCK), jnp.float32)] * 4,
    )(query_proj, key_proj, value_proj, out_grad, factor, weight, state_in, adjoint_in)


def make_on_device(count):
    def on_device(query_proj, key_proj, value_proj, out_grad, decay_rate, residue, group_of):
        high = lax.Precision.HIGHEST
        rows = query_proj.shape[0]
        group_count = decay_rate.shape[0]
        member = (group_of[None, :] == jnp.arange(group_count, dtype=jnp.int32)[:, None]).astype(
            jnp.float32
        )
        rate = jnp.dot(decay_rate.T, member, precision=high)
        weight = jnp.dot(residue.T, member, precision=high)
        factor = jnp.exp(-rate)
        end_state, head_adjoint, local_total = local_carries(
            query_proj, key_proj, value_proj, out_grad, factor
        )

        def span(blocks):
            return jnp.exp(-rate * float(rows * blocks))

        fwd_all = end_state
        bwd_all = head_adjoint
        state_in = jnp.zeros_like(end_state)
        adjoint_in = jnp.zeros_like(head_adjoint)
        shift = 1
        while shift < count:
            ahead = [(i, i + shift) for i in range(count - shift)]
            behind = [(i + shift, i) for i in range(count - shift)]
            got_fwd = lax.ppermute(fwd_all, "ctx", ahead)
            got_bwd = lax.ppermute(bwd_all, "ctx", behind)
            got_fwd, got_bwd = lax.optimization_barrier((got_fwd, got_bwd))
            inner = span(shift - 1)
            outer = span(shift)
            state_in = state_in + inner * got_fwd
            adjoint_in = adjoint_in + inner * got_bwd
            fwd_all = fwd_all + outer * got_fwd
            bwd_all = bwd_all + outer * got_bwd
            shift *= 2

        total = lax.psum(local_total + state_in * factor * head_adjoint, "ctx")
        hyena_out, query_grad, key_grad, value_grad = full_scans(
            query_proj, key_proj, value_proj, out_grad, factor, weight, state_in, adjoint_in
        )
        filter_grad = jnp.dot(total, member.T, precision=high).T
        filter_update = filter_grad / jnp.sqrt(jnp.mean(filter_grad * filter_grad) + 1e-06)
        return (hyena_out, query_grad, key_grad, value_grad, filter_update)

    return on_device


def solution(mesh):
    placed = (
        P(("groups", "ctx"), None),
        P(("groups", "ctx"), None),
        P(("groups", "ctx"), None),
        P(("groups", "ctx"), None),
        P(),
        P(),
        P(),
    )
    return jax.shard_map(
        make_on_device(mesh.shape["ctx"]),
        mesh=mesh,
        in_specs=placed,
        out_specs=(
            P(("groups", "ctx"), None),
            P(("groups", "ctx"), None),
            P(("groups", "ctx"), None),
            P(("groups", "ctx"), None),
            P("groups", None),
        ),
        check_vma=False,
    )
```

```python
import jax
import jax.numpy as jnp
from jax import lax
from jax.experimental import pallas as pl
from jax.experimental.pallas import tpu as pltpu
from jax.sharding import PartitionSpec as P

BLOCK = 1024
SUB = 256
ROWS = 8


def carry_kernel(q_ref, k_ref, v_ref, g_ref, p_ref, xend_ref, head_ref, tot_ref, mix_ref, up_ref):
    f32 = jnp.float32
    mix_ref[...] = (k_ref[...].astype(f32) * v_ref[...].astype(f32)).astype(jnp.bfloat16).astype(f32)
    up_ref[...] = g_ref[...].astype(f32) * q_ref[...].astype(f32)
    rows, width = mix_ref.shape
    chunks = rows // ROWS
    for h in range(width // SUB):
        cols = pl.ds(h * SUB, SUB)
        p = p_ref[:, cols]

        def body(c, carry):
            x, tot, a = carry
            fb = pl.multiple_of(c * ROWS, ROWS)
            bb = pl.multiple_of((chunks - 1 - c) * ROWS, ROWS)
            mt = mix_ref[pl.ds(fb, ROWS), cols]
            ut = up_ref[pl.ds(fb, ROWS), cols]
            ub = up_ref[pl.ds(bb, ROWS), cols]
            for j in range(ROWS):
                x = p * x + mt[j : j + 1, :]
                tot = tot + ut[j : j + 1, :] * x
                jb = ROWS - 1 - j
                a = p * a + ub[jb : jb + 1, :]
            return x, tot, a

        zero = jnp.zeros(p.shape, f32)
        x, tot, a = lax.fori_loop(0, chunks, body, (zero, zero, zero))
        xend_ref[:, cols] = x
        head_ref[:, cols] = a
        tot_ref[:, cols] = tot


def main_kernel(
    q_ref, k_ref, v_ref, g_ref, p_ref, r_ref, s_ref, b_ref,
    ho_ref, qg_ref, kg_ref, vg_ref,
    mix_ref, up_ref, filt_ref, mg_ref,
):
    f32 = jnp.float32
    mix_ref[...] = (k_ref[...].astype(f32) * v_ref[...].astype(f32)).astype(jnp.bfloat16).astype(f32)
    up_ref[...] = g_ref[...].astype(f32) * q_ref[...].astype(f32)
    rows, width = mix_ref.shape
    chunks = rows // ROWS
    for h in range(width // SUB):
        cols = pl.ds(h * SUB, SUB)
        p = p_ref[:, cols]
        r = r_ref[:, cols]

        def body(c, carry):
            x, a = carry
            fb = pl.multiple_of(c * ROWS, ROWS)
            bb = pl.multiple_of((chunks - 1 - c) * ROWS, ROWS)
            mt = mix_ref[pl.ds(fb, ROWS), cols]
            ub = up_ref[pl.ds(bb, ROWS), cols]
            for j in range(ROWS):
                x = p * x + mt[j : j + 1, :]
                filt_ref[pl.ds(fb + j, 1), cols] = jnp.sum(r * x, axis=0, keepdims=True)
                jb = ROWS - 1 - j
                a = p * a + ub[jb : jb + 1, :]
                mg_ref[pl.ds(bb + jb, 1), cols] = jnp.sum(r * a, axis=0, keepdims=True)
            return x, a

        lax.fori_loop(0, chunks, body, (s_ref[:, cols], b_ref[:, cols]))
    filt = filt_ref[...]
    mg = mg_ref[...]
    ho_ref[...] = (q_ref[...].astype(f32) * filt).astype(jnp.bfloat16)
    qg_ref[...] = (g_ref[...].astype(f32) * filt).astype(jnp.bfloat16)
    kg_ref[...] = (mg * v_ref[...].astype(f32)).astype(jnp.bfloat16)
    vg_ref[...] = (mg * k_ref[...].astype(f32)).astype(jnp.bfloat16)


def local_carries(query_proj, key_proj, value_proj, out_grad, factor):
    rows, width = query_proj.shape
    modes = factor.shape[0]
    big = pl.BlockSpec((rows, BLOCK), lambda i: (0, i))
    small = pl.BlockSpec((modes, BLOCK), lambda i: (0, i))
    return pl.pallas_call(
        carry_kernel,
        grid=(width // BLOCK,),
        in_specs=[big, big, big, big, small],
        out_specs=[small, small, small],
        out_shape=[jax.ShapeDtypeStruct((modes, width), jnp.float32)] * 3,
        scratch_shapes=[pltpu.VMEM((rows, BLOCK), jnp.float32)] * 2,
    )(query_proj, key_proj, value_proj, out_grad, factor)


def full_scans(query_proj, key_proj, value_proj, out_grad, factor, weight, state_in, adjoint_in):
    rows, width = query_proj.shape
    modes = factor.shape[0]
    big = pl.BlockSpec((rows, BLOCK), lambda i: (0, i))
    small = pl.BlockSpec((modes, BLOCK), lambda i: (0, i))
    out_big = jax.ShapeDtypeStruct((rows, width), jnp.bfloat16)
    return pl.pallas_call(
        main_kernel,
        grid=(width // BLOCK,),
        in_specs=[big, big, big, big, small, small, small, small],
        out_specs=[big, big, big, big],
        out_shape=[out_big] * 4,
        scratch_shapes=[pltpu.VMEM((rows, BLOCK), jnp.float32)] * 4,
    )(query_proj, key_proj, value_proj, out_grad, factor, weight, state_in, adjoint_in)


def make_on_device(count):
    def on_device(query_proj, key_proj, value_proj, out_grad, decay_rate, residue, group_of):
        high = lax.Precision.HIGHEST
        rows = query_proj.shape[0]
        group_count = decay_rate.shape[0]
        member = (group_of[None, :] == jnp.arange(group_count, dtype=jnp.int32)[:, None]).astype(
            jnp.float32
        )
        rate = jnp.dot(decay_rate.T, member, precision=high)
        weight = jnp.dot(residue.T, member, precision=high)
        factor = jnp.exp(-rate)
        end_state, head_adjoint, local_total = local_carries(
            query_proj, key_proj, value_proj, out_grad, factor
        )

        def span(blocks):
            return jnp.exp(-rate * (blocks * float(rows)))

        def grouped(a):
            return jnp.dot(a, member.T, precision=high)

        place = lax.axis_index("ctx")
        fwd_cube = end_state
        bwd_cube = head_adjoint
        grad_cube = grouped(local_total)
        state_in = jnp.zeros_like(end_state)
        adjoint_in = jnp.zeros_like(head_adjoint)
        bit = 1
        while bit < count:
            pairs = [(i, i ^ bit) for i in range(count)]
            width = fwd_cube.shape[1]
            packed = jnp.concatenate([fwd_cube, bwd_cube, grad_cube], axis=1)
            got = lax.ppermute(packed, "ctx", pairs)
            got_fwd = got[:, :width]
            got_bwd = got[:, width : 2 * width]
            got_grad = got[:, 2 * width :]
            upper = (place & bit) != 0
            offset = (place % bit).astype(jnp.float32)
            low_fwd = jnp.where(upper, got_fwd, fwd_cube)
            high_fwd = jnp.where(upper, fwd_cube, got_fwd)
            low_bwd = jnp.where(upper, got_bwd, bwd_cube)
            high_bwd = jnp.where(upper, bwd_cube, got_bwd)
            low_grad = jnp.where(upper, got_grad, grad_cube)
            high_grad = jnp.where(upper, grad_cube, got_grad)
            state_in = state_in + jnp.where(upper, span(offset) * got_fwd, 0.0)
            adjoint_in = adjoint_in + jnp.where(upper, 0.0, span(bit - 1 - offset) * got_bwd)
            whole = span(bit)
            grad_cube = (low_grad + high_grad) + grouped((factor * low_fwd) * high_bwd)
            fwd_cube = high_fwd + whole * low_fwd
            bwd_cube = low_bwd + whole * high_bwd
            bit *= 2

        hyena_out, query_grad, key_grad, value_grad = full_scans(
            query_proj, key_proj, value_proj, out_grad, factor, weight, state_in, adjoint_in
        )
        filter_grad = grad_cube.T
        filter_update = filter_grad / jnp.sqrt(jnp.mean(filter_grad * filter_grad) + 1e-06)
        return (hyena_out, query_grad, key_grad, value_grad, filter_update)

    return on_device


def solution(mesh):
    placed = (
        P(("groups", "ctx"), None),
        P(("groups", "ctx"), None),
        P(("groups", "ctx"), None),
        P(("groups", "ctx"), None),
        P(),
        P(),
        P(),
    )
    return jax.shard_map(
        make_on_device(mesh.shape["ctx"]),
        mesh=mesh,
        in_specs=placed,
        out_specs=(
            P(("groups", "ctx"), None),
            P(("groups", "ctx"), None),
            P(("groups", "ctx"), None),
            P(("groups", "ctx"), None),
            P("groups", None),
        ),
        check_vma=False,
    )
```

```python
import jax
import jax.numpy as jnp
from jax import lax
from jax.experimental import pallas as pl
from jax.experimental.pallas import tpu as pltpu
from jax.sharding import PartitionSpec as P

BLOCK = 1024
SUB = 256
ROWS = 8


def carry_kernel(q_ref, k_ref, v_ref, g_ref, p_ref, xend_ref, head_ref, tot_ref, mix_ref, up_ref):
    f32 = jnp.float32
    mix_ref[...] = (k_ref[...].astype(f32) * v_ref[...].astype(f32)).astype(jnp.bfloat16).astype(f32)
    up_ref[...] = g_ref[...].astype(f32) * q_ref[...].astype(f32)
    rows, width = mix_ref.shape
    chunks = rows // ROWS
    for h in range(width // SUB):
        cols = pl.ds(h * SUB, SUB)
        p = p_ref[:, cols]

        def body(c, carry):
            x, tot, a = carry
            fb = pl.multiple_of(c * ROWS, ROWS)
            bb = pl.multiple_of((chunks - 1 - c) * ROWS, ROWS)
            mt = mix_ref[pl.ds(fb, ROWS), cols]
            ut = up_ref[pl.ds(fb, ROWS), cols]
            ub = up_ref[pl.ds(bb, ROWS), cols]
            for j in range(ROWS):
                x = p * x + mt[j : j + 1, :]
                tot = tot + ut[j : j + 1, :] * x
                jb = ROWS - 1 - j
                a = p * a + ub[jb : jb + 1, :]
            return x, tot, a

        zero = jnp.zeros(p.shape, f32)
        x, tot, a = lax.fori_loop(0, chunks, body, (zero, zero, zero))
        xend_ref[:, cols] = x
        head_ref[:, cols] = a
        tot_ref[:, cols] = tot


def main_kernel(
    q_ref, k_ref, v_ref, g_ref, p_ref, r_ref, s_ref, b_ref,
    ho_ref, qg_ref, kg_ref, vg_ref,
    mix_ref, up_ref, filt_ref, mg_ref,
):
    f32 = jnp.float32
    mix_ref[...] = (k_ref[...].astype(f32) * v_ref[...].astype(f32)).astype(jnp.bfloat16).astype(f32)
    up_ref[...] = g_ref[...].astype(f32) * q_ref[...].astype(f32)
    rows, width = mix_ref.shape
    chunks = rows // ROWS
    for h in range(width // SUB):
        cols = pl.ds(h * SUB, SUB)
        p = p_ref[:, cols]
        r = r_ref[:, cols]

        def body(c, carry):
            x, a = carry
            fb = pl.multiple_of(c * ROWS, ROWS)
            bb = pl.multiple_of((chunks - 1 - c) * ROWS, ROWS)
            mt = mix_ref[pl.ds(fb, ROWS), cols]
            ub = up_ref[pl.ds(bb, ROWS), cols]
            for j in range(ROWS):
                x = p * x + mt[j : j + 1, :]
                filt_ref[pl.ds(fb + j, 1), cols] = jnp.sum(r * x, axis=0, keepdims=True)
                jb = ROWS - 1 - j
                a = p * a + ub[jb : jb + 1, :]
                mg_ref[pl.ds(bb + jb, 1), cols] = jnp.sum(r * a, axis=0, keepdims=True)
            return x, a

        lax.fori_loop(0, chunks, body, (s_ref[:, cols], b_ref[:, cols]))
    filt = filt_ref[...]
    mg = mg_ref[...]
    ho_ref[...] = (q_ref[...].astype(f32) * filt).astype(jnp.bfloat16)
    qg_ref[...] = (g_ref[...].astype(f32) * filt).astype(jnp.bfloat16)
    kg_ref[...] = (mg * v_ref[...].astype(f32)).astype(jnp.bfloat16)
    vg_ref[...] = (mg * k_ref[...].astype(f32)).astype(jnp.bfloat16)


def local_carries(query_proj, key_proj, value_proj, out_grad, factor):
    rows, width = query_proj.shape
    modes = factor.shape[0]
    big = pl.BlockSpec((rows, BLOCK), lambda i: (0, i))
    small = pl.BlockSpec((modes, BLOCK), lambda i: (0, i))
    return pl.pallas_call(
        carry_kernel,
        grid=(width // BLOCK,),
        in_specs=[big, big, big, big, small],
        out_specs=[small, small, small],
        out_shape=[jax.ShapeDtypeStruct((modes, width), jnp.float32)] * 3,
        scratch_shapes=[pltpu.VMEM((rows, BLOCK), jnp.float32)] * 2,
    )(query_proj, key_proj, value_proj, out_grad, factor)


def full_scans(query_proj, key_proj, value_proj, out_grad, factor, weight, state_in, adjoint_in):
    rows, width = query_proj.shape
    modes = factor.shape[0]
    big = pl.BlockSpec((rows, BLOCK), lambda i: (0, i))
    small = pl.BlockSpec((modes, BLOCK), lambda i: (0, i))
    out_big = jax.ShapeDtypeStruct((rows, width), jnp.bfloat16)
    return pl.pallas_call(
        main_kernel,
        grid=(width // BLOCK,),
        in_specs=[big, big, big, big, small, small, small, small],
        out_specs=[big, big, big, big],
        out_shape=[out_big] * 4,
        scratch_shapes=[pltpu.VMEM((rows, BLOCK), jnp.float32)] * 4,
    )(query_proj, key_proj, value_proj, out_grad, factor, weight, state_in, adjoint_in)


def make_on_device(count):
    def on_device(query_proj, key_proj, value_proj, out_grad, decay_rate, residue, group_of):
        high = lax.Precision.HIGHEST
        rows = query_proj.shape[0]
        group_count = decay_rate.shape[0]
        member = (group_of[None, :] == jnp.arange(group_count, dtype=jnp.int32)[:, None]).astype(
            jnp.float32
        )
        rate = jnp.dot(decay_rate.T, member, precision=high)
        weight = jnp.dot(residue.T, member, precision=high)
        factor = jnp.exp(-rate)
        end_state, head_adjoint, local_total = local_carries(
            query_proj, key_proj, value_proj, out_grad, factor
        )

        def span(blocks):
            return jnp.exp(-rate * (blocks * float(rows)))

        def grouped(a):
            return jnp.dot(a, member.T, precision=high)

        place = lax.axis_index("ctx")
        fwd_cube = end_state
        bwd_cube = head_adjoint
        grad_cube = grouped(local_total)
        state_in = jnp.zeros_like(end_state)
        adjoint_in = jnp.zeros_like(head_adjoint)
        bit = 1
        while bit < count:
            pairs = [(i, i ^ bit) for i in range(count)]
            width = fwd_cube.shape[1]
            packed = jnp.concatenate([fwd_cube, bwd_cube, grad_cube], axis=1)
            if bit == 1:
                got = lax.ppermute(packed, "ctx", pairs)
            else:
                half = packed.shape[1] // 2
                core = place % 2
                mine = lax.dynamic_slice_in_dim(packed, core * half, half, axis=1)
                got_mine = lax.ppermute(mine, "ctx", pairs)
                got_other = lax.ppermute(got_mine, "ctx", [(i, i ^ 1) for i in range(count)])
                first = jnp.where(core == 0, got_mine, got_other)
                second = jnp.where(core == 0, got_other, got_mine)
                got = jnp.concatenate([first, second], axis=1)
            got_fwd = got[:, :width]
            got_bwd = got[:, width : 2 * width]
            got_grad = got[:, 2 * width :]
            upper = (place & bit) != 0
            offset = (place % bit).astype(jnp.float32)
            low_fwd = jnp.where(upper, got_fwd, fwd_cube)
            high_fwd = jnp.where(upper, fwd_cube, got_fwd)
            low_bwd = jnp.where(upper, got_bwd, bwd_cube)
            high_bwd = jnp.where(upper, bwd_cube, got_bwd)
            low_grad = jnp.where(upper, got_grad, grad_cube)
            high_grad = jnp.where(upper, grad_cube, got_grad)
            state_in = state_in + jnp.where(upper, span(offset) * got_fwd, 0.0)
            adjoint_in = adjoint_in + jnp.where(upper, 0.0, span(bit - 1 - offset) * got_bwd)
            whole = span(bit)
            grad_cube = (low_grad + high_grad) + grouped((factor * low_fwd) * high_bwd)
            fwd_cube = high_fwd + whole * low_fwd
            bwd_cube = low_bwd + whole * high_bwd
            bit *= 2

        hyena_out, query_grad, key_grad, value_grad = full_scans(
            query_proj, key_proj, value_proj, out_grad, factor, weight, state_in, adjoint_in
        )
        filter_grad = grad_cube.T
        filter_update = filter_grad / jnp.sqrt(jnp.mean(filter_grad * filter_grad) + 1e-06)
        return (hyena_out, query_grad, key_grad, value_grad, filter_update)

    return on_device


def solution(mesh):
    placed = (
        P(("groups", "ctx"), None),
        P(("groups", "ctx"), None),
        P(("groups", "ctx"), None),
        P(("groups", "ctx"), None),
        P(),
        P(),
        P(),
    )
    return jax.shard_map(
        make_on_device(mesh.shape["ctx"]),
        mesh=mesh,
        in_specs=placed,
        out_specs=(
            P(("groups", "ctx"), None),
            P(("groups", "ctx"), None),
            P(("groups", "ctx"), None),
            P(("groups", "ctx"), None),
            P("groups", None),
        ),
        check_vma=False,
    )
```

```python
import jax
import jax.numpy as jnp
from jax import lax
from jax.experimental import pallas as pl
from jax.experimental.pallas import tpu as pltpu
from jax.sharding import PartitionSpec as P

BLOCK = 1024
SUB = 256
ROWS = 8


def carry_kernel(q_ref, k_ref, v_ref, g_ref, p_ref, xend_ref, head_ref, tot_ref, mix_ref, up_ref):
    f32 = jnp.float32
    mix_ref[...] = (k_ref[...].astype(f32) * v_ref[...].astype(f32)).astype(jnp.bfloat16).astype(f32)
    up_ref[...] = g_ref[...].astype(f32) * q_ref[...].astype(f32)
    rows, width = mix_ref.shape
    chunks = rows // ROWS
    for h in range(width // SUB):
        cols = pl.ds(h * SUB, SUB)
        p = p_ref[:, cols]

        def body(c, carry):
            x, tot, a = carry
            fb = pl.multiple_of(c * ROWS, ROWS)
            bb = pl.multiple_of((chunks - 1 - c) * ROWS, ROWS)
            mt = mix_ref[pl.ds(fb, ROWS), cols]
            ut = up_ref[pl.ds(fb, ROWS), cols]
            ub = up_ref[pl.ds(bb, ROWS), cols]
            for j in range(ROWS):
                x = p * x + mt[j : j + 1, :]
                tot = tot + ut[j : j + 1, :] * x
                jb = ROWS - 1 - j
                a = p * a + ub[jb : jb + 1, :]
            return x, tot, a

        zero = jnp.zeros(p.shape, f32)
        x, tot, a = lax.fori_loop(0, chunks, body, (zero, zero, zero))
        xend_ref[:, cols] = x
        head_ref[:, cols] = a
        tot_ref[:, cols] = tot


def main_kernel(
    q_ref, k_ref, v_ref, g_ref, p_ref, r_ref, s_ref, b_ref,
    ho_ref, qg_ref, kg_ref, vg_ref,
    mix_ref, up_ref, filt_ref, mg_ref,
):
    f32 = jnp.float32
    mix_ref[...] = (k_ref[...].astype(f32) * v_ref[...].astype(f32)).astype(jnp.bfloat16).astype(f32)
    up_ref[...] = g_ref[...].astype(f32) * q_ref[...].astype(f32)
    rows, width = mix_ref.shape
    chunks = rows // ROWS
    for h in range(width // SUB):
        cols = pl.ds(h * SUB, SUB)
        p = p_ref[:, cols]
        r = r_ref[:, cols]

        def body(c, carry):
            x, a = carry
            fb = pl.multiple_of(c * ROWS, ROWS)
            bb = pl.multiple_of((chunks - 1 - c) * ROWS, ROWS)
            mt = mix_ref[pl.ds(fb, ROWS), cols]
            ub = up_ref[pl.ds(bb, ROWS), cols]
            for j in range(ROWS):
                x = p * x + mt[j : j + 1, :]
                filt_ref[pl.ds(fb + j, 1), cols] = jnp.sum(r * x, axis=0, keepdims=True)
                jb = ROWS - 1 - j
                a = p * a + ub[jb : jb + 1, :]
                mg_ref[pl.ds(bb + jb, 1), cols] = jnp.sum(r * a, axis=0, keepdims=True)
            return x, a

        lax.fori_loop(0, chunks, body, (s_ref[:, cols], b_ref[:, cols]))
    filt = filt_ref[...]
    mg = mg_ref[...]
    ho_ref[...] = (q_ref[...].astype(f32) * filt).astype(jnp.bfloat16)
    qg_ref[...] = (g_ref[...].astype(f32) * filt).astype(jnp.bfloat16)
    kg_ref[...] = (mg * v_ref[...].astype(f32)).astype(jnp.bfloat16)
    vg_ref[...] = (mg * k_ref[...].astype(f32)).astype(jnp.bfloat16)


def local_carries(query_proj, key_proj, value_proj, out_grad, factor, first, blocks):
    rows, width = query_proj.shape
    modes = factor.shape[0]
    big = pl.BlockSpec((rows, BLOCK), lambda i: (0, i + first))
    small = pl.BlockSpec((modes, BLOCK), lambda i: (0, i))
    return pl.pallas_call(
        carry_kernel,
        grid=(blocks,),
        in_specs=[big, big, big, big, small],
        out_specs=[small, small, small],
        out_shape=[jax.ShapeDtypeStruct((modes, blocks * BLOCK), jnp.float32)] * 3,
        scratch_shapes=[pltpu.VMEM((rows, BLOCK), jnp.float32)] * 2,
    )(query_proj, key_proj, value_proj, out_grad, factor)


def full_scans(
    query_proj, key_proj, value_proj, out_grad, factor, weight, state_in, adjoint_in,
    first, blocks, previous,
):
    rows, width = query_proj.shape
    modes = factor.shape[0]
    big = pl.BlockSpec((rows, BLOCK), lambda i: (0, i + first))
    small = pl.BlockSpec((modes, BLOCK), lambda i: (0, i))
    out_big = jax.ShapeDtypeStruct((rows, width), jnp.bfloat16)
    operands = [query_proj, key_proj, value_proj, out_grad, factor, weight, state_in, adjoint_in]
    specs = [big, big, big, big, small, small, small, small]
    aliases = {}
    kernel = main_kernel
    if previous is not None:
        operands += list(previous)
        specs += [pl.BlockSpec(memory_space=pl.ANY)] * 4
        aliases = {8: 0, 9: 1, 10: 2, 11: 3}

        def kernel(*refs):
            main_kernel(*refs[:8], *refs[12:])

    return pl.pallas_call(
        kernel,
        grid=(blocks,),
        in_specs=specs,
        out_specs=[big, big, big, big],
        out_shape=[out_big] * 4,
        scratch_shapes=[pltpu.VMEM((rows, BLOCK), jnp.float32)] * 4,
        input_output_aliases=aliases,
    )(*operands)


def make_on_device(count):
    def exchange(query_proj, key_proj, value_proj, out_grad, rate, factor, member, first, blocks, rows, place):
        high = lax.Precision.HIGHEST
        end_state, head_adjoint, local_total = local_carries(
            query_proj, key_proj, value_proj, out_grad, factor, first, blocks
        )

        def span(blocks):
            return jnp.exp(-rate * (blocks * float(rows)))

        def grouped(a):
            return jnp.dot(a, member.T, precision=high)

        fwd_cube = end_state
        bwd_cube = head_adjoint
        grad_cube = grouped(local_total)
        state_in = jnp.zeros_like(end_state)
        adjoint_in = jnp.zeros_like(head_adjoint)
        bit = 1
        while bit < count:
            pairs = [(i, i ^ bit) for i in range(count)]
            width = fwd_cube.shape[1]
            packed = jnp.concatenate([fwd_cube, bwd_cube, grad_cube], axis=1)
            if bit == 1:
                got = lax.ppermute(packed, "ctx", pairs)
            else:
                half = packed.shape[1] // 2
                core = place % 2
                mine = lax.dynamic_slice_in_dim(packed, core * half, half, axis=1)
                got_mine = lax.ppermute(mine, "ctx", pairs)
                got_other = lax.ppermute(got_mine, "ctx", [(i, i ^ 1) for i in range(count)])
                lead = jnp.where(core == 0, got_mine, got_other)
                trail = jnp.where(core == 0, got_other, got_mine)
                got = jnp.concatenate([lead, trail], axis=1)
            got_fwd = got[:, :width]
            got_bwd = got[:, width : 2 * width]
            got_grad = got[:, 2 * width :]
            upper = (place & bit) != 0
            offset = (place % bit).astype(jnp.float32)
            low_fwd = jnp.where(upper, got_fwd, fwd_cube)
            high_fwd = jnp.where(upper, fwd_cube, got_fwd)
            low_bwd = jnp.where(upper, got_bwd, bwd_cube)
            high_bwd = jnp.where(upper, bwd_cube, got_bwd)
            low_grad = jnp.where(upper, got_grad, grad_cube)
            high_grad = jnp.where(upper, grad_cube, got_grad)
            state_in = state_in + jnp.where(upper, span(offset) * got_fwd, 0.0)
            adjoint_in = adjoint_in + jnp.where(upper, 0.0, span(bit - 1 - offset) * got_bwd)
            whole = span(bit)
            grad_cube = (low_grad + high_grad) + grouped((factor * low_fwd) * high_bwd)
            fwd_cube = high_fwd + whole * low_fwd
            bwd_cube = low_bwd + whole * high_bwd
            bit *= 2

        return state_in, adjoint_in, grad_cube

    def on_device(query_proj, key_proj, value_proj, out_grad, decay_rate, residue, group_of):
        high = lax.Precision.HIGHEST
        rows = query_proj.shape[0]
        group_count = decay_rate.shape[0]
        member = (group_of[None, :] == jnp.arange(group_count, dtype=jnp.int32)[:, None]).astype(
            jnp.float32
        )
        rate = jnp.dot(decay_rate.T, member, precision=high)
        weight = jnp.dot(residue.T, member, precision=high)
        factor = jnp.exp(-rate)
        width = query_proj.shape[1]
        pieces = 2 if width % (2 * BLOCK) == 0 else 1
        blocks = width // BLOCK // pieces
        place = lax.axis_index("ctx")
        previous = None
        grad_total = None
        for piece in range(pieces):
            lanes = slice(piece * blocks * BLOCK, (piece + 1) * blocks * BLOCK)
            state_in, adjoint_in, grad_cube = exchange(
                query_proj, key_proj, value_proj, out_grad, rate[:, lanes], factor[:, lanes],
                member[:, lanes], piece * blocks, blocks, rows, place,
            )
            grad_total = grad_cube if grad_total is None else grad_total + grad_cube
            previous = full_scans(
                query_proj, key_proj, value_proj, out_grad, factor[:, lanes], weight[:, lanes],
                state_in, adjoint_in, piece * blocks, blocks, previous,
            )
        hyena_out, query_grad, key_grad, value_grad = previous
        filter_grad = grad_total.T
        filter_update = filter_grad / jnp.sqrt(jnp.mean(filter_grad * filter_grad) + 1e-06)
        return (hyena_out, query_grad, key_grad, value_grad, filter_update)

    return on_device


def solution(mesh):
    placed = (
        P(("groups", "ctx"), None),
        P(("groups", "ctx"), None),
        P(("groups", "ctx"), None),
        P(("groups", "ctx"), None),
        P(),
        P(),
        P(),
    )
    return jax.shard_map(
        make_on_device(mesh.shape["ctx"]),
        mesh=mesh,
        in_specs=placed,
        out_specs=(
            P(("groups", "ctx"), None),
            P(("groups", "ctx"), None),
            P(("groups", "ctx"), None),
            P(("groups", "ctx"), None),
            P("groups", None),
        ),
        check_vma=False,
    )
```

```python
import jax
import jax.numpy as jnp
from jax import lax
from jax.experimental import pallas as pl
from jax.experimental.pallas import tpu as pltpu
from jax.sharding import PartitionSpec as P

BLOCK = 1024
SUB = 256
ROWS = 8
LANE = 128


def carry_kernel(q_ref, k_ref, v_ref, g_ref, p_ref, xend_ref, head_ref, tot_ref, mix_ref, up_ref):
    f32 = jnp.float32
    mix_ref[...] = (k_ref[...].astype(f32) * v_ref[...].astype(f32)).astype(jnp.bfloat16).astype(f32)
    up_ref[...] = g_ref[...].astype(f32) * q_ref[...].astype(f32)
    rows, width = mix_ref.shape
    chunks = rows // ROWS
    for h in range(width // SUB):
        cols = pl.ds(h * SUB, SUB)
        p = p_ref[:, cols]

        def body(c, carry):
            x, tot, a = carry
            fb = pl.multiple_of(c * ROWS, ROWS)
            bb = pl.multiple_of((chunks - 1 - c) * ROWS, ROWS)
            mt = mix_ref[pl.ds(fb, ROWS), cols]
            ut = up_ref[pl.ds(fb, ROWS), cols]
            ub = up_ref[pl.ds(bb, ROWS), cols]
            for j in range(ROWS):
                x = p * x + mt[j : j + 1, :]
                tot = tot + ut[j : j + 1, :] * x
                jb = ROWS - 1 - j
                a = p * a + ub[jb : jb + 1, :]
            return x, tot, a

        zero = jnp.zeros(p.shape, f32)
        x, tot, a = lax.fori_loop(0, chunks, body, (zero, zero, zero))
        xend_ref[:, cols] = x
        head_ref[:, cols] = a
        tot_ref[:, cols] = tot


def main_kernel(
    q_ref, k_ref, v_ref, g_ref, p_ref, r_ref, s_ref, b_ref,
    ho_ref, qg_ref, kg_ref, vg_ref,
    mix_ref, up_ref, filt_ref, mg_ref,
):
    f32 = jnp.float32
    rows, width = q_ref.shape
    lanes = width // LANE
    for c in range(lanes):
        cols = slice(c * LANE, (c + 1) * LANE)
        band = slice(c * rows, (c + 1) * rows)
        kf = k_ref[:, cols].astype(f32)
        vf = v_ref[:, cols].astype(f32)
        mix_ref[band, :] = (kf * vf).astype(jnp.bfloat16).astype(f32)
        up_ref[band, :] = g_ref[:, cols].astype(f32) * q_ref[:, cols].astype(f32)

    def body(t, carry):
        x, a = carry
        p = p_ref[...]
        r = r_ref[...]
        x = p * x + mix_ref[pl.ds(t, lanes, stride=rows), :][None]
        filt_ref[pl.ds(t, lanes, stride=rows), :] = jnp.sum(r * x, axis=0)
        tb = rows - 1 - t
        a = p * a + up_ref[pl.ds(tb, lanes, stride=rows), :][None]
        mg_ref[pl.ds(tb, lanes, stride=rows), :] = jnp.sum(r * a, axis=0)
        return x, a

    lax.fori_loop(0, rows, body, (s_ref[...], b_ref[...]), unroll=2)
    for c in range(lanes):
        cols = slice(c * LANE, (c + 1) * LANE)
        band = slice(c * rows, (c + 1) * rows)
        filt = filt_ref[band, :]
        mg = mg_ref[band, :]
        ho_ref[:, cols] = (q_ref[:, cols].astype(f32) * filt).astype(jnp.bfloat16)
        qg_ref[:, cols] = (g_ref[:, cols].astype(f32) * filt).astype(jnp.bfloat16)
        kg_ref[:, cols] = (mg * v_ref[:, cols].astype(f32)).astype(jnp.bfloat16)
        vg_ref[:, cols] = (mg * k_ref[:, cols].astype(f32)).astype(jnp.bfloat16)


def local_carries(query_proj, key_proj, value_proj, out_grad, factor):
    rows, width = query_proj.shape
    modes = factor.shape[0]
    big = pl.BlockSpec((rows, BLOCK), lambda i: (0, i))
    small = pl.BlockSpec((modes, BLOCK), lambda i: (0, i))
    return pl.pallas_call(
        carry_kernel,
        grid=(width // BLOCK,),
        in_specs=[big, big, big, big, small],
        out_specs=[small, small, small],
        out_shape=[jax.ShapeDtypeStruct((modes, width), jnp.float32)] * 3,
        scratch_shapes=[pltpu.VMEM((rows, BLOCK), jnp.float32)] * 2,
    )(query_proj, key_proj, value_proj, out_grad, factor)


def full_scans(query_proj, key_proj, value_proj, out_grad, factor, weight, state_in, adjoint_in):
    rows, width = query_proj.shape
    modes = factor.shape[0]
    lanes = BLOCK // LANE
    big = pl.BlockSpec((rows, BLOCK), lambda i: (0, i))
    small = pl.BlockSpec((modes, lanes, LANE), lambda i: (0, i, 0))
    out_big = jax.ShapeDtypeStruct((rows, width), jnp.bfloat16)
    tiles = [a.reshape(modes, width // LANE, LANE) for a in (factor, weight, state_in, adjoint_in)]
    return pl.pallas_call(
        main_kernel,
        grid=(width // BLOCK,),
        in_specs=[big, big, big, big, small, small, small, small],
        out_specs=[big, big, big, big],
        out_shape=[out_big] * 4,
        scratch_shapes=[pltpu.VMEM((lanes * rows, LANE), jnp.float32)] * 4,
    )(query_proj, key_proj, value_proj, out_grad, *tiles)


def make_on_device(count):
    def on_device(query_proj, key_proj, value_proj, out_grad, decay_rate, residue, group_of):
        high = lax.Precision.HIGHEST
        rows = query_proj.shape[0]
        group_count = decay_rate.shape[0]
        member = (group_of[None, :] == jnp.arange(group_count, dtype=jnp.int32)[:, None]).astype(
            jnp.float32
        )
        rate = jnp.dot(decay_rate.T, member, precision=high)
        weight = jnp.dot(residue.T, member, precision=high)
        factor = jnp.exp(-rate)
        end_state, head_adjoint, local_total = local_carries(
            query_proj, key_proj, value_proj, out_grad, factor
        )

        def span(blocks):
            return jnp.exp(-rate * (blocks * float(rows)))

        def grouped(a):
            return jnp.dot(a, member.T, precision=high)

        place = lax.axis_index("ctx")
        fwd_cube = end_state
        bwd_cube = head_adjoint
        grad_cube = grouped(local_total)
        state_in = jnp.zeros_like(end_state)
        adjoint_in = jnp.zeros_like(head_adjoint)
        bit = 1
        while bit < count:
            pairs = [(i, i ^ bit) for i in range(count)]
            width = fwd_cube.shape[1]
            packed = jnp.concatenate([fwd_cube, bwd_cube, grad_cube], axis=1)
            if bit == 1:
                got = lax.ppermute(packed, "ctx", pairs)
            else:
                half = packed.shape[1] // 2
                core = place % 2
                mine = lax.dynamic_slice_in_dim(packed, core * half, half, axis=1)
                got_mine = lax.ppermute(mine, "ctx", pairs)
                got_other = lax.ppermute(got_mine, "ctx", [(i, i ^ 1) for i in range(count)])
                first = jnp.where(core == 0, got_mine, got_other)
                second = jnp.where(core == 0, got_other, got_mine)
                got = jnp.concatenate([first, second], axis=1)
            got_fwd = got[:, :width]
            got_bwd = got[:, width : 2 * width]
            got_grad = got[:, 2 * width :]
            upper = (place & bit) != 0
            offset = (place % bit).astype(jnp.float32)
            low_fwd = jnp.where(upper, got_fwd, fwd_cube)
            high_fwd = jnp.where(upper, fwd_cube, got_fwd)
            low_bwd = jnp.where(upper, got_bwd, bwd_cube)
            high_bwd = jnp.where(upper, bwd_cube, got_bwd)
            low_grad = jnp.where(upper, got_grad, grad_cube)
            high_grad = jnp.where(upper, grad_cube, got_grad)
            state_in = state_in + jnp.where(upper, span(offset) * got_fwd, 0.0)
            adjoint_in = adjoint_in + jnp.where(upper, 0.0, span(bit - 1 - offset) * got_bwd)
            whole = span(bit)
            grad_cube = (low_grad + high_grad) + grouped((factor * low_fwd) * high_bwd)
            fwd_cube = high_fwd + whole * low_fwd
            bwd_cube = low_bwd + whole * high_bwd
            bit *= 2

        hyena_out, query_grad, key_grad, value_grad = full_scans(
            query_proj, key_proj, value_proj, out_grad, factor, weight, state_in, adjoint_in
        )
        filter_grad = grad_cube.T
        filter_update = filter_grad / jnp.sqrt(jnp.mean(filter_grad * filter_grad) + 1e-06)
        return (hyena_out, query_grad, key_grad, value_grad, filter_update)

    return on_device


def solution(mesh):
    placed = (
        P(("groups", "ctx"), None),
        P(("groups", "ctx"), None),
        P(("groups", "ctx"), None),
        P(("groups", "ctx"), None),
        P(),
        P(),
        P(),
    )
    return jax.shard_map(
        make_on_device(mesh.shape["ctx"]),
        mesh=mesh,
        in_specs=placed,
        out_specs=(
            P(("groups", "ctx"), None),
            P(("groups", "ctx"), None),
            P(("groups", "ctx"), None),
            P(("groups", "ctx"), None),
            P("groups", None),
        ),
        check_vma=False,
    )
```

```python
import jax
import jax.numpy as jnp
from jax import lax
from jax.experimental import pallas as pl
from jax.experimental.pallas import tpu as pltpu
from jax.sharding import PartitionSpec as P

BLOCK = 1024
SUB = 256
ROWS = 8
LANE = 128


def carry_kernel(q_ref, k_ref, v_ref, g_ref, p_ref, xend_ref, head_ref, tot_ref, mix_ref, up_ref):
    f32 = jnp.float32
    mix_ref[...] = (k_ref[...].astype(f32) * v_ref[...].astype(f32)).astype(jnp.bfloat16).astype(f32)
    up_ref[...] = g_ref[...].astype(f32) * q_ref[...].astype(f32)
    rows, width = mix_ref.shape
    chunks = rows // ROWS
    for h in range(width // SUB):
        cols = pl.ds(h * SUB, SUB)
        p = p_ref[:, cols]

        def body(c, carry):
            x, tot, a = carry
            fb = pl.multiple_of(c * ROWS, ROWS)
            bb = pl.multiple_of((chunks - 1 - c) * ROWS, ROWS)
            mt = mix_ref[pl.ds(fb, ROWS), cols]
            ut = up_ref[pl.ds(fb, ROWS), cols]
            ub = up_ref[pl.ds(bb, ROWS), cols]
            for j in range(ROWS):
                x = p * x + mt[j : j + 1, :]
                tot = tot + ut[j : j + 1, :] * x
                jb = ROWS - 1 - j
                a = p * a + ub[jb : jb + 1, :]
            return x, tot, a

        zero = jnp.zeros(p.shape, f32)
        x, tot, a = lax.fori_loop(0, chunks, body, (zero, zero, zero))
        xend_ref[:, cols] = x
        head_ref[:, cols] = a
        tot_ref[:, cols] = tot


def local_kernel(q_ref, k_ref, v_ref, g_ref, p_ref, r_ref, *refs):
    f32 = jnp.float32
    if len(refs) == 8:
        refs = refs[2:]
    filt_out, mg_out, mix_ref, up_ref, filt_ref, mg_ref = refs
    rows, width = q_ref.shape
    lanes = width // LANE
    for c in range(lanes):
        cols = slice(c * LANE, (c + 1) * LANE)
        band = slice(c * rows, (c + 1) * rows)
        kf = k_ref[:, cols].astype(f32)
        vf = v_ref[:, cols].astype(f32)
        mix_ref[band, :] = (kf * vf).astype(jnp.bfloat16).astype(f32)
        up_ref[band, :] = g_ref[:, cols].astype(f32) * q_ref[:, cols].astype(f32)

    def body(t, carry):
        x, a = carry
        p = p_ref[...]
        r = r_ref[...]
        x = p * x + mix_ref[pl.ds(t, lanes, stride=rows), :][None]
        filt_ref[pl.ds(t, lanes, stride=rows), :] = jnp.sum(r * x, axis=0)
        tb = rows - 1 - t
        a = p * a + up_ref[pl.ds(tb, lanes, stride=rows), :][None]
        mg_ref[pl.ds(tb, lanes, stride=rows), :] = jnp.sum(r * a, axis=0)
        return x, a

    zero = jnp.zeros(p_ref.shape, f32)
    lax.fori_loop(0, rows, body, (zero, zero), unroll=2)
    for c in range(lanes):
        cols = slice(c * LANE, (c + 1) * LANE)
        band = slice(c * rows, (c + 1) * rows)
        filt_out[:, cols] = filt_ref[band, :]
        mg_out[:, cols] = mg_ref[band, :]


def correct_kernel(
    q_ref, k_ref, v_ref, g_ref, fl_ref, ml_ref, p_ref, r_ref, s_ref, b_ref,
    ho_ref, qg_ref, kg_ref, vg_ref,
    filt_ref, mg_ref,
):
    f32 = jnp.float32
    rows, width = q_ref.shape
    lanes = width // LANE

    def body(t, carry):
        z, w = carry
        p = p_ref[...]
        filt_ref[pl.ds(t, lanes, stride=rows), :] = jnp.sum(z, axis=0)
        tb = rows - 1 - t
        mg_ref[pl.ds(tb, lanes, stride=rows), :] = jnp.sum(w, axis=0)
        return z * p, w * p

    p = p_ref[...]
    r = r_ref[...]
    lax.fori_loop(0, rows, body, ((r * p) * s_ref[...], (r * p) * b_ref[...]), unroll=2)
    for c in range(lanes):
        cols = slice(c * LANE, (c + 1) * LANE)
        band = slice(c * rows, (c + 1) * rows)
        filt = fl_ref[:, cols] + filt_ref[band, :]
        mg = ml_ref[:, cols] + mg_ref[band, :]
        ho_ref[:, cols] = (q_ref[:, cols].astype(f32) * filt).astype(jnp.bfloat16)
        qg_ref[:, cols] = (g_ref[:, cols].astype(f32) * filt).astype(jnp.bfloat16)
        kg_ref[:, cols] = (mg * v_ref[:, cols].astype(f32)).astype(jnp.bfloat16)
        vg_ref[:, cols] = (mg * k_ref[:, cols].astype(f32)).astype(jnp.bfloat16)


def local_carries(query_proj, key_proj, value_proj, out_grad, factor):
    rows, width = query_proj.shape
    modes = factor.shape[0]
    big = pl.BlockSpec((rows, BLOCK), lambda i: (0, i))
    small = pl.BlockSpec((modes, BLOCK), lambda i: (0, i))
    return pl.pallas_call(
        carry_kernel,
        grid=(width // BLOCK,),
        in_specs=[big, big, big, big, small],
        out_specs=[small, small, small],
        out_shape=[jax.ShapeDtypeStruct((modes, width), jnp.float32)] * 3,
        scratch_shapes=[pltpu.VMEM((rows, BLOCK), jnp.float32)] * 2,
    )(query_proj, key_proj, value_proj, out_grad, factor)


def local_scans(query_proj, key_proj, value_proj, out_grad, factor4, weight4, first, previous):
    rows, width = query_proj.shape
    modes = factor4.shape[0]
    lanes = BLOCK // LANE
    big = pl.BlockSpec((rows, BLOCK), lambda i: (0, i + first))
    small = pl.BlockSpec((modes, lanes, LANE), lambda i: (0, i + first, 0))
    operands = [query_proj, key_proj, value_proj, out_grad, factor4, weight4]
    specs = [big, big, big, big, small, small]
    aliases = {}
    if previous is not None:
        operands += list(previous)
        specs += [pl.BlockSpec(memory_space=pl.ANY)] * 2
        aliases = {6: 0, 7: 1}
    return pl.pallas_call(
        local_kernel,
        grid=(1,),
        in_specs=specs,
        out_specs=[big, big],
        out_shape=[jax.ShapeDtypeStruct((rows, width), jnp.float32)] * 2,
        scratch_shapes=[pltpu.VMEM((lanes * rows, LANE), jnp.float32)] * 4,
        input_output_aliases=aliases,
    )(*operands)


def corrected(query_proj, key_proj, value_proj, out_grad, local, factor4, weight4, state_in, adjoint_in):
    rows, width = query_proj.shape
    modes = factor4.shape[0]
    lanes = BLOCK // LANE
    big = pl.BlockSpec((rows, BLOCK), lambda i: (0, i))
    small = pl.BlockSpec((modes, lanes, LANE), lambda i: (0, i, 0))
    out_big = jax.ShapeDtypeStruct((rows, width), jnp.bfloat16)
    tiles = [a.reshape(modes, width // LANE, LANE) for a in (state_in, adjoint_in)]
    return pl.pallas_call(
        correct_kernel,
        grid=(width // BLOCK,),
        in_specs=[big] * 6 + [small] * 4,
        out_specs=[big, big, big, big],
        out_shape=[out_big] * 4,
        scratch_shapes=[pltpu.VMEM((lanes * rows, LANE), jnp.float32)] * 2,
    )(query_proj, key_proj, value_proj, out_grad, *local, factor4, weight4, *tiles)


def make_on_device(count):
    def on_device(query_proj, key_proj, value_proj, out_grad, decay_rate, residue, group_of):
        high = lax.Precision.HIGHEST
        rows = query_proj.shape[0]
        group_count = decay_rate.shape[0]
        member = (group_of[None, :] == jnp.arange(group_count, dtype=jnp.int32)[:, None]).astype(
            jnp.float32
        )
        rate = jnp.dot(decay_rate.T, member, precision=high)
        weight = jnp.dot(residue.T, member, precision=high)
        factor = jnp.exp(-rate)
        end_state, head_adjoint, local_total = local_carries(
            query_proj, key_proj, value_proj, out_grad, factor
        )
        width = query_proj.shape[1]
        modes = factor.shape[0]
        factor4 = factor.reshape(modes, width // LANE, LANE)
        weight4 = weight.reshape(modes, width // LANE, LANE)
        pieces = width // BLOCK
        local = None
        made = 0

        def span(blocks):
            return jnp.exp(-rate * (blocks * float(rows)))

        def grouped(a):
            return jnp.dot(a, member.T, precision=high)

        place = lax.axis_index("ctx")
        fwd_cube = end_state
        bwd_cube = head_adjoint
        grad_cube = grouped(local_total)
        state_in = jnp.zeros_like(end_state)
        adjoint_in = jnp.zeros_like(head_adjoint)
        bit = 1
        level = 0
        while bit < count:
            pairs = [(i, i ^ bit) for i in range(count)]
            packed = jnp.concatenate([fwd_cube, bwd_cube, grad_cube], axis=1)
            need = min(pieces, level)
            level += 1
            if bit == 1:
                got = lax.ppermute(packed, "ctx", pairs)
            else:
                half = packed.shape[1] // 2
                core = place % 2
                mine = lax.dynamic_slice_in_dim(packed, core * half, half, axis=1)
                got_mine = lax.ppermute(mine, "ctx", pairs)
                if need > made:
                    while made < need:
                        local = local_scans(
                            query_proj, key_proj, value_proj, out_grad, factor4, weight4, made,
                            local,
                        )
                        made += 1
                    got_mine, local = lax.optimization_barrier((got_mine, local))
                got_other = lax.ppermute(got_mine, "ctx", [(i, i ^ 1) for i in range(count)])
                first = jnp.where(core == 0, got_mine, got_other)
                second = jnp.where(core == 0, got_other, got_mine)
                got = jnp.concatenate([first, second], axis=1)
            got_fwd = got[:, :width]
            got_bwd = got[:, width : 2 * width]
            got_grad = got[:, 2 * width :]
            upper = (place & bit) != 0
            offset = (place % bit).astype(jnp.float32)
            low_fwd = jnp.where(upper, got_fwd, fwd_cube)
            high_fwd = jnp.where(upper, fwd_cube, got_fwd)
            low_bwd = jnp.where(upper, got_bwd, bwd_cube)
            high_bwd = jnp.where(upper, bwd_cube, got_bwd)
            low_grad = jnp.where(upper, got_grad, grad_cube)
            high_grad = jnp.where(upper, grad_cube, got_grad)
            state_in = state_in + jnp.where(upper, span(offset) * got_fwd, 0.0)
            adjoint_in = adjoint_in + jnp.where(upper, 0.0, span(bit - 1 - offset) * got_bwd)
            whole = span(bit)
            grad_cube = (low_grad + high_grad) + grouped((factor * low_fwd) * high_bwd)
            fwd_cube = high_fwd + whole * low_fwd
            bwd_cube = low_bwd + whole * high_bwd
            bit *= 2

        while made < pieces:
            local = local_scans(
                query_proj, key_proj, value_proj, out_grad, factor4, weight4, made, local
            )
            made += 1
        hyena_out, query_grad, key_grad, value_grad = corrected(
            query_proj, key_proj, value_proj, out_grad, local, factor4, weight4, state_in, adjoint_in
        )
        filter_grad = grad_cube.T
        filter_update = filter_grad / jnp.sqrt(jnp.mean(filter_grad * filter_grad) + 1e-06)
        return (hyena_out, query_grad, key_grad, value_grad, filter_update)

    return on_device


def solution(mesh):
    placed = (
        P(("groups", "ctx"), None),
        P(("groups", "ctx"), None),
        P(("groups", "ctx"), None),
        P(("groups", "ctx"), None),
        P(),
        P(),
        P(),
    )
    return jax.shard_map(
        make_on_device(mesh.shape["ctx"]),
        mesh=mesh,
        in_specs=placed,
        out_specs=(
            P(("groups", "ctx"), None),
            P(("groups", "ctx"), None),
            P(("groups", "ctx"), None),
            P(("groups", "ctx"), None),
            P("groups", None),
        ),
        check_vma=False,
    )
```

```python
import jax
import jax.numpy as jnp
from jax import lax
from jax.experimental import pallas as pl
from jax.experimental.pallas import tpu as pltpu
from jax.sharding import PartitionSpec as P

BLOCK = 1024
SUB = 256
ROWS = 8
LANE = 128


def carry_kernel(q_ref, k_ref, v_ref, g_ref, p_ref, xend_ref, head_ref, tot_ref, mix_ref, up_ref):
    f32 = jnp.float32
    mix_ref[...] = (k_ref[...].astype(f32) * v_ref[...].astype(f32)).astype(jnp.bfloat16).astype(f32)
    up_ref[...] = g_ref[...].astype(f32) * q_ref[...].astype(f32)
    rows, width = mix_ref.shape
    chunks = rows // ROWS
    for h in range(width // SUB):
        cols = pl.ds(h * SUB, SUB)
        p = p_ref[:, cols]

        def body(c, carry):
            x, tot, a = carry
            fb = pl.multiple_of(c * ROWS, ROWS)
            bb = pl.multiple_of((chunks - 1 - c) * ROWS, ROWS)
            mt = mix_ref[pl.ds(fb, ROWS), cols]
            ut = up_ref[pl.ds(fb, ROWS), cols]
            ub = up_ref[pl.ds(bb, ROWS), cols]
            for j in range(ROWS):
                x = p * x + mt[j : j + 1, :]
                tot = tot + ut[j : j + 1, :] * x
                jb = ROWS - 1 - j
                a = p * a + ub[jb : jb + 1, :]
            return x, tot, a

        zero = jnp.zeros(p.shape, f32)
        x, tot, a = lax.fori_loop(0, chunks, body, (zero, zero, zero))
        xend_ref[:, cols] = x
        head_ref[:, cols] = a
        tot_ref[:, cols] = tot


def local_kernel(q_ref, k_ref, v_ref, g_ref, p_ref, r_ref, *refs):
    f32 = jnp.float32
    if len(refs) == 8:
        refs = refs[2:]
    filt_out, mg_out, mix_ref, up_ref, filt_ref, mg_ref = refs
    rows, width = q_ref.shape
    lanes = width // LANE
    for c in range(lanes):
        cols = slice(c * LANE, (c + 1) * LANE)
        band = slice(c * rows, (c + 1) * rows)
        kf = k_ref[:, cols].astype(f32)
        vf = v_ref[:, cols].astype(f32)
        mix_ref[band, :] = (kf * vf).astype(jnp.bfloat16).astype(f32)
        up_ref[band, :] = g_ref[:, cols].astype(f32) * q_ref[:, cols].astype(f32)

    def body(t, carry):
        x, a = carry
        p = p_ref[...]
        r = r_ref[...]
        x = p * x + mix_ref[pl.ds(t, lanes, stride=rows), :][None]
        filt_ref[pl.ds(t, lanes, stride=rows), :] = jnp.sum(r * x, axis=0)
        tb = rows - 1 - t
        a = p * a + up_ref[pl.ds(tb, lanes, stride=rows), :][None]
        mg_ref[pl.ds(tb, lanes, stride=rows), :] = jnp.sum(r * a, axis=0)
        return x, a

    zero = jnp.zeros(p_ref.shape, f32)
    lax.fori_loop(0, rows, body, (zero, zero), unroll=2)
    for c in range(lanes):
        cols = slice(c * LANE, (c + 1) * LANE)
        band = slice(c * rows, (c + 1) * rows)
        filt_out[:, cols] = filt_ref[band, :]
        mg_out[:, cols] = mg_ref[band, :]


def correct_kernel(
    q_ref, k_ref, v_ref, g_ref, fl_ref, ml_ref, p_ref, r_ref, s_ref, b_ref,
    ho_ref, qg_ref, kg_ref, vg_ref,
    filt_ref, mg_ref,
):
    f32 = jnp.float32
    rows, width = q_ref.shape
    lanes = width // LANE

    def body(t, carry):
        z, w = carry
        p = p_ref[...]
        filt_ref[pl.ds(t, lanes, stride=rows), :] = jnp.sum(z, axis=0)
        tb = rows - 1 - t
        mg_ref[pl.ds(tb, lanes, stride=rows), :] = jnp.sum(w, axis=0)
        return z * p, w * p

    p = p_ref[...]
    r = r_ref[...]
    lax.fori_loop(0, rows, body, ((r * p) * s_ref[...], (r * p) * b_ref[...]), unroll=2)
    for c in range(lanes):
        cols = slice(c * LANE, (c + 1) * LANE)
        band = slice(c * rows, (c + 1) * rows)
        filt = fl_ref[:, cols] + filt_ref[band, :]
        mg = ml_ref[:, cols] + mg_ref[band, :]
        ho_ref[:, cols] = (q_ref[:, cols].astype(f32) * filt).astype(jnp.bfloat16)
        qg_ref[:, cols] = (g_ref[:, cols].astype(f32) * filt).astype(jnp.bfloat16)
        kg_ref[:, cols] = (mg * v_ref[:, cols].astype(f32)).astype(jnp.bfloat16)
        vg_ref[:, cols] = (mg * k_ref[:, cols].astype(f32)).astype(jnp.bfloat16)


def local_carries(query_proj, key_proj, value_proj, out_grad, factor):
    rows, width = query_proj.shape
    modes = factor.shape[0]
    big = pl.BlockSpec((rows, BLOCK), lambda i: (0, i))
    small = pl.BlockSpec((modes, BLOCK), lambda i: (0, i))
    return pl.pallas_call(
        carry_kernel,
        grid=(width // BLOCK,),
        in_specs=[big, big, big, big, small],
        out_specs=[small, small, small],
        out_shape=[jax.ShapeDtypeStruct((modes, width), jnp.float32)] * 3,
        scratch_shapes=[pltpu.VMEM((rows, BLOCK), jnp.float32)] * 2,
    )(query_proj, key_proj, value_proj, out_grad, factor)


def local_scans(query_proj, key_proj, value_proj, out_grad, factor4, weight4, first, previous):
    rows, width = query_proj.shape
    modes = factor4.shape[0]
    lanes = BLOCK // LANE
    big = pl.BlockSpec((rows, BLOCK), lambda i: (0, i + first))
    small = pl.BlockSpec((modes, lanes, LANE), lambda i: (0, i + first, 0))
    operands = [query_proj, key_proj, value_proj, out_grad, factor4, weight4]
    specs = [big, big, big, big, small, small]
    aliases = {}
    if previous is not None:
        operands += list(previous)
        specs += [pl.BlockSpec(memory_space=pl.ANY)] * 2
        aliases = {6: 0, 7: 1}
    return pl.pallas_call(
        local_kernel,
        grid=(1,),
        in_specs=specs,
        out_specs=[big, big],
        out_shape=[jax.ShapeDtypeStruct((rows, width), jnp.float32)] * 2,
        scratch_shapes=[pltpu.VMEM((lanes * rows, LANE), jnp.float32)] * 4,
        input_output_aliases=aliases,
    )(*operands)


def corrected(query_proj, key_proj, value_proj, out_grad, local, factor4, weight4, state_in, adjoint_in):
    rows, width = query_proj.shape
    modes = factor4.shape[0]
    lanes = BLOCK // LANE
    big = pl.BlockSpec((rows, BLOCK), lambda i: (0, i))
    small = pl.BlockSpec((modes, lanes, LANE), lambda i: (0, i, 0))
    out_big = jax.ShapeDtypeStruct((rows, width), jnp.bfloat16)
    tiles = [a.reshape(modes, width // LANE, LANE) for a in (state_in, adjoint_in)]
    return pl.pallas_call(
        correct_kernel,
        grid=(width // BLOCK,),
        in_specs=[big] * 6 + [small] * 4,
        out_specs=[big, big, big, big],
        out_shape=[out_big] * 4,
        scratch_shapes=[pltpu.VMEM((lanes * rows, LANE), jnp.float32)] * 2,
    )(query_proj, key_proj, value_proj, out_grad, *local, factor4, weight4, *tiles)


def make_on_device(count):
    def on_device(query_proj, key_proj, value_proj, out_grad, decay_rate, residue, group_of):
        high = lax.Precision.HIGHEST
        rows = query_proj.shape[0]
        group_count = decay_rate.shape[0]
        member = (group_of[None, :] == jnp.arange(group_count, dtype=jnp.int32)[:, None]).astype(
            jnp.float32
        )
        rate = jnp.dot(decay_rate.T, member, precision=high)
        weight = jnp.dot(residue.T, member, precision=high)
        factor = jnp.exp(-rate)
        end_state, head_adjoint, local_total = local_carries(
            query_proj, key_proj, value_proj, out_grad, factor
        )
        width = query_proj.shape[1]
        modes = factor.shape[0]
        factor4 = factor.reshape(modes, width // LANE, LANE)
        weight4 = weight.reshape(modes, width // LANE, LANE)
        pieces = width // BLOCK
        local = None
        made = 0

        def span(blocks):
            return jnp.exp(-rate * (blocks * float(rows)))

        def grouped(a):
            return jnp.dot(a, member.T, precision=high)

        place = lax.axis_index("ctx")
        fwd_cube = end_state
        bwd_cube = head_adjoint
        grad_cube = grouped(local_total)
        state_in = jnp.zeros_like(end_state)
        adjoint_in = jnp.zeros_like(head_adjoint)
        bit = 1
        level = 0
        while bit < count:
            pairs = [(i, i ^ bit) for i in range(count)]
            packed = jnp.concatenate([fwd_cube, bwd_cube, grad_cube], axis=1)
            need = pieces if bit * 2 >= count else min(pieces, level)
            level += 1
            if bit == 1:
                got = lax.ppermute(packed, "ctx", pairs)
            else:
                half = packed.shape[1] // 2
                core = place % 2
                mine = lax.dynamic_slice_in_dim(packed, core * half, half, axis=1)
                got_mine = lax.ppermute(mine, "ctx", pairs)
                if need > made:
                    while made < need:
                        local = local_scans(
                            query_proj, key_proj, value_proj, out_grad, factor4, weight4, made,
                            local,
                        )
                        made += 1
                    got_mine, local = lax.optimization_barrier((got_mine, local))
                got_other = lax.ppermute(got_mine, "ctx", [(i, i ^ 1) for i in range(count)])
                first = jnp.where(core == 0, got_mine, got_other)
                second = jnp.where(core == 0, got_other, got_mine)
                got = jnp.concatenate([first, second], axis=1)
            got_fwd = got[:, :width]
            got_bwd = got[:, width : 2 * width]
            got_grad = got[:, 2 * width :]
            upper = (place & bit) != 0
            offset = (place % bit).astype(jnp.float32)
            low_fwd = jnp.where(upper, got_fwd, fwd_cube)
            high_fwd = jnp.where(upper, fwd_cube, got_fwd)
            low_bwd = jnp.where(upper, got_bwd, bwd_cube)
            high_bwd = jnp.where(upper, bwd_cube, got_bwd)
            low_grad = jnp.where(upper, got_grad, grad_cube)
            high_grad = jnp.where(upper, grad_cube, got_grad)
            state_in = state_in + jnp.where(upper, span(offset) * got_fwd, 0.0)
            adjoint_in = adjoint_in + jnp.where(upper, 0.0, span(bit - 1 - offset) * got_bwd)
            whole = span(bit)
            grad_cube = (low_grad + high_grad) + grouped((factor * low_fwd) * high_bwd)
            fwd_cube = high_fwd + whole * low_fwd
            bwd_cube = low_bwd + whole * high_bwd
            bit *= 2

        while made < pieces:
            local = local_scans(
                query_proj, key_proj, value_proj, out_grad, factor4, weight4, made, local
            )
            made += 1
        hyena_out, query_grad, key_grad, value_grad = corrected(
            query_proj, key_proj, value_proj, out_grad, local, factor4, weight4, state_in, adjoint_in
        )
        filter_grad = grad_cube.T
        filter_update = filter_grad / jnp.sqrt(jnp.mean(filter_grad * filter_grad) + 1e-06)
        return (hyena_out, query_grad, key_grad, value_grad, filter_update)

    return on_device


def solution(mesh):
    placed = (
        P(("groups", "ctx"), None),
        P(("groups", "ctx"), None),
        P(("groups", "ctx"), None),
        P(("groups", "ctx"), None),
        P(),
        P(),
        P(),
    )
    return jax.shard_map(
        make_on_device(mesh.shape["ctx"]),
        mesh=mesh,
        in_specs=placed,
        out_specs=(
            P(("groups", "ctx"), None),
            P(("groups", "ctx"), None),
            P(("groups", "ctx"), None),
            P(("groups", "ctx"), None),
            P("groups", None),
        ),
        check_vma=False,
    )
```

```python
import jax
import jax.numpy as jnp
from jax import lax
from jax.experimental import pallas as pl
from jax.experimental.pallas import tpu as pltpu
from jax.sharding import PartitionSpec as P

BLOCK = 1024
SUB = 256
ROWS = 8
LANE = 128


def carry_kernel(q_ref, k_ref, v_ref, g_ref, p_ref, xend_ref, head_ref, tot_ref, mix_ref, up_ref):
    f32 = jnp.float32
    mix_ref[...] = (k_ref[...].astype(f32) * v_ref[...].astype(f32)).astype(jnp.bfloat16).astype(f32)
    up_ref[...] = g_ref[...].astype(f32) * q_ref[...].astype(f32)
    rows, width = mix_ref.shape
    chunks = rows // ROWS
    for h in range(width // SUB):
        cols = pl.ds(h * SUB, SUB)
        p = p_ref[:, cols]

        def body(c, carry):
            x, tot, a = carry
            fb = pl.multiple_of(c * ROWS, ROWS)
            bb = pl.multiple_of((chunks - 1 - c) * ROWS, ROWS)
            mt = mix_ref[pl.ds(fb, ROWS), cols]
            ut = up_ref[pl.ds(fb, ROWS), cols]
            ub = up_ref[pl.ds(bb, ROWS), cols]
            for j in range(ROWS):
                x = p * x + mt[j : j + 1, :]
                tot = tot + ut[j : j + 1, :] * x
                jb = ROWS - 1 - j
                a = p * a + ub[jb : jb + 1, :]
            return x, tot, a

        zero = jnp.zeros(p.shape, f32)
        x, tot, a = lax.fori_loop(0, chunks, body, (zero, zero, zero))
        xend_ref[:, cols] = x
        head_ref[:, cols] = a
        tot_ref[:, cols] = tot


def local_kernel(q_ref, k_ref, v_ref, g_ref, p_ref, r_ref, *refs):
    f32 = jnp.float32
    if len(refs) == 8:
        refs = refs[2:]
    filt_out, mg_out, mix_ref, up_ref, filt_ref, mg_ref = refs
    rows, width = q_ref.shape
    lanes = width // LANE
    for c in range(lanes):
        cols = slice(c * LANE, (c + 1) * LANE)
        band = slice(c * rows, (c + 1) * rows)
        kf = k_ref[:, cols].astype(f32)
        vf = v_ref[:, cols].astype(f32)
        mix_ref[band, :] = (kf * vf).astype(jnp.bfloat16).astype(f32)
        up_ref[band, :] = g_ref[:, cols].astype(f32) * q_ref[:, cols].astype(f32)

    def body(t, carry):
        x, a = carry
        p = p_ref[...]
        r = r_ref[...]
        x = p * x + mix_ref[pl.ds(t, lanes, stride=rows), :][None]
        filt_ref[pl.ds(t, lanes, stride=rows), :] = jnp.sum(r * x, axis=0)
        tb = rows - 1 - t
        a = p * a + up_ref[pl.ds(tb, lanes, stride=rows), :][None]
        mg_ref[pl.ds(tb, lanes, stride=rows), :] = jnp.sum(r * a, axis=0)
        return x, a

    zero = jnp.zeros(p_ref.shape, f32)
    lax.fori_loop(0, rows, body, (zero, zero), unroll=2)
    for c in range(lanes):
        cols = slice(c * LANE, (c + 1) * LANE)
        band = slice(c * rows, (c + 1) * rows)
        filt_out[:, cols] = filt_ref[band, :]
        mg_out[:, cols] = mg_ref[band, :]


def correct_kernel(
    q_ref, k_ref, v_ref, g_ref, fl_ref, ml_ref, p_ref, r_ref, s_ref, b_ref,
    ho_ref, qg_ref, kg_ref, vg_ref,
    filt_ref, mg_ref,
):
    f32 = jnp.float32
    rows, width = q_ref.shape
    lanes = width // LANE

    def body(t, carry):
        z, w = carry
        p = p_ref[...]
        filt_ref[pl.ds(t, lanes, stride=rows), :] = jnp.sum(z, axis=0)
        tb = rows - 1 - t
        mg_ref[pl.ds(tb, lanes, stride=rows), :] = jnp.sum(w, axis=0)
        return z * p, w * p

    p = p_ref[...]
    r = r_ref[...]
    lax.fori_loop(0, rows, body, ((r * p) * s_ref[...], (r * p) * b_ref[...]), unroll=2)
    for c in range(lanes):
        cols = slice(c * LANE, (c + 1) * LANE)
        band = slice(c * rows, (c + 1) * rows)
        filt = fl_ref[:, cols] + filt_ref[band, :]
        mg = ml_ref[:, cols] + mg_ref[band, :]
        ho_ref[:, cols] = (q_ref[:, cols].astype(f32) * filt).astype(jnp.bfloat16)
        qg_ref[:, cols] = (g_ref[:, cols].astype(f32) * filt).astype(jnp.bfloat16)
        kg_ref[:, cols] = (mg * v_ref[:, cols].astype(f32)).astype(jnp.bfloat16)
        vg_ref[:, cols] = (mg * k_ref[:, cols].astype(f32)).astype(jnp.bfloat16)


def local_carries(query_proj, key_proj, value_proj, out_grad, factor):
    rows, width = query_proj.shape
    modes = factor.shape[0]
    big = pl.BlockSpec((rows, BLOCK), lambda i: (0, i))
    small = pl.BlockSpec((modes, BLOCK), lambda i: (0, i))
    return pl.pallas_call(
        carry_kernel,
        grid=(width // BLOCK,),
        in_specs=[big, big, big, big, small],
        out_specs=[small, small, small],
        out_shape=[jax.ShapeDtypeStruct((modes, width), jnp.float32)] * 3,
        scratch_shapes=[pltpu.VMEM((rows, BLOCK), jnp.float32)] * 2,
    )(query_proj, key_proj, value_proj, out_grad, factor)


def local_scans(query_proj, key_proj, value_proj, out_grad, factor4, weight4, first, previous):
    rows, width = query_proj.shape
    modes = factor4.shape[0]
    lanes = BLOCK // LANE
    big = pl.BlockSpec((rows, BLOCK), lambda i: (0, i + first))
    small = pl.BlockSpec((modes, lanes, LANE), lambda i: (0, i + first, 0))
    operands = [query_proj, key_proj, value_proj, out_grad, factor4, weight4]
    specs = [big, big, big, big, small, small]
    aliases = {}
    if previous is not None:
        operands += list(previous)
        specs += [pl.BlockSpec(memory_space=pl.ANY)] * 2
        aliases = {6: 0, 7: 1}
    return pl.pallas_call(
        local_kernel,
        grid=(1,),
        in_specs=specs,
        out_specs=[big, big],
        out_shape=[jax.ShapeDtypeStruct((rows, width), jnp.float32)] * 2,
        scratch_shapes=[pltpu.VMEM((lanes * rows, LANE), jnp.float32)] * 4,
        input_output_aliases=aliases,
    )(*operands)


def corrected(query_proj, key_proj, value_proj, out_grad, local, factor4, weight4, state_in, adjoint_in):
    rows, width = query_proj.shape
    modes = factor4.shape[0]
    lanes = BLOCK // LANE
    big = pl.BlockSpec((rows, BLOCK), lambda i: (0, i))
    small = pl.BlockSpec((modes, lanes, LANE), lambda i: (0, i, 0))
    out_big = jax.ShapeDtypeStruct((rows, width), jnp.bfloat16)
    tiles = [a.reshape(modes, width // LANE, LANE) for a in (state_in, adjoint_in)]
    return pl.pallas_call(
        correct_kernel,
        grid=(width // BLOCK,),
        in_specs=[big] * 6 + [small] * 4,
        out_specs=[big, big, big, big],
        out_shape=[out_big] * 4,
        scratch_shapes=[pltpu.VMEM((lanes * rows, LANE), jnp.float32)] * 2,
    )(query_proj, key_proj, value_proj, out_grad, *local, factor4, weight4, *tiles)


def split_dot(a, member):
    bf16 = jnp.bfloat16
    top = lax.reduce_precision(a, exponent_bits=8, mantissa_bits=7)
    rest = a - top
    middle = lax.reduce_precision(rest, exponent_bits=8, mantissa_bits=7)
    hi = top.astype(bf16)
    mid = middle.astype(bf16)
    lo = (rest - middle).astype(bf16)
    rows = a.shape[0]
    out = jnp.dot(jnp.concatenate([hi, mid, lo], axis=0), member, preferred_element_type=jnp.float32)
    return (out[:rows] + out[rows : 2 * rows]) + out[2 * rows :]


def make_on_device(count):
    def on_device(query_proj, key_proj, value_proj, out_grad, decay_rate, residue, group_of):
        rows = query_proj.shape[0]
        group_count = decay_rate.shape[0]
        member = (group_of[None, :] == jnp.arange(group_count, dtype=jnp.int32)[:, None]).astype(
            jnp.bfloat16
        )
        modes = decay_rate.shape[1]
        params = split_dot(jnp.concatenate([decay_rate.T, residue.T], axis=0), member)
        rate = params[:modes]
        weight = params[modes:]
        factor = jnp.exp(-rate)
        end_state, head_adjoint, local_total = local_carries(
            query_proj, key_proj, value_proj, out_grad, factor
        )
        width = query_proj.shape[1]
        modes = factor.shape[0]
        factor4 = factor.reshape(modes, width // LANE, LANE)
        weight4 = weight.reshape(modes, width // LANE, LANE)
        pieces = width // BLOCK
        local = None
        made = 0

        def span(blocks):
            return jnp.exp(-rate * (blocks * float(rows)))

        member_t = member.T

        def grouped(a):
            return split_dot(a, member_t)

        place = lax.axis_index("ctx")
        fwd_cube = end_state
        bwd_cube = head_adjoint
        grad_cube = grouped(local_total)
        state_in = jnp.zeros_like(end_state)
        adjoint_in = jnp.zeros_like(head_adjoint)
        bit = 1
        level = 0
        while bit < count:
            pairs = [(i, i ^ bit) for i in range(count)]
            packed = jnp.concatenate([fwd_cube, bwd_cube, grad_cube], axis=1)
            need = pieces if bit * 2 >= count else min(pieces, level)
            level += 1
            if bit == 1:
                got = lax.ppermute(packed, "ctx", pairs)
            else:
                half = packed.shape[1] // 2
                core = place % 2
                mine = lax.dynamic_slice_in_dim(packed, core * half, half, axis=1)
                got_mine = lax.ppermute(mine, "ctx", pairs)
                if need > made:
                    while made < need:
                        local = local_scans(
                            query_proj, key_proj, value_proj, out_grad, factor4, weight4, made,
                            local,
                        )
                        made += 1
                    got_mine, local = lax.optimization_barrier((got_mine, local))
                got_other = lax.ppermute(got_mine, "ctx", [(i, i ^ 1) for i in range(count)])
                first = jnp.where(core == 0, got_mine, got_other)
                second = jnp.where(core == 0, got_other, got_mine)
                got = jnp.concatenate([first, second], axis=1)
            got_fwd = got[:, :width]
            got_bwd = got[:, width : 2 * width]
            got_grad = got[:, 2 * width :]
            upper = (place & bit) != 0
            offset = (place % bit).astype(jnp.float32)
            low_fwd = jnp.where(upper, got_fwd, fwd_cube)
            high_fwd = jnp.where(upper, fwd_cube, got_fwd)
            low_bwd = jnp.where(upper, got_bwd, bwd_cube)
            high_bwd = jnp.where(upper, bwd_cube, got_bwd)
            low_grad = jnp.where(upper, got_grad, grad_cube)
            high_grad = jnp.where(upper, grad_cube, got_grad)
            state_in = state_in + jnp.where(upper, span(offset) * got_fwd, 0.0)
            adjoint_in = adjoint_in + jnp.where(upper, 0.0, span(bit - 1 - offset) * got_bwd)
            whole = span(bit)
            grad_cube = (low_grad + high_grad) + grouped((factor * low_fwd) * high_bwd)
            fwd_cube = high_fwd + whole * low_fwd
            bwd_cube = low_bwd + whole * high_bwd
            bit *= 2

        while made < pieces:
            local = local_scans(
                query_proj, key_proj, value_proj, out_grad, factor4, weight4, made, local
            )
            made += 1
        hyena_out, query_grad, key_grad, value_grad = corrected(
            query_proj, key_proj, value_proj, out_grad, local, factor4, weight4, state_in, adjoint_in
        )
        filter_grad = grad_cube.T
        filter_update = filter_grad / jnp.sqrt(jnp.mean(filter_grad * filter_grad) + 1e-06)
        return (hyena_out, query_grad, key_grad, value_grad, filter_update)

    return on_device


def solution(mesh):
    placed = (
        P(("groups", "ctx"), None),
        P(("groups", "ctx"), None),
        P(("groups", "ctx"), None),
        P(("groups", "ctx"), None),
        P(),
        P(),
        P(),
    )
    return jax.shard_map(
        make_on_device(mesh.shape["ctx"]),
        mesh=mesh,
        in_specs=placed,
        out_specs=(
            P(("groups", "ctx"), None),
            P(("groups", "ctx"), None),
            P(("groups", "ctx"), None),
            P(("groups", "ctx"), None),
            P("groups", None),
        ),
        check_vma=False,
    )
```

```python
import jax
import jax.numpy as jnp
from jax import lax
from jax.experimental import pallas as pl
from jax.experimental.pallas import tpu as pltpu
from jax.sharding import PartitionSpec as P

BLOCK = 1024
SUB = 256
ROWS = 8
LANE = 128


def carry_kernel(q_ref, k_ref, v_ref, g_ref, p_ref, xend_ref, head_ref, tot_ref, mix_ref, up_ref):
    f32 = jnp.float32
    mix_ref[...] = (k_ref[...].astype(f32) * v_ref[...].astype(f32)).astype(jnp.bfloat16).astype(f32)
    up_ref[...] = g_ref[...].astype(f32) * q_ref[...].astype(f32)
    rows, width = mix_ref.shape
    chunks = rows // ROWS
    for h in range(width // SUB):
        cols = pl.ds(h * SUB, SUB)
        p = p_ref[:, cols]

        def body(c, carry):
            x, tot, a = carry
            fb = pl.multiple_of(c * ROWS, ROWS)
            bb = pl.multiple_of((chunks - 1 - c) * ROWS, ROWS)
            mt = mix_ref[pl.ds(fb, ROWS), cols]
            ut = up_ref[pl.ds(fb, ROWS), cols]
            ub = up_ref[pl.ds(bb, ROWS), cols]
            for j in range(ROWS):
                x = p * x + mt[j : j + 1, :]
                tot = tot + ut[j : j + 1, :] * x
                jb = ROWS - 1 - j
                a = p * a + ub[jb : jb + 1, :]
            return x, tot, a

        zero = jnp.zeros(p.shape, f32)
        x, tot, a = lax.fori_loop(0, chunks, body, (zero, zero, zero))
        xend_ref[:, cols] = x
        head_ref[:, cols] = a
        tot_ref[:, cols] = tot


def to_modes(src_ref, stage_ref, dst_ref):
    modes, width = src_ref.shape
    lanes = width // LANE
    for c in range(lanes):
        stage_ref[c * modes : (c + 1) * modes, :] = src_ref[:, c * LANE : (c + 1) * LANE]
    for m in range(modes):
        dst_ref[m] = stage_ref[pl.ds(m, lanes, stride=modes), :]


def local_kernel(q_ref, k_ref, v_ref, g_ref, pw_ref, rw_ref, *refs):
    f32 = jnp.float32
    if len(refs) == 11:
        refs = refs[2:]
    filt_out, mg_out, mix_ref, up_ref, filt_ref, mg_ref, stage_ref, p_ref, r_ref = refs
    to_modes(pw_ref, stage_ref, p_ref)
    to_modes(rw_ref, stage_ref, r_ref)
    rows, width = q_ref.shape
    lanes = width // LANE
    for c in range(lanes):
        cols = slice(c * LANE, (c + 1) * LANE)
        band = slice(c * rows, (c + 1) * rows)
        kf = k_ref[:, cols].astype(f32)
        vf = v_ref[:, cols].astype(f32)
        mix_ref[band, :] = (kf * vf).astype(jnp.bfloat16).astype(f32)
        up_ref[band, :] = g_ref[:, cols].astype(f32) * q_ref[:, cols].astype(f32)

    def body(t, carry):
        x, a = carry
        p = p_ref[...]
        r = r_ref[...]
        x = p * x + mix_ref[pl.ds(t, lanes, stride=rows), :][None]
        filt_ref[pl.ds(t, lanes, stride=rows), :] = jnp.sum(r * x, axis=0)
        tb = rows - 1 - t
        a = p * a + up_ref[pl.ds(tb, lanes, stride=rows), :][None]
        mg_ref[pl.ds(tb, lanes, stride=rows), :] = jnp.sum(r * a, axis=0)
        return x, a

    zero = jnp.zeros(p_ref.shape, f32)
    lax.fori_loop(0, rows, body, (zero, zero), unroll=2)
    for c in range(lanes):
        cols = slice(c * LANE, (c + 1) * LANE)
        band = slice(c * rows, (c + 1) * rows)
        filt_out[:, cols] = filt_ref[band, :]
        mg_out[:, cols] = mg_ref[band, :]


def correct_kernel(
    q_ref, k_ref, v_ref, g_ref, fl_ref, ml_ref, pw_ref, rw_ref, sw_ref, bw_ref,
    ho_ref, qg_ref, kg_ref, vg_ref,
    filt_ref, mg_ref, stage_ref, p_ref, r_ref, s_ref, b_ref,
):
    f32 = jnp.float32
    for src, dst in ((pw_ref, p_ref), (rw_ref, r_ref), (sw_ref, s_ref), (bw_ref, b_ref)):
        to_modes(src, stage_ref, dst)
    rows, width = q_ref.shape
    lanes = width // LANE

    def body(t, carry):
        z, w = carry
        p = p_ref[...]
        filt_ref[pl.ds(t, lanes, stride=rows), :] = jnp.sum(z, axis=0)
        tb = rows - 1 - t
        mg_ref[pl.ds(tb, lanes, stride=rows), :] = jnp.sum(w, axis=0)
        return z * p, w * p

    p = p_ref[...]
    r = r_ref[...]
    lax.fori_loop(0, rows, body, ((r * p) * s_ref[...], (r * p) * b_ref[...]), unroll=2)
    for c in range(lanes):
        cols = slice(c * LANE, (c + 1) * LANE)
        band = slice(c * rows, (c + 1) * rows)
        filt = fl_ref[:, cols] + filt_ref[band, :]
        mg = ml_ref[:, cols] + mg_ref[band, :]
        ho_ref[:, cols] = (q_ref[:, cols].astype(f32) * filt).astype(jnp.bfloat16)
        qg_ref[:, cols] = (g_ref[:, cols].astype(f32) * filt).astype(jnp.bfloat16)
        kg_ref[:, cols] = (mg * v_ref[:, cols].astype(f32)).astype(jnp.bfloat16)
        vg_ref[:, cols] = (mg * k_ref[:, cols].astype(f32)).astype(jnp.bfloat16)


def local_carries(query_proj, key_proj, value_proj, out_grad, factor):
    rows, width = query_proj.shape
    modes = factor.shape[0]
    big = pl.BlockSpec((rows, BLOCK), lambda i: (0, i))
    small = pl.BlockSpec((modes, BLOCK), lambda i: (0, i))
    return pl.pallas_call(
        carry_kernel,
        grid=(width // BLOCK,),
        in_specs=[big, big, big, big, small],
        out_specs=[small, small, small],
        out_shape=[jax.ShapeDtypeStruct((modes, width), jnp.float32)] * 3,
        scratch_shapes=[pltpu.VMEM((rows, BLOCK), jnp.float32)] * 2,
    )(query_proj, key_proj, value_proj, out_grad, factor)


def local_scans(query_proj, key_proj, value_proj, out_grad, factor, weight, first, previous):
    rows, width = query_proj.shape
    modes = factor.shape[0]
    lanes = BLOCK // LANE
    big = pl.BlockSpec((rows, BLOCK), lambda i: (0, i + first))
    small = pl.BlockSpec((modes, BLOCK), lambda i: (0, i + first))
    operands = [query_proj, key_proj, value_proj, out_grad, factor, weight]
    specs = [big, big, big, big, small, small]
    aliases = {}
    if previous is not None:
        operands += list(previous)
        specs += [pl.BlockSpec(memory_space=pl.ANY)] * 2
        aliases = {6: 0, 7: 1}
    return pl.pallas_call(
        local_kernel,
        grid=(1,),
        in_specs=specs,
        out_specs=[big, big],
        out_shape=[jax.ShapeDtypeStruct((rows, width), jnp.float32)] * 2,
        scratch_shapes=[pltpu.VMEM((lanes * rows, LANE), jnp.float32)] * 4
        + [pltpu.VMEM((lanes * modes, LANE), jnp.float32)]
        + [pltpu.VMEM((modes, lanes, LANE), jnp.float32)] * 2,
        input_output_aliases=aliases,
    )(*operands)


def corrected(query_proj, key_proj, value_proj, out_grad, local, factor, weight, state_in, adjoint_in):
    rows, width = query_proj.shape
    modes = factor.shape[0]
    lanes = BLOCK // LANE
    big = pl.BlockSpec((rows, BLOCK), lambda i: (0, i))
    small = pl.BlockSpec((modes, BLOCK), lambda i: (0, i))
    out_big = jax.ShapeDtypeStruct((rows, width), jnp.bfloat16)
    return pl.pallas_call(
        correct_kernel,
        grid=(width // BLOCK,),
        in_specs=[big] * 6 + [small] * 4,
        out_specs=[big, big, big, big],
        out_shape=[out_big] * 4,
        scratch_shapes=[pltpu.VMEM((lanes * rows, LANE), jnp.float32)] * 2
        + [pltpu.VMEM((lanes * modes, LANE), jnp.float32)]
        + [pltpu.VMEM((modes, lanes, LANE), jnp.float32)] * 4,
    )(query_proj, key_proj, value_proj, out_grad, *local, factor, weight, state_in, adjoint_in)


def split_dot(a, member):
    bf16 = jnp.bfloat16
    top = lax.reduce_precision(a, exponent_bits=8, mantissa_bits=7)
    rest = a - top
    middle = lax.reduce_precision(rest, exponent_bits=8, mantissa_bits=7)
    hi = top.astype(bf16)
    mid = middle.astype(bf16)
    lo = (rest - middle).astype(bf16)
    rows = a.shape[0]
    out = jnp.dot(jnp.concatenate([hi, mid, lo], axis=0), member, preferred_element_type=jnp.float32)
    return (out[:rows] + out[rows : 2 * rows]) + out[2 * rows :]


def make_on_device(count):
    def on_device(query_proj, key_proj, value_proj, out_grad, decay_rate, residue, group_of):
        rows = query_proj.shape[0]
        group_count = decay_rate.shape[0]
        member = (group_of[None, :] == jnp.arange(group_count, dtype=jnp.int32)[:, None]).astype(
            jnp.bfloat16
        )
        modes = decay_rate.shape[1]
        params = split_dot(jnp.concatenate([decay_rate.T, residue.T], axis=0), member)
        rate = params[:modes]
        weight = params[modes:]
        factor = jnp.exp(-rate)
        end_state, head_adjoint, local_total = local_carries(
            query_proj, key_proj, value_proj, out_grad, factor
        )
        width = query_proj.shape[1]
        modes = factor.shape[0]
        pieces = width // BLOCK
        local = None
        made = 0

        def span(blocks):
            return jnp.exp(-rate * (blocks * float(rows)))

        member_t = member.T

        def grouped(a):
            return split_dot(a, member_t)

        place = lax.axis_index("ctx")
        fwd_cube = end_state
        bwd_cube = head_adjoint
        grad_cube = grouped(local_total)
        state_in = jnp.zeros_like(end_state)
        adjoint_in = jnp.zeros_like(head_adjoint)
        bit = 1
        level = 0
        while bit < count:
            pairs = [(i, i ^ bit) for i in range(count)]
            packed = jnp.concatenate([fwd_cube, bwd_cube, grad_cube], axis=1)
            need = pieces if bit * 2 >= count else min(pieces, level)
            level += 1
            if bit == 1:
                got = lax.ppermute(packed, "ctx", pairs)
            else:
                half = packed.shape[1] // 2
                core = place % 2
                mine = lax.dynamic_slice_in_dim(packed, core * half, half, axis=1)
                got_mine = lax.ppermute(mine, "ctx", pairs)
                if need > made:
                    while made < need:
                        local = local_scans(
                            query_proj, key_proj, value_proj, out_grad, factor, weight, made,
                            local,
                        )
                        made += 1
                    got_mine, local = lax.optimization_barrier((got_mine, local))
                got_other = lax.ppermute(got_mine, "ctx", [(i, i ^ 1) for i in range(count)])
                first = jnp.where(core == 0, got_mine, got_other)
                second = jnp.where(core == 0, got_other, got_mine)
                got = jnp.concatenate([first, second], axis=1)
            got_fwd = got[:, :width]
            got_bwd = got[:, width : 2 * width]
            got_grad = got[:, 2 * width :]
            upper = (place & bit) != 0
            offset = (place % bit).astype(jnp.float32)
            low_fwd = jnp.where(upper, got_fwd, fwd_cube)
            high_fwd = jnp.where(upper, fwd_cube, got_fwd)
            low_bwd = jnp.where(upper, got_bwd, bwd_cube)
            high_bwd = jnp.where(upper, bwd_cube, got_bwd)
            low_grad = jnp.where(upper, got_grad, grad_cube)
            high_grad = jnp.where(upper, grad_cube, got_grad)
            state_in = state_in + jnp.where(upper, span(offset) * got_fwd, 0.0)
            adjoint_in = adjoint_in + jnp.where(upper, 0.0, span(bit - 1 - offset) * got_bwd)
            whole = span(bit)
            grad_cube = (low_grad + high_grad) + grouped((factor * low_fwd) * high_bwd)
            fwd_cube = high_fwd + whole * low_fwd
            bwd_cube = low_bwd + whole * high_bwd
            bit *= 2

        while made < pieces:
            local = local_scans(
                query_proj, key_proj, value_proj, out_grad, factor, weight, made, local
            )
            made += 1
        hyena_out, query_grad, key_grad, value_grad = corrected(
            query_proj, key_proj, value_proj, out_grad, local, factor, weight, state_in, adjoint_in
        )
        filter_grad = grad_cube.T
        filter_update = filter_grad / jnp.sqrt(jnp.mean(filter_grad * filter_grad) + 1e-06)
        return (hyena_out, query_grad, key_grad, value_grad, filter_update)

    return on_device


def solution(mesh):
    placed = (
        P(("groups", "ctx"), None),
        P(("groups", "ctx"), None),
        P(("groups", "ctx"), None),
        P(("groups", "ctx"), None),
        P(),
        P(),
        P(),
    )
    return jax.shard_map(
        make_on_device(mesh.shape["ctx"]),
        mesh=mesh,
        in_specs=placed,
        out_specs=(
            P(("groups", "ctx"), None),
            P(("groups", "ctx"), None),
            P(("groups", "ctx"), None),
            P(("groups", "ctx"), None),
            P("groups", None),
        ),
        check_vma=False,
    )
```

```python
import jax
import jax.numpy as jnp
from jax import lax
from jax.experimental import pallas as pl
from jax.experimental.pallas import tpu as pltpu
from jax.sharding import PartitionSpec as P

BLOCK = 1024
SUB = 256
ROWS = 8
LANE = 128


def carry_kernel(q_ref, k_ref, v_ref, g_ref, p_ref, xend_ref, head_ref, tot_ref, mix_ref, up_ref):
    f32 = jnp.float32
    mix_ref[...] = (k_ref[...].astype(f32) * v_ref[...].astype(f32)).astype(jnp.bfloat16).astype(f32)
    up_ref[...] = g_ref[...].astype(f32) * q_ref[...].astype(f32)
    rows, width = mix_ref.shape
    chunks = rows // ROWS
    for h in range(width // SUB):
        cols = pl.ds(h * SUB, SUB)
        p = p_ref[:, cols]

        def body(c, carry):
            x, tot, a = carry
            fb = pl.multiple_of(c * ROWS, ROWS)
            bb = pl.multiple_of((chunks - 1 - c) * ROWS, ROWS)
            mt = mix_ref[pl.ds(fb, ROWS), cols]
            ut = up_ref[pl.ds(fb, ROWS), cols]
            ub = up_ref[pl.ds(bb, ROWS), cols]
            for j in range(ROWS):
                x = p * x + mt[j : j + 1, :]
                tot = tot + ut[j : j + 1, :] * x
                jb = ROWS - 1 - j
                a = p * a + ub[jb : jb + 1, :]
            return x, tot, a

        zero = jnp.zeros(p.shape, f32)
        x, tot, a = lax.fori_loop(0, chunks, body, (zero, zero, zero))
        xend_ref[:, cols] = x
        head_ref[:, cols] = a
        tot_ref[:, cols] = tot


def to_modes(src_ref, stage_ref, dst_ref):
    modes, width = src_ref.shape
    lanes = width // LANE
    for c in range(lanes):
        stage_ref[c * modes : (c + 1) * modes, :] = src_ref[:, c * LANE : (c + 1) * LANE]
    for m in range(modes):
        dst_ref[m] = stage_ref[pl.ds(m, lanes, stride=modes), :]


def local_kernel(q_ref, k_ref, v_ref, g_ref, pw_ref, rw_ref, *refs):
    f32 = jnp.float32
    if len(refs) == 11:
        refs = refs[2:]
    filt_out, mg_out, mix_ref, up_ref, filt_ref, mg_ref, stage_ref, p_ref, r_ref = refs
    to_modes(pw_ref, stage_ref, p_ref)
    to_modes(rw_ref, stage_ref, r_ref)
    rows, width = q_ref.shape
    lanes = width // LANE
    for c in range(lanes):
        cols = slice(c * LANE, (c + 1) * LANE)
        band = slice(c * rows, (c + 1) * rows)
        kf = k_ref[:, cols].astype(f32)
        vf = v_ref[:, cols].astype(f32)
        mix_ref[band, :] = (kf * vf).astype(jnp.bfloat16).astype(f32)
        up_ref[band, :] = g_ref[:, cols].astype(f32) * q_ref[:, cols].astype(f32)

    def body(t, carry):
        x, a = carry
        p = p_ref[...]
        r = r_ref[...]
        x = p * x + mix_ref[pl.ds(t, lanes, stride=rows), :][None]
        filt_ref[pl.ds(t, lanes, stride=rows), :] = jnp.sum(r * x, axis=0)
        tb = rows - 1 - t
        a = p * a + up_ref[pl.ds(tb, lanes, stride=rows), :][None]
        mg_ref[pl.ds(tb, lanes, stride=rows), :] = jnp.sum(r * a, axis=0)
        return x, a

    zero = jnp.zeros(p_ref.shape, f32)
    lax.fori_loop(0, rows, body, (zero, zero), unroll=2)
    for c in range(lanes):
        cols = slice(c * LANE, (c + 1) * LANE)
        band = slice(c * rows, (c + 1) * rows)
        filt_out[:, cols] = filt_ref[band, :]
        mg_out[:, cols] = mg_ref[band, :]


def correct_kernel(
    q_ref, k_ref, v_ref, g_ref, fl_ref, ml_ref, pw_ref, rw_ref, sw_ref, bw_ref,
    ho_ref, qg_ref, kg_ref, vg_ref,
    filt_ref, mg_ref, stage_ref, p_ref, r_ref, s_ref, b_ref,
):
    f32 = jnp.float32
    for src, dst in ((pw_ref, p_ref), (rw_ref, r_ref), (sw_ref, s_ref), (bw_ref, b_ref)):
        to_modes(src, stage_ref, dst)
    rows, width = q_ref.shape
    lanes = width // LANE

    def body(t, carry):
        z, w = carry
        p = p_ref[...]
        filt_ref[pl.ds(t, lanes, stride=rows), :] = jnp.sum(z, axis=0)
        tb = rows - 1 - t
        mg_ref[pl.ds(tb, lanes, stride=rows), :] = jnp.sum(w, axis=0)
        return z * p, w * p

    p = p_ref[...]
    r = r_ref[...]
    lax.fori_loop(0, rows, body, ((r * p) * s_ref[...], (r * p) * b_ref[...]), unroll=4)
    for c in range(lanes):
        cols = slice(c * LANE, (c + 1) * LANE)
        band = slice(c * rows, (c + 1) * rows)
        filt = fl_ref[:, cols] + filt_ref[band, :]
        mg = ml_ref[:, cols] + mg_ref[band, :]
        ho_ref[:, cols] = (q_ref[:, cols].astype(f32) * filt).astype(jnp.bfloat16)
        qg_ref[:, cols] = (g_ref[:, cols].astype(f32) * filt).astype(jnp.bfloat16)
        kg_ref[:, cols] = (mg * v_ref[:, cols].astype(f32)).astype(jnp.bfloat16)
        vg_ref[:, cols] = (mg * k_ref[:, cols].astype(f32)).astype(jnp.bfloat16)


def local_carries(query_proj, key_proj, value_proj, out_grad, factor):
    rows, width = query_proj.shape
    modes = factor.shape[0]
    big = pl.BlockSpec((rows, BLOCK), lambda i: (0, i))
    small = pl.BlockSpec((modes, BLOCK), lambda i: (0, i))
    return pl.pallas_call(
        carry_kernel,
        grid=(width // BLOCK,),
        in_specs=[big, big, big, big, small],
        out_specs=[small, small, small],
        out_shape=[jax.ShapeDtypeStruct((modes, width), jnp.float32)] * 3,
        scratch_shapes=[pltpu.VMEM((rows, BLOCK), jnp.float32)] * 2,
    )(query_proj, key_proj, value_proj, out_grad, factor)


def local_scans(query_proj, key_proj, value_proj, out_grad, factor, weight, first, previous):
    rows, width = query_proj.shape
    modes = factor.shape[0]
    lanes = BLOCK // LANE
    big = pl.BlockSpec((rows, BLOCK), lambda i: (0, i + first))
    small = pl.BlockSpec((modes, BLOCK), lambda i: (0, i + first))
    operands = [query_proj, key_proj, value_proj, out_grad, factor, weight]
    specs = [big, big, big, big, small, small]
    aliases = {}
    if previous is not None:
        operands += list(previous)
        specs += [pl.BlockSpec(memory_space=pl.ANY)] * 2
        aliases = {6: 0, 7: 1}
    return pl.pallas_call(
        local_kernel,
        grid=(1,),
        in_specs=specs,
        out_specs=[big, big],
        out_shape=[jax.ShapeDtypeStruct((rows, width), jnp.float32)] * 2,
        scratch_shapes=[pltpu.VMEM((lanes * rows, LANE), jnp.float32)] * 4
        + [pltpu.VMEM((lanes * modes, LANE), jnp.float32)]
        + [pltpu.VMEM((modes, lanes, LANE), jnp.float32)] * 2,
        input_output_aliases=aliases,
    )(*operands)


def corrected(query_proj, key_proj, value_proj, out_grad, local, factor, weight, state_in, adjoint_in):
    rows, width = query_proj.shape
    modes = factor.shape[0]
    lanes = BLOCK // LANE
    big = pl.BlockSpec((rows, BLOCK), lambda i: (0, i))
    small = pl.BlockSpec((modes, BLOCK), lambda i: (0, i))
    out_big = jax.ShapeDtypeStruct((rows, width), jnp.bfloat16)
    return pl.pallas_call(
        correct_kernel,
        grid=(width // BLOCK,),
        in_specs=[big] * 6 + [small] * 4,
        out_specs=[big, big, big, big],
        out_shape=[out_big] * 4,
        scratch_shapes=[pltpu.VMEM((lanes * rows, LANE), jnp.float32)] * 2
        + [pltpu.VMEM((lanes * modes, LANE), jnp.float32)]
        + [pltpu.VMEM((modes, lanes, LANE), jnp.float32)] * 4,
    )(query_proj, key_proj, value_proj, out_grad, *local, factor, weight, state_in, adjoint_in)


def split_dot(a, member):
    bf16 = jnp.bfloat16
    top = lax.reduce_precision(a, exponent_bits=8, mantissa_bits=7)
    rest = a - top
    middle = lax.reduce_precision(rest, exponent_bits=8, mantissa_bits=7)
    hi = top.astype(bf16)
    mid = middle.astype(bf16)
    lo = (rest - middle).astype(bf16)
    rows = a.shape[0]
    out = jnp.dot(jnp.concatenate([hi, mid, lo], axis=0), member, preferred_element_type=jnp.float32)
    return (out[:rows] + out[rows : 2 * rows]) + out[2 * rows :]


def make_on_device(count):
    def on_device(query_proj, key_proj, value_proj, out_grad, decay_rate, residue, group_of):
        rows = query_proj.shape[0]
        group_count = decay_rate.shape[0]
        member = (group_of[None, :] == jnp.arange(group_count, dtype=jnp.int32)[:, None]).astype(
            jnp.bfloat16
        )
        modes = decay_rate.shape[1]
        params = split_dot(jnp.concatenate([decay_rate.T, residue.T], axis=0), member)
        rate = params[:modes]
        weight = params[modes:]
        factor = jnp.exp(-rate)
        end_state, head_adjoint, local_total = local_carries(
            query_proj, key_proj, value_proj, out_grad, factor
        )
        width = query_proj.shape[1]
        modes = factor.shape[0]
        pieces = width // BLOCK
        local = None
        made = 0

        def span(blocks):
            return jnp.exp(-rate * (blocks * float(rows)))

        member_t = member.T

        def grouped(a):
            return split_dot(a, member_t)

        place = lax.axis_index("ctx")
        fwd_cube = end_state
        bwd_cube = head_adjoint
        grad_cube = grouped(local_total)
        state_in = jnp.zeros_like(end_state)
        adjoint_in = jnp.zeros_like(head_adjoint)
        bit = 1
        level = 0
        while bit < count:
            pairs = [(i, i ^ bit) for i in range(count)]
            packed = jnp.concatenate([fwd_cube, bwd_cube, grad_cube], axis=1)
            need = pieces if bit * 2 >= count else min(pieces, level)
            level += 1
            if bit == 1:
                got = lax.ppermute(packed, "ctx", pairs)
            else:
                half = packed.shape[1] // 2
                core = place % 2
                mine = lax.dynamic_slice_in_dim(packed, core * half, half, axis=1)
                got_mine = lax.ppermute(mine, "ctx", pairs)
                if need > made:
                    while made < need:
                        local = local_scans(
                            query_proj, key_proj, value_proj, out_grad, factor, weight, made,
                            local,
                        )
                        made += 1
                    got_mine, local = lax.optimization_barrier((got_mine, local))
                got_other = lax.ppermute(got_mine, "ctx", [(i, i ^ 1) for i in range(count)])
                first = jnp.where(core == 0, got_mine, got_other)
                second = jnp.where(core == 0, got_other, got_mine)
                got = jnp.concatenate([first, second], axis=1)
            got_fwd = got[:, :width]
            got_bwd = got[:, width : 2 * width]
            got_grad = got[:, 2 * width :]
            upper = (place & bit) != 0
            offset = (place % bit).astype(jnp.float32)
            low_fwd = jnp.where(upper, got_fwd, fwd_cube)
            high_fwd = jnp.where(upper, fwd_cube, got_fwd)
            low_bwd = jnp.where(upper, got_bwd, bwd_cube)
            high_bwd = jnp.where(upper, bwd_cube, got_bwd)
            low_grad = jnp.where(upper, got_grad, grad_cube)
            high_grad = jnp.where(upper, grad_cube, got_grad)
            state_in = state_in + jnp.where(upper, span(offset) * got_fwd, 0.0)
            adjoint_in = adjoint_in + jnp.where(upper, 0.0, span(bit - 1 - offset) * got_bwd)
            whole = span(bit)
            grad_cube = (low_grad + high_grad) + grouped((factor * low_fwd) * high_bwd)
            fwd_cube = high_fwd + whole * low_fwd
            bwd_cube = low_bwd + whole * high_bwd
            bit *= 2

        while made < pieces:
            local = local_scans(
                query_proj, key_proj, value_proj, out_grad, factor, weight, made, local
            )
            made += 1
        hyena_out, query_grad, key_grad, value_grad = corrected(
            query_proj, key_proj, value_proj, out_grad, local, factor, weight, state_in, adjoint_in
        )
        filter_grad = grad_cube.T
        filter_update = filter_grad / jnp.sqrt(jnp.mean(filter_grad * filter_grad) + 1e-06)
        return (hyena_out, query_grad, key_grad, value_grad, filter_update)

    return on_device


def solution(mesh):
    placed = (
        P(("groups", "ctx"), None),
        P(("groups", "ctx"), None),
        P(("groups", "ctx"), None),
        P(("groups", "ctx"), None),
        P(),
        P(),
        P(),
    )
    return jax.shard_map(
        make_on_device(mesh.shape["ctx"]),
        mesh=mesh,
        in_specs=placed,
        out_specs=(
            P(("groups", "ctx"), None),
            P(("groups", "ctx"), None),
            P(("groups", "ctx"), None),
            P(("groups", "ctx"), None),
            P("groups", None),
        ),
        check_vma=False,
    )
```

```python
import jax
import jax.numpy as jnp
from jax import lax
from jax.experimental import pallas as pl
from jax.experimental.pallas import tpu as pltpu
from jax.sharding import PartitionSpec as P

BLOCK = 1024
SUB = 256
ROWS = 8
LANE = 128


def carry_kernel(q_ref, k_ref, v_ref, g_ref, p_ref, xend_ref, head_ref, tot_ref, mix_ref, up_ref):
    f32 = jnp.float32
    mix_ref[...] = (k_ref[...].astype(f32) * v_ref[...].astype(f32)).astype(jnp.bfloat16).astype(f32)
    up_ref[...] = g_ref[...].astype(f32) * q_ref[...].astype(f32)
    rows, width = mix_ref.shape
    chunks = rows // ROWS
    for h in range(width // SUB):
        cols = pl.ds(h * SUB, SUB)
        p = p_ref[:, cols]

        def body(c, carry):
            x, tot, a = carry
            fb = pl.multiple_of(c * ROWS, ROWS)
            bb = pl.multiple_of((chunks - 1 - c) * ROWS, ROWS)
            mt = mix_ref[pl.ds(fb, ROWS), cols]
            ut = up_ref[pl.ds(fb, ROWS), cols]
            ub = up_ref[pl.ds(bb, ROWS), cols]
            for j in range(ROWS):
                x = p * x + mt[j : j + 1, :]
                tot = tot + ut[j : j + 1, :] * x
                jb = ROWS - 1 - j
                a = p * a + ub[jb : jb + 1, :]
            return x, tot, a

        zero = jnp.zeros(p.shape, f32)
        x, tot, a = lax.fori_loop(0, chunks, body, (zero, zero, zero))
        xend_ref[:, cols] = x
        head_ref[:, cols] = a
        tot_ref[:, cols] = tot


def to_modes(src_ref, stage_ref, dst_ref):
    modes, width = src_ref.shape
    lanes = width // LANE
    for c in range(lanes):
        stage_ref[c * modes : (c + 1) * modes, :] = src_ref[:, c * LANE : (c + 1) * LANE]
    for m in range(modes):
        dst_ref[m] = stage_ref[pl.ds(m, lanes, stride=modes), :]


def local_kernel(q_ref, k_ref, v_ref, g_ref, pw_ref, rw_ref, *refs):
    f32 = jnp.float32
    if len(refs) == 11:
        refs = refs[2:]
    filt_out, mg_out, mix_ref, up_ref, filt_ref, mg_ref, stage_ref, p_ref, r_ref = refs
    to_modes(pw_ref, stage_ref, p_ref)
    to_modes(rw_ref, stage_ref, r_ref)
    rows, width = q_ref.shape
    lanes = width // LANE
    for c in range(lanes):
        cols = slice(c * LANE, (c + 1) * LANE)
        band = slice(c * rows, (c + 1) * rows)
        kf = k_ref[:, cols].astype(f32)
        vf = v_ref[:, cols].astype(f32)
        mix_ref[band, :] = (kf * vf).astype(jnp.bfloat16).astype(f32)
        up_ref[band, :] = g_ref[:, cols].astype(f32) * q_ref[:, cols].astype(f32)

    def body(t, carry):
        x, a = carry
        p = p_ref[...]
        r = r_ref[...]
        x = p * x + mix_ref[pl.ds(t, lanes, stride=rows), :][None]
        filt_ref[pl.ds(t, lanes, stride=rows), :] = jnp.sum(r * x, axis=0)
        tb = rows - 1 - t
        a = p * a + up_ref[pl.ds(tb, lanes, stride=rows), :][None]
        mg_ref[pl.ds(tb, lanes, stride=rows), :] = jnp.sum(r * a, axis=0)
        return x, a

    zero = jnp.zeros(p_ref.shape, f32)
    lax.fori_loop(0, rows, body, (zero, zero), unroll=4)
    for c in range(lanes):
        cols = slice(c * LANE, (c + 1) * LANE)
        band = slice(c * rows, (c + 1) * rows)
        filt_out[:, cols] = filt_ref[band, :]
        mg_out[:, cols] = mg_ref[band, :]


def correct_kernel(
    q_ref, k_ref, v_ref, g_ref, fl_ref, ml_ref, pw_ref, rw_ref, sw_ref, bw_ref,
    ho_ref, qg_ref, kg_ref, vg_ref,
    filt_ref, mg_ref, stage_ref, p_ref, r_ref, s_ref, b_ref,
):
    f32 = jnp.float32
    for src, dst in ((pw_ref, p_ref), (rw_ref, r_ref), (sw_ref, s_ref), (bw_ref, b_ref)):
        to_modes(src, stage_ref, dst)
    rows, width = q_ref.shape
    lanes = width // LANE

    def body(t, carry):
        z, w = carry
        p = p_ref[...]
        filt_ref[pl.ds(t, lanes, stride=rows), :] = jnp.sum(z, axis=0)
        tb = rows - 1 - t
        mg_ref[pl.ds(tb, lanes, stride=rows), :] = jnp.sum(w, axis=0)
        return z * p, w * p

    p = p_ref[...]
    r = r_ref[...]
    lax.fori_loop(0, rows, body, ((r * p) * s_ref[...], (r * p) * b_ref[...]), unroll=4)
    for c in range(lanes):
        cols = slice(c * LANE, (c + 1) * LANE)
        band = slice(c * rows, (c + 1) * rows)
        filt = fl_ref[:, cols] + filt_ref[band, :]
        mg = ml_ref[:, cols] + mg_ref[band, :]
        ho_ref[:, cols] = (q_ref[:, cols].astype(f32) * filt).astype(jnp.bfloat16)
        qg_ref[:, cols] = (g_ref[:, cols].astype(f32) * filt).astype(jnp.bfloat16)
        kg_ref[:, cols] = (mg * v_ref[:, cols].astype(f32)).astype(jnp.bfloat16)
        vg_ref[:, cols] = (mg * k_ref[:, cols].astype(f32)).astype(jnp.bfloat16)


def local_carries(query_proj, key_proj, value_proj, out_grad, factor):
    rows, width = query_proj.shape
    modes = factor.shape[0]
    big = pl.BlockSpec((rows, BLOCK), lambda i: (0, i))
    small = pl.BlockSpec((modes, BLOCK), lambda i: (0, i))
    return pl.pallas_call(
        carry_kernel,
        grid=(width // BLOCK,),
        in_specs=[big, big, big, big, small],
        out_specs=[small, small, small],
        out_shape=[jax.ShapeDtypeStruct((modes, width), jnp.float32)] * 3,
        scratch_shapes=[pltpu.VMEM((rows, BLOCK), jnp.float32)] * 2,
    )(query_proj, key_proj, value_proj, out_grad, factor)


def local_scans(query_proj, key_proj, value_proj, out_grad, factor, weight, first, previous):
    rows, width = query_proj.shape
    modes = factor.shape[0]
    lanes = BLOCK // LANE
    big = pl.BlockSpec((rows, BLOCK), lambda i: (0, i + first))
    small = pl.BlockSpec((modes, BLOCK), lambda i: (0, i + first))
    operands = [query_proj, key_proj, value_proj, out_grad, factor, weight]
    specs = [big, big, big, big, small, small]
    aliases = {}
    if previous is not None:
        operands += list(previous)
        specs += [pl.BlockSpec(memory_space=pl.ANY)] * 2
        aliases = {6: 0, 7: 1}
    return pl.pallas_call(
        local_kernel,
        grid=(1,),
        in_specs=specs,
        out_specs=[big, big],
        out_shape=[jax.ShapeDtypeStruct((rows, width), jnp.float32)] * 2,
        scratch_shapes=[pltpu.VMEM((lanes * rows, LANE), jnp.float32)] * 4
        + [pltpu.VMEM((lanes * modes, LANE), jnp.float32)]
        + [pltpu.VMEM((modes, lanes, LANE), jnp.float32)] * 2,
        input_output_aliases=aliases,
    )(*operands)


def corrected(query_proj, key_proj, value_proj, out_grad, local, factor, weight, state_in, adjoint_in):
    rows, width = query_proj.shape
    modes = factor.shape[0]
    lanes = BLOCK // LANE
    big = pl.BlockSpec((rows, BLOCK), lambda i: (0, i))
    small = pl.BlockSpec((modes, BLOCK), lambda i: (0, i))
    out_big = jax.ShapeDtypeStruct((rows, width), jnp.bfloat16)
    return pl.pallas_call(
        correct_kernel,
        grid=(width // BLOCK,),
        in_specs=[big] * 6 + [small] * 4,
        out_specs=[big, big, big, big],
        out_shape=[out_big] * 4,
        scratch_shapes=[pltpu.VMEM((lanes * rows, LANE), jnp.float32)] * 2
        + [pltpu.VMEM((lanes * modes, LANE), jnp.float32)]
        + [pltpu.VMEM((modes, lanes, LANE), jnp.float32)] * 4,
    )(query_proj, key_proj, value_proj, out_grad, *local, factor, weight, state_in, adjoint_in)


def split_dot(a, member):
    bf16 = jnp.bfloat16
    top = lax.reduce_precision(a, exponent_bits=8, mantissa_bits=7)
    rest = a - top
    middle = lax.reduce_precision(rest, exponent_bits=8, mantissa_bits=7)
    hi = top.astype(bf16)
    mid = middle.astype(bf16)
    lo = (rest - middle).astype(bf16)
    rows = a.shape[0]
    out = jnp.dot(jnp.concatenate([hi, mid, lo], axis=0), member, preferred_element_type=jnp.float32)
    return (out[:rows] + out[rows : 2 * rows]) + out[2 * rows :]


def make_on_device(count):
    def on_device(query_proj, key_proj, value_proj, out_grad, decay_rate, residue, group_of):
        rows = query_proj.shape[0]
        group_count = decay_rate.shape[0]
        member = (group_of[None, :] == jnp.arange(group_count, dtype=jnp.int32)[:, None]).astype(
            jnp.bfloat16
        )
        modes = decay_rate.shape[1]
        params = split_dot(jnp.concatenate([decay_rate.T, residue.T], axis=0), member)
        rate = params[:modes]
        weight = params[modes:]
        factor = jnp.exp(-rate)
        end_state, head_adjoint, local_total = local_carries(
            query_proj, key_proj, value_proj, out_grad, factor
        )
        width = query_proj.shape[1]
        modes = factor.shape[0]
        pieces = width // BLOCK
        local = None
        made = 0

        def span(blocks):
            return jnp.exp(-rate * (blocks * float(rows)))

        member_t = member.T

        def grouped(a):
            return split_dot(a, member_t)

        place = lax.axis_index("ctx")
        fwd_cube = end_state
        bwd_cube = head_adjoint
        grad_cube = grouped(local_total)
        state_in = jnp.zeros_like(end_state)
        adjoint_in = jnp.zeros_like(head_adjoint)
        bit = 1
        level = 0
        while bit < count:
            pairs = [(i, i ^ bit) for i in range(count)]
            packed = jnp.concatenate([fwd_cube, bwd_cube, grad_cube], axis=1)
            need = pieces if bit * 2 >= count else min(pieces, level)
            level += 1
            if bit == 1:
                got = lax.ppermute(packed, "ctx", pairs)
            else:
                half = packed.shape[1] // 2
                core = place % 2
                mine = lax.dynamic_slice_in_dim(packed, core * half, half, axis=1)
                got_mine = lax.ppermute(mine, "ctx", pairs)
                if need > made:
                    while made < need:
                        local = local_scans(
                            query_proj, key_proj, value_proj, out_grad, factor, weight, made,
                            local,
                        )
                        made += 1
                    got_mine, local = lax.optimization_barrier((got_mine, local))
                got_other = lax.ppermute(got_mine, "ctx", [(i, i ^ 1) for i in range(count)])
                first = jnp.where(core == 0, got_mine, got_other)
                second = jnp.where(core == 0, got_other, got_mine)
                got = jnp.concatenate([first, second], axis=1)
            got_fwd = got[:, :width]
            got_bwd = got[:, width : 2 * width]
            got_grad = got[:, 2 * width :]
            upper = (place & bit) != 0
            offset = (place % bit).astype(jnp.float32)
            low_fwd = jnp.where(upper, got_fwd, fwd_cube)
            high_fwd = jnp.where(upper, fwd_cube, got_fwd)
            low_bwd = jnp.where(upper, got_bwd, bwd_cube)
            high_bwd = jnp.where(upper, bwd_cube, got_bwd)
            low_grad = jnp.where(upper, got_grad, grad_cube)
            high_grad = jnp.where(upper, grad_cube, got_grad)
            state_in = state_in + jnp.where(upper, span(offset) * got_fwd, 0.0)
            adjoint_in = adjoint_in + jnp.where(upper, 0.0, span(bit - 1 - offset) * got_bwd)
            whole = span(bit)
            grad_cube = (low_grad + high_grad) + grouped((factor * low_fwd) * high_bwd)
            fwd_cube = high_fwd + whole * low_fwd
            bwd_cube = low_bwd + whole * high_bwd
            bit *= 2

        while made < pieces:
            local = local_scans(
                query_proj, key_proj, value_proj, out_grad, factor, weight, made, local
            )
            made += 1
        hyena_out, query_grad, key_grad, value_grad = corrected(
            query_proj, key_proj, value_proj, out_grad, local, factor, weight, state_in, adjoint_in
        )
        filter_grad = grad_cube.T
        filter_update = filter_grad / jnp.sqrt(jnp.mean(filter_grad * filter_grad) + 1e-06)
        return (hyena_out, query_grad, key_grad, value_grad, filter_update)

    return on_device


def solution(mesh):
    placed = (
        P(("groups", "ctx"), None),
        P(("groups", "ctx"), None),
        P(("groups", "ctx"), None),
        P(("groups", "ctx"), None),
        P(),
        P(),
        P(),
    )
    return jax.shard_map(
        make_on_device(mesh.shape["ctx"]),
        mesh=mesh,
        in_specs=placed,
        out_specs=(
            P(("groups", "ctx"), None),
            P(("groups", "ctx"), None),
            P(("groups", "ctx"), None),
            P(("groups", "ctx"), None),
            P("groups", None),
        ),
        check_vma=False,
    )
```

```python
import jax
import jax.numpy as jnp
from jax import lax
from jax.experimental import pallas as pl
from jax.experimental.pallas import tpu as pltpu
from jax.sharding import PartitionSpec as P

BLOCK = 1024
SUB = 256
ROWS = 8
LANE = 128


def carry_kernel(q_ref, k_ref, v_ref, g_ref, rate_ref, xend_ref, head_ref, tot_ref, p_ref, mix_ref, up_ref):
    f32 = jnp.float32
    p_ref[...] = jnp.exp(-rate_ref[...])
    mix_ref[...] = (k_ref[...].astype(f32) * v_ref[...].astype(f32)).astype(jnp.bfloat16).astype(f32)
    up_ref[...] = g_ref[...].astype(f32) * q_ref[...].astype(f32)
    rows, width = mix_ref.shape
    chunks = rows // ROWS
    for h in range(width // SUB):
        cols = pl.ds(h * SUB, SUB)
        p = p_ref[:, cols]

        def body(c, carry):
            x, tot, a = carry
            fb = pl.multiple_of(c * ROWS, ROWS)
            bb = pl.multiple_of((chunks - 1 - c) * ROWS, ROWS)
            mt = mix_ref[pl.ds(fb, ROWS), cols]
            ut = up_ref[pl.ds(fb, ROWS), cols]
            ub = up_ref[pl.ds(bb, ROWS), cols]
            for j in range(ROWS):
                x = p * x + mt[j : j + 1, :]
                tot = tot + ut[j : j + 1, :] * x
                jb = ROWS - 1 - j
                a = p * a + ub[jb : jb + 1, :]
            return x, tot, a

        zero = jnp.zeros(p.shape, f32)
        x, tot, a = lax.fori_loop(0, chunks, body, (zero, zero, zero))
        xend_ref[:, cols] = x
        head_ref[:, cols] = a
        tot_ref[:, cols] = tot


def to_modes(src_ref, stage_ref, dst_ref):
    modes, width = src_ref.shape
    lanes = width // LANE
    for c in range(lanes):
        stage_ref[c * modes : (c + 1) * modes, :] = src_ref[:, c * LANE : (c + 1) * LANE]
    for m in range(modes):
        dst_ref[m] = stage_ref[pl.ds(m, lanes, stride=modes), :]


def local_kernel(q_ref, k_ref, v_ref, g_ref, pw_ref, rw_ref, *refs):
    f32 = jnp.float32
    if len(refs) == 11:
        refs = refs[2:]
    filt_out, mg_out, mix_ref, up_ref, filt_ref, mg_ref, stage_ref, p_ref, r_ref = refs
    to_modes(pw_ref, stage_ref, p_ref)
    to_modes(rw_ref, stage_ref, r_ref)
    rows, width = q_ref.shape
    lanes = width // LANE
    for c in range(lanes):
        cols = slice(c * LANE, (c + 1) * LANE)
        band = slice(c * rows, (c + 1) * rows)
        kf = k_ref[:, cols].astype(f32)
        vf = v_ref[:, cols].astype(f32)
        mix_ref[band, :] = (kf * vf).astype(jnp.bfloat16).astype(f32)
        up_ref[band, :] = g_ref[:, cols].astype(f32) * q_ref[:, cols].astype(f32)

    def body(t, carry):
        x, a = carry
        p = p_ref[...]
        r = r_ref[...]
        x = p * x + mix_ref[pl.ds(t, lanes, stride=rows), :][None]
        filt_ref[pl.ds(t, lanes, stride=rows), :] = jnp.sum(r * x, axis=0)
        tb = rows - 1 - t
        a = p * a + up_ref[pl.ds(tb, lanes, stride=rows), :][None]
        mg_ref[pl.ds(tb, lanes, stride=rows), :] = jnp.sum(r * a, axis=0)
        return x, a

    zero = jnp.zeros(p_ref.shape, f32)
    lax.fori_loop(0, rows, body, (zero, zero), unroll=4)
    for c in range(lanes):
        cols = slice(c * LANE, (c + 1) * LANE)
        band = slice(c * rows, (c + 1) * rows)
        filt_out[:, cols] = filt_ref[band, :]
        mg_out[:, cols] = mg_ref[band, :]


def correct_kernel(
    q_ref, k_ref, v_ref, g_ref, fl_ref, ml_ref, pw_ref, rw_ref, sw_ref, bw_ref,
    ho_ref, qg_ref, kg_ref, vg_ref,
    filt_ref, mg_ref, stage_ref, p_ref, r_ref, s_ref, b_ref,
):
    f32 = jnp.float32
    for src, dst in ((pw_ref, p_ref), (rw_ref, r_ref), (sw_ref, s_ref), (bw_ref, b_ref)):
        to_modes(src, stage_ref, dst)
    rows, width = q_ref.shape
    lanes = width // LANE

    def body(t, carry):
        z, w = carry
        p = p_ref[...]
        filt_ref[pl.ds(t, lanes, stride=rows), :] = jnp.sum(z, axis=0)
        tb = rows - 1 - t
        mg_ref[pl.ds(tb, lanes, stride=rows), :] = jnp.sum(w, axis=0)
        return z * p, w * p

    p = p_ref[...]
    r = r_ref[...]
    lax.fori_loop(0, rows, body, ((r * p) * s_ref[...], (r * p) * b_ref[...]), unroll=4)
    for c in range(lanes):
        cols = slice(c * LANE, (c + 1) * LANE)
        band = slice(c * rows, (c + 1) * rows)
        filt = fl_ref[:, cols] + filt_ref[band, :]
        mg = ml_ref[:, cols] + mg_ref[band, :]
        ho_ref[:, cols] = (q_ref[:, cols].astype(f32) * filt).astype(jnp.bfloat16)
        qg_ref[:, cols] = (g_ref[:, cols].astype(f32) * filt).astype(jnp.bfloat16)
        kg_ref[:, cols] = (mg * v_ref[:, cols].astype(f32)).astype(jnp.bfloat16)
        vg_ref[:, cols] = (mg * k_ref[:, cols].astype(f32)).astype(jnp.bfloat16)


def local_carries(query_proj, key_proj, value_proj, out_grad, rate):
    rows, width = query_proj.shape
    modes = rate.shape[0]
    big = pl.BlockSpec((rows, BLOCK), lambda i: (0, i))
    small = pl.BlockSpec((modes, BLOCK), lambda i: (0, i))
    return pl.pallas_call(
        carry_kernel,
        grid=(width // BLOCK,),
        in_specs=[big, big, big, big, small],
        out_specs=[small, small, small, small],
        out_shape=[jax.ShapeDtypeStruct((modes, width), jnp.float32)] * 4,
        scratch_shapes=[pltpu.VMEM((rows, BLOCK), jnp.float32)] * 2,
    )(query_proj, key_proj, value_proj, out_grad, rate)


def local_scans(query_proj, key_proj, value_proj, out_grad, factor, weight, first, previous):
    rows, width = query_proj.shape
    modes = factor.shape[0]
    lanes = BLOCK // LANE
    big = pl.BlockSpec((rows, BLOCK), lambda i: (0, i + first))
    small = pl.BlockSpec((modes, BLOCK), lambda i: (0, i + first))
    operands = [query_proj, key_proj, value_proj, out_grad, factor, weight]
    specs = [big, big, big, big, small, small]
    aliases = {}
    if previous is not None:
        operands += list(previous)
        specs += [pl.BlockSpec(memory_space=pl.ANY)] * 2
        aliases = {6: 0, 7: 1}
    return pl.pallas_call(
        local_kernel,
        grid=(1,),
        in_specs=specs,
        out_specs=[big, big],
        out_shape=[jax.ShapeDtypeStruct((rows, width), jnp.float32)] * 2,
        scratch_shapes=[pltpu.VMEM((lanes * rows, LANE), jnp.float32)] * 4
        + [pltpu.VMEM((lanes * modes, LANE), jnp.float32)]
        + [pltpu.VMEM((modes, lanes, LANE), jnp.float32)] * 2,
        input_output_aliases=aliases,
    )(*operands)


def corrected(query_proj, key_proj, value_proj, out_grad, local, factor, weight, state_in, adjoint_in):
    rows, width = query_proj.shape
    modes = factor.shape[0]
    lanes = BLOCK // LANE
    big = pl.BlockSpec((rows, BLOCK), lambda i: (0, i))
    small = pl.BlockSpec((modes, BLOCK), lambda i: (0, i))
    out_big = jax.ShapeDtypeStruct((rows, width), jnp.bfloat16)
    return pl.pallas_call(
        correct_kernel,
        grid=(width // BLOCK,),
        in_specs=[big] * 6 + [small] * 4,
        out_specs=[big, big, big, big],
        out_shape=[out_big] * 4,
        scratch_shapes=[pltpu.VMEM((lanes * rows, LANE), jnp.float32)] * 2
        + [pltpu.VMEM((lanes * modes, LANE), jnp.float32)]
        + [pltpu.VMEM((modes, lanes, LANE), jnp.float32)] * 4,
    )(query_proj, key_proj, value_proj, out_grad, *local, factor, weight, state_in, adjoint_in)


def split_dot(a, member):
    bf16 = jnp.bfloat16
    top = lax.reduce_precision(a, exponent_bits=8, mantissa_bits=7)
    rest = a - top
    middle = lax.reduce_precision(rest, exponent_bits=8, mantissa_bits=7)
    hi = top.astype(bf16)
    mid = middle.astype(bf16)
    lo = (rest - middle).astype(bf16)
    rows = a.shape[0]
    out = jnp.dot(jnp.concatenate([hi, mid, lo], axis=0), member, preferred_element_type=jnp.float32)
    return (out[:rows] + out[rows : 2 * rows]) + out[2 * rows :]


def make_on_device(count):
    def on_device(query_proj, key_proj, value_proj, out_grad, decay_rate, residue, group_of):
        rows = query_proj.shape[0]
        group_count = decay_rate.shape[0]
        member = (group_of[None, :] == jnp.arange(group_count, dtype=jnp.int32)[:, None]).astype(
            jnp.bfloat16
        )
        rate = split_dot(decay_rate.T, member)
        weight = split_dot(residue.T, member)
        end_state, head_adjoint, local_total, factor = local_carries(
            query_proj, key_proj, value_proj, out_grad, rate
        )
        width = query_proj.shape[1]
        modes = factor.shape[0]
        pieces = width // BLOCK
        local = None
        made = 0

        def span(blocks):
            return jnp.exp(-rate * (blocks * float(rows)))

        member_t = member.T

        def grouped(a):
            return split_dot(a, member_t)

        place = lax.axis_index("ctx")
        fwd_cube = end_state
        bwd_cube = head_adjoint
        grad_cube = grouped(local_total)
        state_in = jnp.zeros_like(end_state)
        adjoint_in = jnp.zeros_like(head_adjoint)
        bit = 1
        level = 0
        while bit < count:
            pairs = [(i, i ^ bit) for i in range(count)]
            packed = jnp.concatenate([fwd_cube, bwd_cube, grad_cube], axis=1)
            need = pieces if bit * 2 >= count else min(pieces, level)
            level += 1
            if bit == 1:
                got = lax.ppermute(packed, "ctx", pairs)
            else:
                half = packed.shape[1] // 2
                core = place % 2
                mine = lax.dynamic_slice_in_dim(packed, core * half, half, axis=1)
                got_mine = lax.ppermute(mine, "ctx", pairs)
                if need > made:
                    while made < need:
                        local = local_scans(
                            query_proj, key_proj, value_proj, out_grad, factor, weight, made,
                            local,
                        )
                        made += 1
                    got_mine, local = lax.optimization_barrier((got_mine, local))
                got_other = lax.ppermute(got_mine, "ctx", [(i, i ^ 1) for i in range(count)])
                first = jnp.where(core == 0, got_mine, got_other)
                second = jnp.where(core == 0, got_other, got_mine)
                got = jnp.concatenate([first, second], axis=1)
            got_fwd = got[:, :width]
            got_bwd = got[:, width : 2 * width]
            got_grad = got[:, 2 * width :]
            upper = (place & bit) != 0
            offset = (place % bit).astype(jnp.float32)
            low_fwd = jnp.where(upper, got_fwd, fwd_cube)
            high_fwd = jnp.where(upper, fwd_cube, got_fwd)
            low_bwd = jnp.where(upper, got_bwd, bwd_cube)
            high_bwd = jnp.where(upper, bwd_cube, got_bwd)
            low_grad = jnp.where(upper, got_grad, grad_cube)
            high_grad = jnp.where(upper, grad_cube, got_grad)
            state_in = state_in + jnp.where(upper, span(offset) * got_fwd, 0.0)
            adjoint_in = adjoint_in + jnp.where(upper, 0.0, span(bit - 1 - offset) * got_bwd)
            whole = span(bit)
            grad_cube = (low_grad + high_grad) + grouped((factor * low_fwd) * high_bwd)
            fwd_cube = high_fwd + whole * low_fwd
            bwd_cube = low_bwd + whole * high_bwd
            bit *= 2

        while made < pieces:
            local = local_scans(
                query_proj, key_proj, value_proj, out_grad, factor, weight, made, local
            )
            made += 1
        hyena_out, query_grad, key_grad, value_grad = corrected(
            query_proj, key_proj, value_proj, out_grad, local, factor, weight, state_in, adjoint_in
        )
        filter_grad = grad_cube.T
        filter_update = filter_grad / jnp.sqrt(jnp.mean(filter_grad * filter_grad) + 1e-06)
        return (hyena_out, query_grad, key_grad, value_grad, filter_update)

    return on_device


def solution(mesh):
    placed = (
        P(("groups", "ctx"), None),
        P(("groups", "ctx"), None),
        P(("groups", "ctx"), None),
        P(("groups", "ctx"), None),
        P(),
        P(),
        P(),
    )
    return jax.shard_map(
        make_on_device(mesh.shape["ctx"]),
        mesh=mesh,
        in_specs=placed,
        out_specs=(
            P(("groups", "ctx"), None),
            P(("groups", "ctx"), None),
            P(("groups", "ctx"), None),
            P(("groups", "ctx"), None),
            P("groups", None),
        ),
        check_vma=False,
    )
```

```python
import jax
import jax.numpy as jnp
from jax import lax
from jax.experimental import pallas as pl
from jax.experimental.pallas import tpu as pltpu
from jax.sharding import PartitionSpec as P

BLOCK = 1024
SUB = 256
ROWS = 8
LANE = 128


def carry_kernel(q_ref, k_ref, v_ref, g_ref, p_ref, xend_ref, head_ref, tot_ref, mix_ref, up_ref):
    f32 = jnp.float32
    mix_ref[...] = (k_ref[...].astype(f32) * v_ref[...].astype(f32)).astype(jnp.bfloat16).astype(f32)
    up_ref[...] = g_ref[...].astype(f32) * q_ref[...].astype(f32)
    rows, width = mix_ref.shape
    chunks = rows // ROWS
    for h in range(width // SUB):
        cols = pl.ds(h * SUB, SUB)
        p = p_ref[:, cols]

        def body(c, carry):
            x, tot, a = carry
            fb = pl.multiple_of(c * ROWS, ROWS)
            bb = pl.multiple_of((chunks - 1 - c) * ROWS, ROWS)
            mt = mix_ref[pl.ds(fb, ROWS), cols]
            ut = up_ref[pl.ds(fb, ROWS), cols]
            ub = up_ref[pl.ds(bb, ROWS), cols]
            for j in range(ROWS):
                x = p * x + mt[j : j + 1, :]
                tot = tot + ut[j : j + 1, :] * x
                jb = ROWS - 1 - j
                a = p * a + ub[jb : jb + 1, :]
            return x, tot, a

        zero = jnp.zeros(p.shape, f32)
        x, tot, a = lax.fori_loop(0, chunks, body, (zero, zero, zero))
        xend_ref[:, cols] = x
        head_ref[:, cols] = a
        tot_ref[:, cols] = tot


def to_modes(src_ref, stage_ref, dst_ref):
    modes, width = src_ref.shape
    lanes = width // LANE
    for c in range(lanes):
        stage_ref[c * modes : (c + 1) * modes, :] = src_ref[:, c * LANE : (c + 1) * LANE]
    for m in range(modes):
        dst_ref[m] = stage_ref[pl.ds(m, lanes, stride=modes), :]


def local_kernel(q_ref, k_ref, v_ref, g_ref, pw_ref, rw_ref, *refs):
    f32 = jnp.float32
    if len(refs) == 11:
        refs = refs[2:]
    filt_out, mg_out, mix_ref, up_ref, filt_ref, mg_ref, stage_ref, p_ref, r_ref = refs
    to_modes(pw_ref, stage_ref, p_ref)
    to_modes(rw_ref, stage_ref, r_ref)
    rows, width = q_ref.shape
    lanes = width // LANE
    for c in range(lanes):
        cols = slice(c * LANE, (c + 1) * LANE)
        band = slice(c * rows, (c + 1) * rows)
        kf = k_ref[:, cols].astype(f32)
        vf = v_ref[:, cols].astype(f32)
        mix_ref[band, :] = (kf * vf).astype(jnp.bfloat16).astype(f32)
        up_ref[band, :] = g_ref[:, cols].astype(f32) * q_ref[:, cols].astype(f32)

    def body(t, carry):
        x, a = carry
        p = p_ref[...]
        r = r_ref[...]
        x = p * x + mix_ref[pl.ds(t, lanes, stride=rows), :][None]
        filt_ref[pl.ds(t, lanes, stride=rows), :] = jnp.sum(r * x, axis=0)
        tb = rows - 1 - t
        a = p * a + up_ref[pl.ds(tb, lanes, stride=rows), :][None]
        mg_ref[pl.ds(tb, lanes, stride=rows), :] = jnp.sum(r * a, axis=0)
        return x, a

    zero = jnp.zeros(p_ref.shape, f32)
    lax.fori_loop(0, rows, body, (zero, zero), unroll=4)
    for c in range(lanes):
        cols = slice(c * LANE, (c + 1) * LANE)
        band = slice(c * rows, (c + 1) * rows)
        filt_out[:, cols] = filt_ref[band, :]
        mg_out[:, cols] = mg_ref[band, :]


def correct_kernel(
    q_ref, k_ref, v_ref, g_ref, fl_ref, ml_ref, pw_ref, rw_ref, sw_ref, bw_ref,
    ho_ref, qg_ref, kg_ref, vg_ref,
    filt_ref, mg_ref, stage_ref, p_ref, r_ref, s_ref, b_ref,
):
    f32 = jnp.float32
    for src, dst in ((pw_ref, p_ref), (rw_ref, r_ref), (sw_ref, s_ref), (bw_ref, b_ref)):
        to_modes(src, stage_ref, dst)
    rows, width = q_ref.shape
    lanes = width // LANE

    def body(t, carry):
        z, w = carry
        p = p_ref[...]
        filt_ref[pl.ds(t, lanes, stride=rows), :] = jnp.sum(z, axis=0)
        tb = rows - 1 - t
        mg_ref[pl.ds(tb, lanes, stride=rows), :] = jnp.sum(w, axis=0)
        return z * p, w * p

    p = p_ref[...]
    r = r_ref[...]
    lax.fori_loop(0, rows, body, ((r * p) * s_ref[...], (r * p) * b_ref[...]), unroll=8)
    for c in range(lanes):
        cols = slice(c * LANE, (c + 1) * LANE)
        band = slice(c * rows, (c + 1) * rows)
        filt = fl_ref[:, cols] + filt_ref[band, :]
        mg = ml_ref[:, cols] + mg_ref[band, :]
        ho_ref[:, cols] = (q_ref[:, cols].astype(f32) * filt).astype(jnp.bfloat16)
        qg_ref[:, cols] = (g_ref[:, cols].astype(f32) * filt).astype(jnp.bfloat16)
        kg_ref[:, cols] = (mg * v_ref[:, cols].astype(f32)).astype(jnp.bfloat16)
        vg_ref[:, cols] = (mg * k_ref[:, cols].astype(f32)).astype(jnp.bfloat16)


def local_carries(query_proj, key_proj, value_proj, out_grad, factor):
    rows, width = query_proj.shape
    modes = factor.shape[0]
    big = pl.BlockSpec((rows, BLOCK), lambda i: (0, i))
    small = pl.BlockSpec((modes, BLOCK), lambda i: (0, i))
    return pl.pallas_call(
        carry_kernel,
        grid=(width // BLOCK,),
        in_specs=[big, big, big, big, small],
        out_specs=[small, small, small],
        out_shape=[jax.ShapeDtypeStruct((modes, width), jnp.float32)] * 3,
        scratch_shapes=[pltpu.VMEM((rows, BLOCK), jnp.float32)] * 2,
    )(query_proj, key_proj, value_proj, out_grad, factor)


def local_scans(query_proj, key_proj, value_proj, out_grad, factor, weight, first, previous):
    rows, width = query_proj.shape
    modes = factor.shape[0]
    lanes = BLOCK // LANE
    big = pl.BlockSpec((rows, BLOCK), lambda i: (0, i + first))
    small = pl.BlockSpec((modes, BLOCK), lambda i: (0, i + first))
    operands = [query_proj, key_proj, value_proj, out_grad, factor, weight]
    specs = [big, big, big, big, small, small]
    aliases = {}
    if previous is not None:
        operands += list(previous)
        specs += [pl.BlockSpec(memory_space=pl.ANY)] * 2
        aliases = {6: 0, 7: 1}
    return pl.pallas_call(
        local_kernel,
        grid=(1,),
        in_specs=specs,
        out_specs=[big, big],
        out_shape=[jax.ShapeDtypeStruct((rows, width), jnp.float32)] * 2,
        scratch_shapes=[pltpu.VMEM((lanes * rows, LANE), jnp.float32)] * 4
        + [pltpu.VMEM((lanes * modes, LANE), jnp.float32)]
        + [pltpu.VMEM((modes, lanes, LANE), jnp.float32)] * 2,
        input_output_aliases=aliases,
    )(*operands)


def corrected(query_proj, key_proj, value_proj, out_grad, local, factor, weight, state_in, adjoint_in):
    rows, width = query_proj.shape
    modes = factor.shape[0]
    lanes = BLOCK // LANE
    big = pl.BlockSpec((rows, BLOCK), lambda i: (0, i))
    small = pl.BlockSpec((modes, BLOCK), lambda i: (0, i))
    out_big = jax.ShapeDtypeStruct((rows, width), jnp.bfloat16)
    return pl.pallas_call(
        correct_kernel,
        grid=(width // BLOCK,),
        in_specs=[big] * 6 + [small] * 4,
        out_specs=[big, big, big, big],
        out_shape=[out_big] * 4,
        scratch_shapes=[pltpu.VMEM((lanes * rows, LANE), jnp.float32)] * 2
        + [pltpu.VMEM((lanes * modes, LANE), jnp.float32)]
        + [pltpu.VMEM((modes, lanes, LANE), jnp.float32)] * 4,
    )(query_proj, key_proj, value_proj, out_grad, *local, factor, weight, state_in, adjoint_in)


def split_dot(a, member):
    bf16 = jnp.bfloat16
    top = lax.reduce_precision(a, exponent_bits=8, mantissa_bits=7)
    rest = a - top
    middle = lax.reduce_precision(rest, exponent_bits=8, mantissa_bits=7)
    hi = top.astype(bf16)
    mid = middle.astype(bf16)
    lo = (rest - middle).astype(bf16)
    rows = a.shape[0]
    out = jnp.dot(jnp.concatenate([hi, mid, lo], axis=0), member, preferred_element_type=jnp.float32)
    return (out[:rows] + out[rows : 2 * rows]) + out[2 * rows :]


def make_on_device(count):
    def on_device(query_proj, key_proj, value_proj, out_grad, decay_rate, residue, group_of):
        rows = query_proj.shape[0]
        group_count = decay_rate.shape[0]
        member = (group_of[None, :] == jnp.arange(group_count, dtype=jnp.int32)[:, None]).astype(
            jnp.bfloat16
        )
        modes = decay_rate.shape[1]
        params = split_dot(jnp.concatenate([decay_rate.T, residue.T], axis=0), member)
        rate = params[:modes]
        weight = params[modes:]
        factor = jnp.exp(-rate)
        end_state, head_adjoint, local_total = local_carries(
            query_proj, key_proj, value_proj, out_grad, factor
        )
        width = query_proj.shape[1]
        modes = factor.shape[0]
        pieces = width // BLOCK
        local = None
        made = 0

        def span(blocks):
            return jnp.exp(-rate * (blocks * float(rows)))

        member_t = member.T

        def grouped(a):
            return split_dot(a, member_t)

        place = lax.axis_index("ctx")
        fwd_cube = end_state
        bwd_cube = head_adjoint
        grad_cube = grouped(local_total)
        state_in = jnp.zeros_like(end_state)
        adjoint_in = jnp.zeros_like(head_adjoint)
        bit = 1
        level = 0
        while bit < count:
            pairs = [(i, i ^ bit) for i in range(count)]
            packed = jnp.concatenate([fwd_cube, bwd_cube, grad_cube], axis=1)
            need = pieces if bit * 2 >= count else min(pieces, level)
            level += 1
            if bit == 1:
                got = lax.ppermute(packed, "ctx", pairs)
            else:
                half = packed.shape[1] // 2
                core = place % 2
                mine = lax.dynamic_slice_in_dim(packed, core * half, half, axis=1)
                got_mine = lax.ppermute(mine, "ctx", pairs)
                if need > made:
                    while made < need:
                        local = local_scans(
                            query_proj, key_proj, value_proj, out_grad, factor, weight, made,
                            local,
                        )
                        made += 1
                    got_mine, local = lax.optimization_barrier((got_mine, local))
                got_other = lax.ppermute(got_mine, "ctx", [(i, i ^ 1) for i in range(count)])
                first = jnp.where(core == 0, got_mine, got_other)
                second = jnp.where(core == 0, got_other, got_mine)
                got = jnp.concatenate([first, second], axis=1)
            got_fwd = got[:, :width]
            got_bwd = got[:, width : 2 * width]
            got_grad = got[:, 2 * width :]
            upper = (place & bit) != 0
            offset = (place % bit).astype(jnp.float32)
            low_fwd = jnp.where(upper, got_fwd, fwd_cube)
            high_fwd = jnp.where(upper, fwd_cube, got_fwd)
            low_bwd = jnp.where(upper, got_bwd, bwd_cube)
            high_bwd = jnp.where(upper, bwd_cube, got_bwd)
            low_grad = jnp.where(upper, got_grad, grad_cube)
            high_grad = jnp.where(upper, grad_cube, got_grad)
            state_in = state_in + jnp.where(upper, span(offset) * got_fwd, 0.0)
            adjoint_in = adjoint_in + jnp.where(upper, 0.0, span(bit - 1 - offset) * got_bwd)
            whole = span(bit)
            grad_cube = (low_grad + high_grad) + grouped((factor * low_fwd) * high_bwd)
            fwd_cube = high_fwd + whole * low_fwd
            bwd_cube = low_bwd + whole * high_bwd
            bit *= 2

        while made < pieces:
            local = local_scans(
                query_proj, key_proj, value_proj, out_grad, factor, weight, made, local
            )
            made += 1
        hyena_out, query_grad, key_grad, value_grad = corrected(
            query_proj, key_proj, value_proj, out_grad, local, factor, weight, state_in, adjoint_in
        )
        filter_grad = grad_cube.T
        filter_update = filter_grad / jnp.sqrt(jnp.mean(filter_grad * filter_grad) + 1e-06)
        return (hyena_out, query_grad, key_grad, value_grad, filter_update)

    return on_device


def solution(mesh):
    placed = (
        P(("groups", "ctx"), None),
        P(("groups", "ctx"), None),
        P(("groups", "ctx"), None),
        P(("groups", "ctx"), None),
        P(),
        P(),
        P(),
    )
    return jax.shard_map(
        make_on_device(mesh.shape["ctx"]),
        mesh=mesh,
        in_specs=placed,
        out_specs=(
            P(("groups", "ctx"), None),
            P(("groups", "ctx"), None),
            P(("groups", "ctx"), None),
            P(("groups", "ctx"), None),
            P("groups", None),
        ),
        check_vma=False,
    )
```

```python
import jax
import jax.numpy as jnp
from jax import lax
from jax.experimental import pallas as pl
from jax.experimental.pallas import tpu as pltpu
from jax.sharding import PartitionSpec as P

BLOCK = 1024
SUB = 256
ROWS = 8
LANE = 128


def carry_kernel(q_ref, k_ref, v_ref, g_ref, p_ref, xend_ref, head_ref, tot_ref, mix_ref, up_ref):
    f32 = jnp.float32
    mix_ref[...] = (k_ref[...].astype(f32) * v_ref[...].astype(f32)).astype(jnp.bfloat16).astype(f32)
    up_ref[...] = g_ref[...].astype(f32) * q_ref[...].astype(f32)
    rows, width = mix_ref.shape
    chunks = rows // ROWS
    for h in range(width // SUB):
        cols = pl.ds(h * SUB, SUB)
        p = p_ref[:, cols]

        def body(c, carry):
            x, tot, a = carry
            fb = pl.multiple_of(c * ROWS, ROWS)
            bb = pl.multiple_of((chunks - 1 - c) * ROWS, ROWS)
            mt = mix_ref[pl.ds(fb, ROWS), cols]
            ut = up_ref[pl.ds(fb, ROWS), cols]
            ub = up_ref[pl.ds(bb, ROWS), cols]
            for j in range(ROWS):
                x = p * x + mt[j : j + 1, :]
                tot = tot + ut[j : j + 1, :] * x
                jb = ROWS - 1 - j
                a = p * a + ub[jb : jb + 1, :]
            return x, tot, a

        zero = jnp.zeros(p.shape, f32)
        x, tot, a = lax.fori_loop(0, chunks, body, (zero, zero, zero))
        xend_ref[:, cols] = x
        head_ref[:, cols] = a
        tot_ref[:, cols] = tot


def to_modes(src_ref, stage_ref, dst_ref):
    modes, width = src_ref.shape
    lanes = width // LANE
    for c in range(lanes):
        stage_ref[c * modes : (c + 1) * modes, :] = src_ref[:, c * LANE : (c + 1) * LANE]
    for m in range(modes):
        dst_ref[m] = stage_ref[pl.ds(m, lanes, stride=modes), :]


def local_kernel(q_ref, k_ref, v_ref, g_ref, pw_ref, rw_ref, *refs):
    f32 = jnp.float32
    if len(refs) == 11:
        refs = refs[2:]
    filt_out, mg_out, mix_ref, up_ref, filt_ref, mg_ref, stage_ref, p_ref, r_ref = refs
    to_modes(pw_ref, stage_ref, p_ref)
    to_modes(rw_ref, stage_ref, r_ref)
    rows, width = q_ref.shape
    lanes = width // LANE
    for c in range(lanes):
        cols = slice(c * LANE, (c + 1) * LANE)
        band = slice(c * rows, (c + 1) * rows)
        kf = k_ref[:, cols].astype(f32)
        vf = v_ref[:, cols].astype(f32)
        mix_ref[band, :] = (kf * vf).astype(jnp.bfloat16).astype(f32)
        up_ref[band, :] = g_ref[:, cols].astype(f32) * q_ref[:, cols].astype(f32)

    def body(t, carry):
        x, a = carry
        p = p_ref[...]
        r = r_ref[...]
        x = p * x + mix_ref[pl.ds(t, lanes, stride=rows), :][None]
        filt_ref[pl.ds(t, lanes, stride=rows), :] = jnp.sum(r * x, axis=0)
        tb = rows - 1 - t
        a = p * a + up_ref[pl.ds(tb, lanes, stride=rows), :][None]
        mg_ref[pl.ds(tb, lanes, stride=rows), :] = jnp.sum(r * a, axis=0)
        return x, a

    zero = jnp.zeros(p_ref.shape, f32)
    lax.fori_loop(0, rows, body, (zero, zero), unroll=8)
    for c in range(lanes):
        cols = slice(c * LANE, (c + 1) * LANE)
        band = slice(c * rows, (c + 1) * rows)
        filt_out[:, cols] = filt_ref[band, :]
        mg_out[:, cols] = mg_ref[band, :]


def correct_kernel(
    q_ref, k_ref, v_ref, g_ref, fl_ref, ml_ref, pw_ref, rw_ref, sw_ref, bw_ref,
    ho_ref, qg_ref, kg_ref, vg_ref,
    filt_ref, mg_ref, stage_ref, p_ref, r_ref, s_ref, b_ref,
):
    f32 = jnp.float32
    for src, dst in ((pw_ref, p_ref), (rw_ref, r_ref), (sw_ref, s_ref), (bw_ref, b_ref)):
        to_modes(src, stage_ref, dst)
    rows, width = q_ref.shape
    lanes = width // LANE

    def body(t, carry):
        z, w = carry
        p = p_ref[...]
        filt_ref[pl.ds(t, lanes, stride=rows), :] = jnp.sum(z, axis=0)
        tb = rows - 1 - t
        mg_ref[pl.ds(tb, lanes, stride=rows), :] = jnp.sum(w, axis=0)
        return z * p, w * p

    p = p_ref[...]
    r = r_ref[...]
    lax.fori_loop(0, rows, body, ((r * p) * s_ref[...], (r * p) * b_ref[...]), unroll=8)
    for c in range(lanes):
        cols = slice(c * LANE, (c + 1) * LANE)
        band = slice(c * rows, (c + 1) * rows)
        filt = fl_ref[:, cols] + filt_ref[band, :]
        mg = ml_ref[:, cols] + mg_ref[band, :]
        ho_ref[:, cols] = (q_ref[:, cols].astype(f32) * filt).astype(jnp.bfloat16)
        qg_ref[:, cols] = (g_ref[:, cols].astype(f32) * filt).astype(jnp.bfloat16)
        kg_ref[:, cols] = (mg * v_ref[:, cols].astype(f32)).astype(jnp.bfloat16)
        vg_ref[:, cols] = (mg * k_ref[:, cols].astype(f32)).astype(jnp.bfloat16)


def local_carries(query_proj, key_proj, value_proj, out_grad, factor):
    rows, width = query_proj.shape
    modes = factor.shape[0]
    big = pl.BlockSpec((rows, BLOCK), lambda i: (0, i))
    small = pl.BlockSpec((modes, BLOCK), lambda i: (0, i))
    return pl.pallas_call(
        carry_kernel,
        grid=(width // BLOCK,),
        in_specs=[big, big, big, big, small],
        out_specs=[small, small, small],
        out_shape=[jax.ShapeDtypeStruct((modes, width), jnp.float32)] * 3,
        scratch_shapes=[pltpu.VMEM((rows, BLOCK), jnp.float32)] * 2,
    )(query_proj, key_proj, value_proj, out_grad, factor)


def local_scans(query_proj, key_proj, value_proj, out_grad, factor, weight, first, previous):
    rows, width = query_proj.shape
    modes = factor.shape[0]
    lanes = BLOCK // LANE
    big = pl.BlockSpec((rows, BLOCK), lambda i: (0, i + first))
    small = pl.BlockSpec((modes, BLOCK), lambda i: (0, i + first))
    operands = [query_proj, key_proj, value_proj, out_grad, factor, weight]
    specs = [big, big, big, big, small, small]
    aliases = {}
    if previous is not None:
        operands += list(previous)
        specs += [pl.BlockSpec(memory_space=pl.ANY)] * 2
        aliases = {6: 0, 7: 1}
    return pl.pallas_call(
        local_kernel,
        grid=(1,),
        in_specs=specs,
        out_specs=[big, big],
        out_shape=[jax.ShapeDtypeStruct((rows, width), jnp.float32)] * 2,
        scratch_shapes=[pltpu.VMEM((lanes * rows, LANE), jnp.float32)] * 4
        + [pltpu.VMEM((lanes * modes, LANE), jnp.float32)]
        + [pltpu.VMEM((modes, lanes, LANE), jnp.float32)] * 2,
        input_output_aliases=aliases,
    )(*operands)


def corrected(query_proj, key_proj, value_proj, out_grad, local, factor, weight, state_in, adjoint_in):
    rows, width = query_proj.shape
    modes = factor.shape[0]
    lanes = BLOCK // LANE
    big = pl.BlockSpec((rows, BLOCK), lambda i: (0, i))
    small = pl.BlockSpec((modes, BLOCK), lambda i: (0, i))
    out_big = jax.ShapeDtypeStruct((rows, width), jnp.bfloat16)
    return pl.pallas_call(
        correct_kernel,
        grid=(width // BLOCK,),
        in_specs=[big] * 6 + [small] * 4,
        out_specs=[big, big, big, big],
        out_shape=[out_big] * 4,
        scratch_shapes=[pltpu.VMEM((lanes * rows, LANE), jnp.float32)] * 2
        + [pltpu.VMEM((lanes * modes, LANE), jnp.float32)]
        + [pltpu.VMEM((modes, lanes, LANE), jnp.float32)] * 4,
    )(query_proj, key_proj, value_proj, out_grad, *local, factor, weight, state_in, adjoint_in)


def split_dot(a, member):
    bf16 = jnp.bfloat16
    top = lax.reduce_precision(a, exponent_bits=8, mantissa_bits=7)
    rest = a - top
    middle = lax.reduce_precision(rest, exponent_bits=8, mantissa_bits=7)
    hi = top.astype(bf16)
    mid = middle.astype(bf16)
    lo = (rest - middle).astype(bf16)
    rows = a.shape[0]
    out = jnp.dot(jnp.concatenate([hi, mid, lo], axis=0), member, preferred_element_type=jnp.float32)
    return (out[:rows] + out[rows : 2 * rows]) + out[2 * rows :]


def make_on_device(count):
    def on_device(query_proj, key_proj, value_proj, out_grad, decay_rate, residue, group_of):
        rows = query_proj.shape[0]
        group_count = decay_rate.shape[0]
        member = (group_of[None, :] == jnp.arange(group_count, dtype=jnp.int32)[:, None]).astype(
            jnp.bfloat16
        )
        modes = decay_rate.shape[1]
        params = split_dot(jnp.concatenate([decay_rate.T, residue.T], axis=0), member)
        rate = params[:modes]
        weight = params[modes:]
        factor = jnp.exp(-rate)
        end_state, head_adjoint, local_total = local_carries(
            query_proj, key_proj, value_proj, out_grad, factor
        )
        width = query_proj.shape[1]
        modes = factor.shape[0]
        pieces = width // BLOCK
        local = None
        made = 0

        def span(blocks):
            return jnp.exp(-rate * (blocks * float(rows)))

        member_t = member.T

        def grouped(a):
            return split_dot(a, member_t)

        place = lax.axis_index("ctx")
        fwd_cube = end_state
        bwd_cube = head_adjoint
        grad_cube = grouped(local_total)
        state_in = jnp.zeros_like(end_state)
        adjoint_in = jnp.zeros_like(head_adjoint)
        bit = 1
        level = 0
        while bit < count:
            pairs = [(i, i ^ bit) for i in range(count)]
            packed = jnp.concatenate([fwd_cube, bwd_cube, grad_cube], axis=1)
            need = pieces if bit * 2 >= count else min(pieces, level)
            level += 1
            if bit == 1:
                got = lax.ppermute(packed, "ctx", pairs)
            else:
                half = packed.shape[1] // 2
                core = place % 2
                mine = lax.dynamic_slice_in_dim(packed, core * half, half, axis=1)
                got_mine = lax.ppermute(mine, "ctx", pairs)
                if need > made:
                    while made < need:
                        local = local_scans(
                            query_proj, key_proj, value_proj, out_grad, factor, weight, made,
                            local,
                        )
                        made += 1
                    got_mine, local = lax.optimization_barrier((got_mine, local))
                got_other = lax.ppermute(got_mine, "ctx", [(i, i ^ 1) for i in range(count)])
                first = jnp.where(core == 0, got_mine, got_other)
                second = jnp.where(core == 0, got_other, got_mine)
                got = jnp.concatenate([first, second], axis=1)
            got_fwd = got[:, :width]
            got_bwd = got[:, width : 2 * width]
            got_grad = got[:, 2 * width :]
            upper = (place & bit) != 0
            offset = (place % bit).astype(jnp.float32)
            low_fwd = jnp.where(upper, got_fwd, fwd_cube)
            high_fwd = jnp.where(upper, fwd_cube, got_fwd)
            low_bwd = jnp.where(upper, got_bwd, bwd_cube)
            high_bwd = jnp.where(upper, bwd_cube, got_bwd)
            low_grad = jnp.where(upper, got_grad, grad_cube)
            high_grad = jnp.where(upper, grad_cube, got_grad)
            state_in = state_in + jnp.where(upper, span(offset) * got_fwd, 0.0)
            adjoint_in = adjoint_in + jnp.where(upper, 0.0, span(bit - 1 - offset) * got_bwd)
            whole = span(bit)
            grad_cube = (low_grad + high_grad) + grouped((factor * low_fwd) * high_bwd)
            fwd_cube = high_fwd + whole * low_fwd
            bwd_cube = low_bwd + whole * high_bwd
            bit *= 2

        while made < pieces:
            local = local_scans(
                query_proj, key_proj, value_proj, out_grad, factor, weight, made, local
            )
            made += 1
        hyena_out, query_grad, key_grad, value_grad = corrected(
            query_proj, key_proj, value_proj, out_grad, local, factor, weight, state_in, adjoint_in
        )
        filter_grad = grad_cube.T
        filter_update = filter_grad / jnp.sqrt(jnp.mean(filter_grad * filter_grad) + 1e-06)
        return (hyena_out, query_grad, key_grad, value_grad, filter_update)

    return on_device


def solution(mesh):
    placed = (
        P(("groups", "ctx"), None),
        P(("groups", "ctx"), None),
        P(("groups", "ctx"), None),
        P(("groups", "ctx"), None),
        P(),
        P(),
        P(),
    )
    return jax.shard_map(
        make_on_device(mesh.shape["ctx"]),
        mesh=mesh,
        in_specs=placed,
        out_specs=(
            P(("groups", "ctx"), None),
            P(("groups", "ctx"), None),
            P(("groups", "ctx"), None),
            P(("groups", "ctx"), None),
            P("groups", None),
        ),
        check_vma=False,
    )
```

```python
import jax
import jax.numpy as jnp
from jax import lax
from jax.experimental import pallas as pl
from jax.experimental.pallas import tpu as pltpu
from jax.sharding import PartitionSpec as P

BLOCK = 1024
SUB = 256
ROWS = 8
LANE = 128


def carry_kernel(
    q_ref, k_ref, v_ref, g_ref, grp_ref, par_ref,
    xend_ref, head_ref, tot_ref, rate_ref, p_ref, w_ref, mix_ref, up_ref,
):
    f32 = jnp.float32
    bf16 = jnp.bfloat16
    groups = par_ref.shape[1]
    modes = rate_ref.shape[0]
    ids = lax.broadcasted_iota(jnp.int32, (groups, grp_ref.shape[1]), 0)
    member = (ids == grp_ref[...]).astype(bf16)
    par = par_ref[...]
    hi = par.astype(bf16)
    rest = par - hi.astype(f32)
    mid = rest.astype(bf16)
    lo = (rest - mid.astype(f32)).astype(bf16)
    prod = jnp.dot(jnp.concatenate([hi, mid, lo], axis=0), member, preferred_element_type=f32)
    both = 2 * modes
    rate = (prod[0:modes] + prod[both : both + modes]) + prod[2 * both : 2 * both + modes]
    weight = (prod[modes:both] + prod[both + modes : 2 * both]) + prod[2 * both + modes :]
    rate_ref[...] = rate
    w_ref[...] = weight
    p_ref[...] = jnp.exp(-rate)
    mix_ref[...] = (k_ref[...].astype(f32) * v_ref[...].astype(f32)).astype(jnp.bfloat16).astype(f32)
    up_ref[...] = g_ref[...].astype(f32) * q_ref[...].astype(f32)
    rows, width = mix_ref.shape
    chunks = rows // ROWS
    for h in range(width // SUB):
        cols = pl.ds(h * SUB, SUB)
        p = p_ref[:, cols]

        def body(c, carry):
            x, tot, a = carry
            fb = pl.multiple_of(c * ROWS, ROWS)
            bb = pl.multiple_of((chunks - 1 - c) * ROWS, ROWS)
            mt = mix_ref[pl.ds(fb, ROWS), cols]
            ut = up_ref[pl.ds(fb, ROWS), cols]
            ub = up_ref[pl.ds(bb, ROWS), cols]
            for j in range(ROWS):
                x = p * x + mt[j : j + 1, :]
                tot = tot + ut[j : j + 1, :] * x
                jb = ROWS - 1 - j
                a = p * a + ub[jb : jb + 1, :]
            return x, tot, a

        zero = jnp.zeros(p.shape, f32)
        x, tot, a = lax.fori_loop(0, chunks, body, (zero, zero, zero))
        xend_ref[:, cols] = x
        head_ref[:, cols] = a
        tot_ref[:, cols] = tot


def to_modes(src_ref, stage_ref, dst_ref):
    modes, width = src_ref.shape
    lanes = width // LANE
    for c in range(lanes):
        stage_ref[c * modes : (c + 1) * modes, :] = src_ref[:, c * LANE : (c + 1) * LANE]
    for m in range(modes):
        dst_ref[m] = stage_ref[pl.ds(m, lanes, stride=modes), :]


def local_kernel(q_ref, k_ref, v_ref, g_ref, pw_ref, rw_ref, *refs):
    f32 = jnp.float32
    if len(refs) == 11:
        refs = refs[2:]
    filt_out, mg_out, mix_ref, up_ref, filt_ref, mg_ref, stage_ref, p_ref, r_ref = refs
    to_modes(pw_ref, stage_ref, p_ref)
    to_modes(rw_ref, stage_ref, r_ref)
    rows, width = q_ref.shape
    lanes = width // LANE
    for c in range(lanes):
        cols = slice(c * LANE, (c + 1) * LANE)
        band = slice(c * rows, (c + 1) * rows)
        kf = k_ref[:, cols].astype(f32)
        vf = v_ref[:, cols].astype(f32)
        mix_ref[band, :] = (kf * vf).astype(jnp.bfloat16).astype(f32)
        up_ref[band, :] = g_ref[:, cols].astype(f32) * q_ref[:, cols].astype(f32)

    def body(t, carry):
        x, a = carry
        p = p_ref[...]
        r = r_ref[...]
        x = p * x + mix_ref[pl.ds(t, lanes, stride=rows), :][None]
        filt_ref[pl.ds(t, lanes, stride=rows), :] = jnp.sum(r * x, axis=0)
        tb = rows - 1 - t
        a = p * a + up_ref[pl.ds(tb, lanes, stride=rows), :][None]
        mg_ref[pl.ds(tb, lanes, stride=rows), :] = jnp.sum(r * a, axis=0)
        return x, a

    zero = jnp.zeros(p_ref.shape, f32)
    lax.fori_loop(0, rows, body, (zero, zero), unroll=4)
    for c in range(lanes):
        cols = slice(c * LANE, (c + 1) * LANE)
        band = slice(c * rows, (c + 1) * rows)
        filt_out[:, cols] = filt_ref[band, :]
        mg_out[:, cols] = mg_ref[band, :]


def correct_kernel(
    q_ref, k_ref, v_ref, g_ref, fl_ref, ml_ref, pw_ref, rw_ref, sw_ref, bw_ref,
    ho_ref, qg_ref, kg_ref, vg_ref,
    filt_ref, mg_ref, stage_ref, p_ref, r_ref, s_ref, b_ref,
):
    f32 = jnp.float32
    for src, dst in ((pw_ref, p_ref), (rw_ref, r_ref), (sw_ref, s_ref), (bw_ref, b_ref)):
        to_modes(src, stage_ref, dst)
    rows, width = q_ref.shape
    lanes = width // LANE

    def body(t, carry):
        z, w = carry
        p = p_ref[...]
        filt_ref[pl.ds(t, lanes, stride=rows), :] = jnp.sum(z, axis=0)
        tb = rows - 1 - t
        mg_ref[pl.ds(tb, lanes, stride=rows), :] = jnp.sum(w, axis=0)
        return z * p, w * p

    p = p_ref[...]
    r = r_ref[...]
    lax.fori_loop(0, rows, body, ((r * p) * s_ref[...], (r * p) * b_ref[...]), unroll=8)
    for c in range(lanes):
        cols = slice(c * LANE, (c + 1) * LANE)
        band = slice(c * rows, (c + 1) * rows)
        filt = fl_ref[:, cols] + filt_ref[band, :]
        mg = ml_ref[:, cols] + mg_ref[band, :]
        ho_ref[:, cols] = (q_ref[:, cols].astype(f32) * filt).astype(jnp.bfloat16)
        qg_ref[:, cols] = (g_ref[:, cols].astype(f32) * filt).astype(jnp.bfloat16)
        kg_ref[:, cols] = (mg * v_ref[:, cols].astype(f32)).astype(jnp.bfloat16)
        vg_ref[:, cols] = (mg * k_ref[:, cols].astype(f32)).astype(jnp.bfloat16)


def local_carries(query_proj, key_proj, value_proj, out_grad, group_row, params):
    rows, width = query_proj.shape
    modes = params.shape[0] // 2
    big = pl.BlockSpec((rows, BLOCK), lambda i: (0, i))
    small = pl.BlockSpec((modes, BLOCK), lambda i: (0, i))
    row = pl.BlockSpec((1, BLOCK), lambda i: (0, i))
    whole = pl.BlockSpec(params.shape, lambda i: (0, 0))
    return pl.pallas_call(
        carry_kernel,
        grid=(width // BLOCK,),
        in_specs=[big, big, big, big, row, whole],
        out_specs=[small] * 6,
        out_shape=[jax.ShapeDtypeStruct((modes, width), jnp.float32)] * 6,
        scratch_shapes=[pltpu.VMEM((rows, BLOCK), jnp.float32)] * 2,
    )(query_proj, key_proj, value_proj, out_grad, group_row, params)


def local_scans(query_proj, key_proj, value_proj, out_grad, factor, weight, first, previous):
    rows, width = query_proj.shape
    modes = factor.shape[0]
    lanes = BLOCK // LANE
    big = pl.BlockSpec((rows, BLOCK), lambda i: (0, i + first))
    small = pl.BlockSpec((modes, BLOCK), lambda i: (0, i + first))
    operands = [query_proj, key_proj, value_proj, out_grad, factor, weight]
    specs = [big, big, big, big, small, small]
    aliases = {}
    if previous is not None:
        operands += list(previous)
        specs += [pl.BlockSpec(memory_space=pl.ANY)] * 2
        aliases = {6: 0, 7: 1}
    return pl.pallas_call(
        local_kernel,
        grid=(1,),
        in_specs=specs,
        out_specs=[big, big],
        out_shape=[jax.ShapeDtypeStruct((rows, width), jnp.float32)] * 2,
        scratch_shapes=[pltpu.VMEM((lanes * rows, LANE), jnp.float32)] * 4
        + [pltpu.VMEM((lanes * modes, LANE), jnp.float32)]
        + [pltpu.VMEM((modes, lanes, LANE), jnp.float32)] * 2,
        input_output_aliases=aliases,
    )(*operands)


def corrected(query_proj, key_proj, value_proj, out_grad, local, factor, weight, state_in, adjoint_in):
    rows, width = query_proj.shape
    modes = factor.shape[0]
    lanes = BLOCK // LANE
    big = pl.BlockSpec((rows, BLOCK), lambda i: (0, i))
    small = pl.BlockSpec((modes, BLOCK), lambda i: (0, i))
    out_big = jax.ShapeDtypeStruct((rows, width), jnp.bfloat16)
    return pl.pallas_call(
        correct_kernel,
        grid=(width // BLOCK,),
        in_specs=[big] * 6 + [small] * 4,
        out_specs=[big, big, big, big],
        out_shape=[out_big] * 4,
        scratch_shapes=[pltpu.VMEM((lanes * rows, LANE), jnp.float32)] * 2
        + [pltpu.VMEM((lanes * modes, LANE), jnp.float32)]
        + [pltpu.VMEM((modes, lanes, LANE), jnp.float32)] * 4,
    )(query_proj, key_proj, value_proj, out_grad, *local, factor, weight, state_in, adjoint_in)


def split_dot(a, member):
    bf16 = jnp.bfloat16
    top = lax.reduce_precision(a, exponent_bits=8, mantissa_bits=7)
    rest = a - top
    middle = lax.reduce_precision(rest, exponent_bits=8, mantissa_bits=7)
    hi = top.astype(bf16)
    mid = middle.astype(bf16)
    lo = (rest - middle).astype(bf16)
    rows = a.shape[0]
    out = jnp.dot(jnp.concatenate([hi, mid, lo], axis=0), member, preferred_element_type=jnp.float32)
    return (out[:rows] + out[rows : 2 * rows]) + out[2 * rows :]


def make_on_device(count):
    def on_device(query_proj, key_proj, value_proj, out_grad, decay_rate, residue, group_of):
        rows = query_proj.shape[0]
        group_count = decay_rate.shape[0]
        member = (group_of[None, :] == jnp.arange(group_count, dtype=jnp.int32)[:, None]).astype(
            jnp.bfloat16
        )
        params = jnp.concatenate([decay_rate.T, residue.T], axis=0)
        end_state, head_adjoint, local_total, rate, factor, weight = local_carries(
            query_proj, key_proj, value_proj, out_grad, group_of.reshape(1, -1), params
        )
        width = query_proj.shape[1]
        modes = factor.shape[0]
        pieces = width // BLOCK
        local = None
        made = 0

        def span(blocks):
            return jnp.exp(-rate * (blocks * float(rows)))

        member_t = member.T

        def grouped(a):
            return split_dot(a, member_t)

        place = lax.axis_index("ctx")
        fwd_cube = end_state
        bwd_cube = head_adjoint
        grad_cube = grouped(local_total)
        state_in = jnp.zeros_like(end_state)
        adjoint_in = jnp.zeros_like(head_adjoint)
        bit = 1
        level = 0
        while bit < count:
            pairs = [(i, i ^ bit) for i in range(count)]
            packed = jnp.concatenate([fwd_cube, bwd_cube, grad_cube], axis=1)
            need = pieces if bit * 2 >= count else min(pieces, level)
            level += 1
            if bit == 1:
                got = lax.ppermute(packed, "ctx", pairs)
            else:
                half = packed.shape[1] // 2
                core = place % 2
                mine = lax.dynamic_slice_in_dim(packed, core * half, half, axis=1)
                got_mine = lax.ppermute(mine, "ctx", pairs)
                if need > made:
                    while made < need:
                        local = local_scans(
                            query_proj, key_proj, value_proj, out_grad, factor, weight, made,
                            local,
                        )
                        made += 1
                    got_mine, local = lax.optimization_barrier((got_mine, local))
                got_other = lax.ppermute(got_mine, "ctx", [(i, i ^ 1) for i in range(count)])
                first = jnp.where(core == 0, got_mine, got_other)
                second = jnp.where(core == 0, got_other, got_mine)
                got = jnp.concatenate([first, second], axis=1)
            got_fwd = got[:, :width]
            got_bwd = got[:, width : 2 * width]
            got_grad = got[:, 2 * width :]
            upper = (place & bit) != 0
            offset = (place % bit).astype(jnp.float32)
            low_fwd = jnp.where(upper, got_fwd, fwd_cube)
            high_fwd = jnp.where(upper, fwd_cube, got_fwd)
            low_bwd = jnp.where(upper, got_bwd, bwd_cube)
            high_bwd = jnp.where(upper, bwd_cube, got_bwd)
            low_grad = jnp.where(upper, got_grad, grad_cube)
            high_grad = jnp.where(upper, grad_cube, got_grad)
            state_in = state_in + jnp.where(upper, span(offset) * got_fwd, 0.0)
            adjoint_in = adjoint_in + jnp.where(upper, 0.0, span(bit - 1 - offset) * got_bwd)
            whole = span(bit)
            grad_cube = (low_grad + high_grad) + grouped((factor * low_fwd) * high_bwd)
            fwd_cube = high_fwd + whole * low_fwd
            bwd_cube = low_bwd + whole * high_bwd
            bit *= 2

        while made < pieces:
            local = local_scans(
                query_proj, key_proj, value_proj, out_grad, factor, weight, made, local
            )
            made += 1
        hyena_out, query_grad, key_grad, value_grad = corrected(
            query_proj, key_proj, value_proj, out_grad, local, factor, weight, state_in, adjoint_in
        )
        filter_grad = grad_cube.T
        filter_update = filter_grad / jnp.sqrt(jnp.mean(filter_grad * filter_grad) + 1e-06)
        return (hyena_out, query_grad, key_grad, value_grad, filter_update)

    return on_device


def solution(mesh):
    placed = (
        P(("groups", "ctx"), None),
        P(("groups", "ctx"), None),
        P(("groups", "ctx"), None),
        P(("groups", "ctx"), None),
        P(),
        P(),
        P(),
    )
    return jax.shard_map(
        make_on_device(mesh.shape["ctx"]),
        mesh=mesh,
        in_specs=placed,
        out_specs=(
            P(("groups", "ctx"), None),
            P(("groups", "ctx"), None),
            P(("groups", "ctx"), None),
            P(("groups", "ctx"), None),
            P("groups", None),
        ),
        check_vma=False,
    )
```

```python
import jax
import jax.numpy as jnp
from jax import lax
from jax.experimental import pallas as pl
from jax.experimental.pallas import tpu as pltpu
from jax.sharding import PartitionSpec as P

BLOCK = 1024
SUB = 256
ROWS = 8
LANE = 128


def gathered(par, member):
    f32 = jnp.float32
    bf16 = jnp.bfloat16
    hi = par.astype(bf16)
    rest = par - hi.astype(f32)
    mid = rest.astype(bf16)
    lo = (rest - mid.astype(f32)).astype(bf16)
    dims = (((0,), (0,)), ((), ()))

    def one(piece):
        return lax.dot_general(piece, member, dims, preferred_element_type=f32)

    return (one(hi) + one(mid)) + one(lo)


def carry_kernel(
    q_ref, k_ref, v_ref, g_ref, grp_ref, dr_ref, rs_ref,
    xend_ref, head_ref, tot_ref, rate_ref, p_ref, w_ref, mix_ref, up_ref,
):
    f32 = jnp.float32
    bf16 = jnp.bfloat16
    groups = dr_ref.shape[0]
    ids = lax.broadcasted_iota(jnp.int32, (groups, grp_ref.shape[1]), 0)
    member = (ids == grp_ref[...]).astype(bf16)
    rate = gathered(dr_ref[...], member)
    weight = gathered(rs_ref[...], member)
    rate_ref[...] = rate
    w_ref[...] = weight
    p_ref[...] = jnp.exp(-rate)
    mix_ref[...] = (k_ref[...].astype(f32) * v_ref[...].astype(f32)).astype(jnp.bfloat16).astype(f32)
    up_ref[...] = g_ref[...].astype(f32) * q_ref[...].astype(f32)
    rows, width = mix_ref.shape
    chunks = rows // ROWS
    for h in range(width // SUB):
        cols = pl.ds(h * SUB, SUB)
        p = p_ref[:, cols]

        def body(c, carry):
            x, tot, a = carry
            fb = pl.multiple_of(c * ROWS, ROWS)
            bb = pl.multiple_of((chunks - 1 - c) * ROWS, ROWS)
            mt = mix_ref[pl.ds(fb, ROWS), cols]
            ut = up_ref[pl.ds(fb, ROWS), cols]
            ub = up_ref[pl.ds(bb, ROWS), cols]
            for j in range(ROWS):
                x = p * x + mt[j : j + 1, :]
                tot = tot + ut[j : j + 1, :] * x
                jb = ROWS - 1 - j
                a = p * a + ub[jb : jb + 1, :]
            return x, tot, a

        zero = jnp.zeros(p.shape, f32)
        x, tot, a = lax.fori_loop(0, chunks, body, (zero, zero, zero))
        xend_ref[:, cols] = x
        head_ref[:, cols] = a
        tot_ref[:, cols] = tot


def to_modes(src_ref, stage_ref, dst_ref):
    modes, width = src_ref.shape
    lanes = width // LANE
    for c in range(lanes):
        stage_ref[c * modes : (c + 1) * modes, :] = src_ref[:, c * LANE : (c + 1) * LANE]
    for m in range(modes):
        dst_ref[m] = stage_ref[pl.ds(m, lanes, stride=modes), :]


def local_kernel(q_ref, k_ref, v_ref, g_ref, pw_ref, rw_ref, *refs):
    f32 = jnp.float32
    if len(refs) == 11:
        refs = refs[2:]
    filt_out, mg_out, mix_ref, up_ref, filt_ref, mg_ref, stage_ref, p_ref, r_ref = refs
    to_modes(pw_ref, stage_ref, p_ref)
    to_modes(rw_ref, stage_ref, r_ref)
    rows, width = q_ref.shape
    lanes = width // LANE
    for c in range(lanes):
        cols = slice(c * LANE, (c + 1) * LANE)
        band = slice(c * rows, (c + 1) * rows)
        kf = k_ref[:, cols].astype(f32)
        vf = v_ref[:, cols].astype(f32)
        mix_ref[band, :] = (kf * vf).astype(jnp.bfloat16).astype(f32)
        up_ref[band, :] = g_ref[:, cols].astype(f32) * q_ref[:, cols].astype(f32)

    def body(t, carry):
        x, a = carry
        p = p_ref[...]
        r = r_ref[...]
        x = p * x + mix_ref[pl.ds(t, lanes, stride=rows), :][None]
        filt_ref[pl.ds(t, lanes, stride=rows), :] = jnp.sum(r * x, axis=0)
        tb = rows - 1 - t
        a = p * a + up_ref[pl.ds(tb, lanes, stride=rows), :][None]
        mg_ref[pl.ds(tb, lanes, stride=rows), :] = jnp.sum(r * a, axis=0)
        return x, a

    zero = jnp.zeros(p_ref.shape, f32)
    lax.fori_loop(0, rows, body, (zero, zero), unroll=4)
    for c in range(lanes):
        cols = slice(c * LANE, (c + 1) * LANE)
        band = slice(c * rows, (c + 1) * rows)
        filt_out[:, cols] = filt_ref[band, :]
        mg_out[:, cols] = mg_ref[band, :]


def correct_kernel(
    q_ref, k_ref, v_ref, g_ref, fl_ref, ml_ref, pw_ref, rw_ref, sw_ref, bw_ref,
    ho_ref, qg_ref, kg_ref, vg_ref,
    filt_ref, mg_ref, stage_ref, p_ref, r_ref, s_ref, b_ref,
):
    f32 = jnp.float32
    for src, dst in ((pw_ref, p_ref), (rw_ref, r_ref), (sw_ref, s_ref), (bw_ref, b_ref)):
        to_modes(src, stage_ref, dst)
    rows, width = q_ref.shape
    lanes = width // LANE

    def body(t, carry):
        z, w = carry
        p = p_ref[...]
        filt_ref[pl.ds(t, lanes, stride=rows), :] = jnp.sum(z, axis=0)
        tb = rows - 1 - t
        mg_ref[pl.ds(tb, lanes, stride=rows), :] = jnp.sum(w, axis=0)
        return z * p, w * p

    p = p_ref[...]
    r = r_ref[...]
    lax.fori_loop(0, rows, body, ((r * p) * s_ref[...], (r * p) * b_ref[...]), unroll=8)
    for c in range(lanes):
        cols = slice(c * LANE, (c + 1) * LANE)
        band = slice(c * rows, (c + 1) * rows)
        filt = fl_ref[:, cols] + filt_ref[band, :]
        mg = ml_ref[:, cols] + mg_ref[band, :]
        ho_ref[:, cols] = (q_ref[:, cols].astype(f32) * filt).astype(jnp.bfloat16)
        qg_ref[:, cols] = (g_ref[:, cols].astype(f32) * filt).astype(jnp.bfloat16)
        kg_ref[:, cols] = (mg * v_ref[:, cols].astype(f32)).astype(jnp.bfloat16)
        vg_ref[:, cols] = (mg * k_ref[:, cols].astype(f32)).astype(jnp.bfloat16)


def local_carries(query_proj, key_proj, value_proj, out_grad, group_row, decay_rate, residue):
    rows, width = query_proj.shape
    modes = decay_rate.shape[1]
    big = pl.BlockSpec((rows, BLOCK), lambda i: (0, i))
    small = pl.BlockSpec((modes, BLOCK), lambda i: (0, i))
    row = pl.BlockSpec((1, BLOCK), lambda i: (0, i))
    whole = pl.BlockSpec(decay_rate.shape, lambda i: (0, 0))
    return pl.pallas_call(
        carry_kernel,
        grid=(width // BLOCK,),
        in_specs=[big, big, big, big, row, whole, whole],
        out_specs=[small] * 6,
        out_shape=[jax.ShapeDtypeStruct((modes, width), jnp.float32)] * 6,
        scratch_shapes=[pltpu.VMEM((rows, BLOCK), jnp.float32)] * 2,
    )(query_proj, key_proj, value_proj, out_grad, group_row, decay_rate, residue)


def local_scans(query_proj, key_proj, value_proj, out_grad, factor, weight, first, previous):
    rows, width = query_proj.shape
    modes = factor.shape[0]
    lanes = BLOCK // LANE
    big = pl.BlockSpec((rows, BLOCK), lambda i: (0, i + first))
    small = pl.BlockSpec((modes, BLOCK), lambda i: (0, i + first))
    operands = [query_proj, key_proj, value_proj, out_grad, factor, weight]
    specs = [big, big, big, big, small, small]
    aliases = {}
    if previous is not None:
        operands += list(previous)
        specs += [pl.BlockSpec(memory_space=pl.ANY)] * 2
        aliases = {6: 0, 7: 1}
    return pl.pallas_call(
        local_kernel,
        grid=(1,),
        in_specs=specs,
        out_specs=[big, big],
        out_shape=[jax.ShapeDtypeStruct((rows, width), jnp.float32)] * 2,
        scratch_shapes=[pltpu.VMEM((lanes * rows, LANE), jnp.float32)] * 4
        + [pltpu.VMEM((lanes * modes, LANE), jnp.float32)]
        + [pltpu.VMEM((modes, lanes, LANE), jnp.float32)] * 2,
        input_output_aliases=aliases,
    )(*operands)


def corrected(query_proj, key_proj, value_proj, out_grad, local, factor, weight, state_in, adjoint_in):
    rows, width = query_proj.shape
    modes = factor.shape[0]
    lanes = BLOCK // LANE
    big = pl.BlockSpec((rows, BLOCK), lambda i: (0, i))
    small = pl.BlockSpec((modes, BLOCK), lambda i: (0, i))
    out_big = jax.ShapeDtypeStruct((rows, width), jnp.bfloat16)
    return pl.pallas_call(
        correct_kernel,
        grid=(width // BLOCK,),
        in_specs=[big] * 6 + [small] * 4,
        out_specs=[big, big, big, big],
        out_shape=[out_big] * 4,
        scratch_shapes=[pltpu.VMEM((lanes * rows, LANE), jnp.float32)] * 2
        + [pltpu.VMEM((lanes * modes, LANE), jnp.float32)]
        + [pltpu.VMEM((modes, lanes, LANE), jnp.float32)] * 4,
    )(query_proj, key_proj, value_proj, out_grad, *local, factor, weight, state_in, adjoint_in)


def split_dot(a, member):
    bf16 = jnp.bfloat16
    top = lax.reduce_precision(a, exponent_bits=8, mantissa_bits=7)
    rest = a - top
    middle = lax.reduce_precision(rest, exponent_bits=8, mantissa_bits=7)
    hi = top.astype(bf16)
    mid = middle.astype(bf16)
    lo = (rest - middle).astype(bf16)
    rows = a.shape[0]
    out = jnp.dot(jnp.concatenate([hi, mid, lo], axis=0), member, preferred_element_type=jnp.float32)
    return (out[:rows] + out[rows : 2 * rows]) + out[2 * rows :]


def make_on_device(count):
    def on_device(query_proj, key_proj, value_proj, out_grad, decay_rate, residue, group_of):
        rows = query_proj.shape[0]
        group_count = decay_rate.shape[0]
        member = (group_of[None, :] == jnp.arange(group_count, dtype=jnp.int32)[:, None]).astype(
            jnp.bfloat16
        )
        end_state, head_adjoint, local_total, rate, factor, weight = local_carries(
            query_proj, key_proj, value_proj, out_grad, group_of.reshape(1, -1), decay_rate, residue
        )
        width = query_proj.shape[1]
        modes = factor.shape[0]
        pieces = width // BLOCK
        local = None
        made = 0

        def span(blocks):
            return jnp.exp(-rate * (blocks * float(rows)))

        member_t = member.T

        def grouped(a):
            return split_dot(a, member_t)

        place = lax.axis_index("ctx")
        fwd_cube = end_state
        bwd_cube = head_adjoint
        grad_cube = grouped(local_total)
        state_in = jnp.zeros_like(end_state)
        adjoint_in = jnp.zeros_like(head_adjoint)
        bit = 1
        level = 0
        while bit < count:
            pairs = [(i, i ^ bit) for i in range(count)]
            packed = jnp.concatenate([fwd_cube, bwd_cube, grad_cube], axis=1)
            need = pieces if bit * 2 >= count else min(pieces, level)
            level += 1
            if bit == 1:
                got = lax.ppermute(packed, "ctx", pairs)
            else:
                half = packed.shape[1] // 2
                core = place % 2
                mine = lax.dynamic_slice_in_dim(packed, core * half, half, axis=1)
                got_mine = lax.ppermute(mine, "ctx", pairs)
                if need > made:
                    while made < need:
                        local = local_scans(
                            query_proj, key_proj, value_proj, out_grad, factor, weight, made,
                            local,
                        )
                        made += 1
                    got_mine, local = lax.optimization_barrier((got_mine, local))
                got_other = lax.ppermute(got_mine, "ctx", [(i, i ^ 1) for i in range(count)])
                first = jnp.where(core == 0, got_mine, got_other)
                second = jnp.where(core == 0, got_other, got_mine)
                got = jnp.concatenate([first, second], axis=1)
            got_fwd = got[:, :width]
            got_bwd = got[:, width : 2 * width]
            got_grad = got[:, 2 * width :]
            upper = (place & bit) != 0
            offset = (place % bit).astype(jnp.float32)
            low_fwd = jnp.where(upper, got_fwd, fwd_cube)
            high_fwd = jnp.where(upper, fwd_cube, got_fwd)
            low_bwd = jnp.where(upper, got_bwd, bwd_cube)
            high_bwd = jnp.where(upper, bwd_cube, got_bwd)
            low_grad = jnp.where(upper, got_grad, grad_cube)
            high_grad = jnp.where(upper, grad_cube, got_grad)
            state_in = state_in + jnp.where(upper, span(offset) * got_fwd, 0.0)
            adjoint_in = adjoint_in + jnp.where(upper, 0.0, span(bit - 1 - offset) * got_bwd)
            whole = span(bit)
            grad_cube = (low_grad + high_grad) + grouped((factor * low_fwd) * high_bwd)
            fwd_cube = high_fwd + whole * low_fwd
            bwd_cube = low_bwd + whole * high_bwd
            bit *= 2

        while made < pieces:
            local = local_scans(
                query_proj, key_proj, value_proj, out_grad, factor, weight, made, local
            )
            made += 1
        hyena_out, query_grad, key_grad, value_grad = corrected(
            query_proj, key_proj, value_proj, out_grad, local, factor, weight, state_in, adjoint_in
        )
        filter_grad = grad_cube.T
        filter_update = filter_grad / jnp.sqrt(jnp.mean(filter_grad * filter_grad) + 1e-06)
        return (hyena_out, query_grad, key_grad, value_grad, filter_update)

    return on_device


def solution(mesh):
    placed = (
        P(("groups", "ctx"), None),
        P(("groups", "ctx"), None),
        P(("groups", "ctx"), None),
        P(("groups", "ctx"), None),
        P(),
        P(),
        P(),
    )
    return jax.shard_map(
        make_on_device(mesh.shape["ctx"]),
        mesh=mesh,
        in_specs=placed,
        out_specs=(
            P(("groups", "ctx"), None),
            P(("groups", "ctx"), None),
            P(("groups", "ctx"), None),
            P(("groups", "ctx"), None),
            P("groups", None),
        ),
        check_vma=False,
    )
```

```python
import jax
import jax.numpy as jnp
from jax import lax
from jax.experimental import pallas as pl
from jax.experimental.pallas import tpu as pltpu
from jax.sharding import PartitionSpec as P

BLOCK = 1024
SUB = 256
ROWS = 8
LANE = 128


def carry_kernel(
    q_ref, k_ref, v_ref, g_ref, grp_ref, par_ref,
    xend_ref, head_ref, tot_ref, rate_ref, p_ref, w_ref, mix_ref, up_ref,
):
    f32 = jnp.float32
    bf16 = jnp.bfloat16
    groups = par_ref.shape[1]
    modes = rate_ref.shape[0]
    ids = lax.broadcasted_iota(jnp.int32, (groups, grp_ref.shape[1]), 0)
    member = (ids == grp_ref[...]).astype(bf16)
    par = par_ref[...]
    hi = par.astype(bf16)
    rest = par - hi.astype(f32)
    mid = rest.astype(bf16)
    lo = (rest - mid.astype(f32)).astype(bf16)
    prod = jnp.dot(jnp.concatenate([hi, mid, lo], axis=0), member, preferred_element_type=f32)
    both = 2 * modes
    rate = (prod[0:modes] + prod[both : both + modes]) + prod[2 * both : 2 * both + modes]
    weight = (prod[modes:both] + prod[both + modes : 2 * both]) + prod[2 * both + modes :]
    rate_ref[...] = rate
    w_ref[...] = weight
    p_ref[...] = jnp.exp(-rate)
    mix_ref[...] = (k_ref[...].astype(f32) * v_ref[...].astype(f32)).astype(jnp.bfloat16).astype(f32)
    up_ref[...] = g_ref[...].astype(f32) * q_ref[...].astype(f32)
    rows, width = mix_ref.shape
    chunks = rows // ROWS
    for h in range(width // SUB):
        cols = pl.ds(h * SUB, SUB)
        p = p_ref[:, cols]

        def body(c, carry):
            x, tot, a = carry
            fb = pl.multiple_of(c * ROWS, ROWS)
            bb = pl.multiple_of((chunks - 1 - c) * ROWS, ROWS)
            mt = mix_ref[pl.ds(fb, ROWS), cols]
            ut = up_ref[pl.ds(fb, ROWS), cols]
            ub = up_ref[pl.ds(bb, ROWS), cols]
            for j in range(ROWS):
                x = p * x + mt[j : j + 1, :]
                tot = tot + ut[j : j + 1, :] * x
                jb = ROWS - 1 - j
                a = p * a + ub[jb : jb + 1, :]
            return x, tot, a

        zero = jnp.zeros(p.shape, f32)
        x, tot, a = lax.fori_loop(0, chunks, body, (zero, zero, zero))
        xend_ref[:, cols] = x
        head_ref[:, cols] = a
        tot_ref[:, cols] = tot


def to_modes(src_ref, stage_ref, dst_ref):
    modes, width = src_ref.shape
    lanes = width // LANE
    for c in range(lanes):
        stage_ref[c * modes : (c + 1) * modes, :] = src_ref[:, c * LANE : (c + 1) * LANE]
    for m in range(modes):
        dst_ref[m] = stage_ref[pl.ds(m, lanes, stride=modes), :]


def local_kernel(q_ref, k_ref, v_ref, g_ref, pw_ref, rw_ref, *refs):
    f32 = jnp.float32
    if len(refs) == 11:
        refs = refs[2:]
    filt_out, mg_out, mix_ref, up_ref, filt_ref, mg_ref, stage_ref, p_ref, r_ref = refs
    to_modes(pw_ref, stage_ref, p_ref)
    to_modes(rw_ref, stage_ref, r_ref)
    rows, width = q_ref.shape
    lanes = width // LANE
    for c in range(lanes):
        cols = slice(c * LANE, (c + 1) * LANE)
        band = slice(c * rows, (c + 1) * rows)
        kf = k_ref[:, cols].astype(f32)
        vf = v_ref[:, cols].astype(f32)
        mix_ref[band, :] = (kf * vf).astype(jnp.bfloat16).astype(f32)
        up_ref[band, :] = g_ref[:, cols].astype(f32) * q_ref[:, cols].astype(f32)

    def body(t, carry):
        x, a = carry
        p = p_ref[...]
        r = r_ref[...]
        x = p * x + mix_ref[pl.ds(t, lanes, stride=rows), :][None]
        filt_ref[pl.ds(t, lanes, stride=rows), :] = jnp.sum(r * x, axis=0)
        tb = rows - 1 - t
        a = p * a + up_ref[pl.ds(tb, lanes, stride=rows), :][None]
        mg_ref[pl.ds(tb, lanes, stride=rows), :] = jnp.sum(r * a, axis=0)
        return x, a

    zero = jnp.zeros(p_ref.shape, f32)
    lax.fori_loop(0, rows, body, (zero, zero), unroll=4)
    for c in range(lanes):
        cols = slice(c * LANE, (c + 1) * LANE)
        band = slice(c * rows, (c + 1) * rows)
        filt_out[:, cols] = filt_ref[band, :]
        mg_out[:, cols] = mg_ref[band, :]


def correct_kernel(
    q_ref, k_ref, v_ref, g_ref, fl_ref, ml_ref, pw_ref, rw_ref, sw_ref, bw_ref,
    ho_ref, qg_ref, kg_ref, vg_ref,
    filt_ref, mg_ref, stage_ref, p_ref, r_ref, s_ref, b_ref,
):
    f32 = jnp.float32
    for src, dst in ((pw_ref, p_ref), (rw_ref, r_ref), (sw_ref, s_ref), (bw_ref, b_ref)):
        to_modes(src, stage_ref, dst)
    rows, width = q_ref.shape
    lanes = width // LANE

    def body(t, carry):
        z, w = carry
        p = p_ref[...]
        filt_ref[pl.ds(t, lanes, stride=rows), :] = jnp.sum(z, axis=0)
        tb = rows - 1 - t
        mg_ref[pl.ds(tb, lanes, stride=rows), :] = jnp.sum(w, axis=0)
        return z * p, w * p

    p = p_ref[...]
    r = r_ref[...]
    lax.fori_loop(0, rows, body, ((r * p) * s_ref[...], (r * p) * b_ref[...]), unroll=16)
    for c in range(lanes):
        cols = slice(c * LANE, (c + 1) * LANE)
        band = slice(c * rows, (c + 1) * rows)
        filt = fl_ref[:, cols] + filt_ref[band, :]
        mg = ml_ref[:, cols] + mg_ref[band, :]
        ho_ref[:, cols] = (q_ref[:, cols].astype(f32) * filt).astype(jnp.bfloat16)
        qg_ref[:, cols] = (g_ref[:, cols].astype(f32) * filt).astype(jnp.bfloat16)
        kg_ref[:, cols] = (mg * v_ref[:, cols].astype(f32)).astype(jnp.bfloat16)
        vg_ref[:, cols] = (mg * k_ref[:, cols].astype(f32)).astype(jnp.bfloat16)


def local_carries(query_proj, key_proj, value_proj, out_grad, group_row, params):
    rows, width = query_proj.shape
    modes = params.shape[0] // 2
    big = pl.BlockSpec((rows, BLOCK), lambda i: (0, i))
    small = pl.BlockSpec((modes, BLOCK), lambda i: (0, i))
    row = pl.BlockSpec((1, BLOCK), lambda i: (0, i))
    whole = pl.BlockSpec(params.shape, lambda i: (0, 0))
    return pl.pallas_call(
        carry_kernel,
        grid=(width // BLOCK,),
        in_specs=[big, big, big, big, row, whole],
        out_specs=[small] * 6,
        out_shape=[jax.ShapeDtypeStruct((modes, width), jnp.float32)] * 6,
        scratch_shapes=[pltpu.VMEM((rows, BLOCK), jnp.float32)] * 2,
    )(query_proj, key_proj, value_proj, out_grad, group_row, params)


def local_scans(query_proj, key_proj, value_proj, out_grad, factor, weight, first, previous):
    rows, width = query_proj.shape
    modes = factor.shape[0]
    lanes = BLOCK // LANE
    big = pl.BlockSpec((rows, BLOCK), lambda i: (0, i + first))
    small = pl.BlockSpec((modes, BLOCK), lambda i: (0, i + first))
    operands = [query_proj, key_proj, value_proj, out_grad, factor, weight]
    specs = [big, big, big, big, small, small]
    aliases = {}
    if previous is not None:
        operands += list(previous)
        specs += [pl.BlockSpec(memory_space=pl.ANY)] * 2
        aliases = {6: 0, 7: 1}
    return pl.pallas_call(
        local_kernel,
        grid=(1,),
        in_specs=specs,
        out_specs=[big, big],
        out_shape=[jax.ShapeDtypeStruct((rows, width), jnp.float32)] * 2,
        scratch_shapes=[pltpu.VMEM((lanes * rows, LANE), jnp.float32)] * 4
        + [pltpu.VMEM((lanes * modes, LANE), jnp.float32)]
        + [pltpu.VMEM((modes, lanes, LANE), jnp.float32)] * 2,
        input_output_aliases=aliases,
    )(*operands)


def corrected(query_proj, key_proj, value_proj, out_grad, local, factor, weight, state_in, adjoint_in):
    rows, width = query_proj.shape
    modes = factor.shape[0]
    lanes = BLOCK // LANE
    big = pl.BlockSpec((rows, BLOCK), lambda i: (0, i))
    small = pl.BlockSpec((modes, BLOCK), lambda i: (0, i))
    out_big = jax.ShapeDtypeStruct((rows, width), jnp.bfloat16)
    return pl.pallas_call(
        correct_kernel,
        grid=(width // BLOCK,),
        in_specs=[big] * 6 + [small] * 4,
        out_specs=[big, big, big, big],
        out_shape=[out_big] * 4,
        scratch_shapes=[pltpu.VMEM((lanes * rows, LANE), jnp.float32)] * 2
        + [pltpu.VMEM((lanes * modes, LANE), jnp.float32)]
        + [pltpu.VMEM((modes, lanes, LANE), jnp.float32)] * 4,
    )(query_proj, key_proj, value_proj, out_grad, *local, factor, weight, state_in, adjoint_in)


def split_dot(a, member):
    bf16 = jnp.bfloat16
    top = lax.reduce_precision(a, exponent_bits=8, mantissa_bits=7)
    rest = a - top
    middle = lax.reduce_precision(rest, exponent_bits=8, mantissa_bits=7)
    hi = top.astype(bf16)
    mid = middle.astype(bf16)
    lo = (rest - middle).astype(bf16)
    rows = a.shape[0]
    out = jnp.dot(jnp.concatenate([hi, mid, lo], axis=0), member, preferred_element_type=jnp.float32)
    return (out[:rows] + out[rows : 2 * rows]) + out[2 * rows :]


def make_on_device(count):
    def on_device(query_proj, key_proj, value_proj, out_grad, decay_rate, residue, group_of):
        rows = query_proj.shape[0]
        group_count = decay_rate.shape[0]
        member = (group_of[None, :] == jnp.arange(group_count, dtype=jnp.int32)[:, None]).astype(
            jnp.bfloat16
        )
        params = jnp.concatenate([decay_rate.T, residue.T], axis=0)
        end_state, head_adjoint, local_total, rate, factor, weight = local_carries(
            query_proj, key_proj, value_proj, out_grad, group_of.reshape(1, -1), params
        )
        width = query_proj.shape[1]
        modes = factor.shape[0]
        pieces = width // BLOCK
        local = None
        made = 0

        def span(blocks):
            return jnp.exp(-rate * (blocks * float(rows)))

        member_t = member.T

        def grouped(a):
            return split_dot(a, member_t)

        place = lax.axis_index("ctx")
        fwd_cube = end_state
        bwd_cube = head_adjoint
        grad_cube = grouped(local_total)
        state_in = jnp.zeros_like(end_state)
        adjoint_in = jnp.zeros_like(head_adjoint)
        bit = 1
        level = 0
        while bit < count:
            pairs = [(i, i ^ bit) for i in range(count)]
            packed = jnp.concatenate([fwd_cube, bwd_cube, grad_cube], axis=1)
            need = pieces if bit * 2 >= count else min(pieces, level)
            level += 1
            if bit == 1:
                got = lax.ppermute(packed, "ctx", pairs)
            else:
                half = packed.shape[1] // 2
                core = place % 2
                mine = lax.dynamic_slice_in_dim(packed, core * half, half, axis=1)
                got_mine = lax.ppermute(mine, "ctx", pairs)
                if need > made:
                    while made < need:
                        local = local_scans(
                            query_proj, key_proj, value_proj, out_grad, factor, weight, made,
                            local,
                        )
                        made += 1
                    got_mine, local = lax.optimization_barrier((got_mine, local))
                got_other = lax.ppermute(got_mine, "ctx", [(i, i ^ 1) for i in range(count)])
                first = jnp.where(core == 0, got_mine, got_other)
                second = jnp.where(core == 0, got_other, got_mine)
                got = jnp.concatenate([first, second], axis=1)
            got_fwd = got[:, :width]
            got_bwd = got[:, width : 2 * width]
            got_grad = got[:, 2 * width :]
            upper = (place & bit) != 0
            offset = (place % bit).astype(jnp.float32)
            low_fwd = jnp.where(upper, got_fwd, fwd_cube)
            high_fwd = jnp.where(upper, fwd_cube, got_fwd)
            low_bwd = jnp.where(upper, got_bwd, bwd_cube)
            high_bwd = jnp.where(upper, bwd_cube, got_bwd)
            low_grad = jnp.where(upper, got_grad, grad_cube)
            high_grad = jnp.where(upper, grad_cube, got_grad)
            state_in = state_in + jnp.where(upper, span(offset) * got_fwd, 0.0)
            adjoint_in = adjoint_in + jnp.where(upper, 0.0, span(bit - 1 - offset) * got_bwd)
            whole = span(bit)
            grad_cube = (low_grad + high_grad) + grouped((factor * low_fwd) * high_bwd)
            fwd_cube = high_fwd + whole * low_fwd
            bwd_cube = low_bwd + whole * high_bwd
            bit *= 2

        while made < pieces:
            local = local_scans(
                query_proj, key_proj, value_proj, out_grad, factor, weight, made, local
            )
            made += 1
        hyena_out, query_grad, key_grad, value_grad = corrected(
            query_proj, key_proj, value_proj, out_grad, local, factor, weight, state_in, adjoint_in
        )
        filter_grad = grad_cube.T
        filter_update = filter_grad / jnp.sqrt(jnp.mean(filter_grad * filter_grad) + 1e-06)
        return (hyena_out, query_grad, key_grad, value_grad, filter_update)

    return on_device


def solution(mesh):
    placed = (
        P(("groups", "ctx"), None),
        P(("groups", "ctx"), None),
        P(("groups", "ctx"), None),
        P(("groups", "ctx"), None),
        P(),
        P(),
        P(),
    )
    return jax.shard_map(
        make_on_device(mesh.shape["ctx"]),
        mesh=mesh,
        in_specs=placed,
        out_specs=(
            P(("groups", "ctx"), None),
            P(("groups", "ctx"), None),
            P(("groups", "ctx"), None),
            P(("groups", "ctx"), None),
            P("groups", None),
        ),
        check_vma=False,
    )
```

```python
import jax
import jax.numpy as jnp
from jax import lax
from jax.experimental import pallas as pl
from jax.experimental.pallas import tpu as pltpu
from jax.sharding import PartitionSpec as P

BLOCK = 1024
SUB = 256
ROWS = 8
LANE = 128


def carry_kernel(
    q_ref, k_ref, v_ref, g_ref, grp_ref, par_ref,
    xend_ref, head_ref, tot_ref, rate_ref, p_ref, w_ref, mix_ref, up_ref,
):
    f32 = jnp.float32
    bf16 = jnp.bfloat16
    groups = par_ref.shape[1]
    modes = rate_ref.shape[0]
    ids = lax.broadcasted_iota(jnp.int32, (groups, grp_ref.shape[1]), 0)
    member = (ids == grp_ref[...]).astype(bf16)
    par = par_ref[...]
    hi = par.astype(bf16)
    rest = par - hi.astype(f32)
    mid = rest.astype(bf16)
    lo = (rest - mid.astype(f32)).astype(bf16)
    prod = jnp.dot(jnp.concatenate([hi, mid, lo], axis=0), member, preferred_element_type=f32)
    both = 2 * modes
    rate = (prod[0:modes] + prod[both : both + modes]) + prod[2 * both : 2 * both + modes]
    weight = (prod[modes:both] + prod[both + modes : 2 * both]) + prod[2 * both + modes :]
    rate_ref[...] = rate
    w_ref[...] = weight
    p_ref[...] = jnp.exp(-rate)
    mix_ref[...] = (k_ref[...].astype(f32) * v_ref[...].astype(f32)).astype(jnp.bfloat16).astype(f32)
    up_ref[...] = g_ref[...].astype(f32) * q_ref[...].astype(f32)
    rows, width = mix_ref.shape
    chunks = rows // ROWS
    for h in range(width // SUB):
        cols = pl.ds(h * SUB, SUB)
        p = p_ref[:, cols]

        def body(c, carry):
            x, tot, a = carry
            fb = pl.multiple_of(c * ROWS, ROWS)
            bb = pl.multiple_of((chunks - 1 - c) * ROWS, ROWS)
            mt = mix_ref[pl.ds(fb, ROWS), cols]
            ut = up_ref[pl.ds(fb, ROWS), cols]
            ub = up_ref[pl.ds(bb, ROWS), cols]
            for j in range(ROWS):
                x = p * x + mt[j : j + 1, :]
                tot = tot + ut[j : j + 1, :] * x
                jb = ROWS - 1 - j
                a = p * a + ub[jb : jb + 1, :]
            return x, tot, a

        zero = jnp.zeros(p.shape, f32)
        x, tot, a = lax.fori_loop(0, chunks, body, (zero, zero, zero), unroll=2)
        xend_ref[:, cols] = x
        head_ref[:, cols] = a
        tot_ref[:, cols] = tot


def to_modes(src_ref, stage_ref, dst_ref):
    modes, width = src_ref.shape
    lanes = width // LANE
    for c in range(lanes):
        stage_ref[c * modes : (c + 1) * modes, :] = src_ref[:, c * LANE : (c + 1) * LANE]
    for m in range(modes):
        dst_ref[m] = stage_ref[pl.ds(m, lanes, stride=modes), :]


def local_kernel(q_ref, k_ref, v_ref, g_ref, pw_ref, rw_ref, *refs):
    f32 = jnp.float32
    if len(refs) == 11:
        refs = refs[2:]
    filt_out, mg_out, mix_ref, up_ref, filt_ref, mg_ref, stage_ref, p_ref, r_ref = refs
    to_modes(pw_ref, stage_ref, p_ref)
    to_modes(rw_ref, stage_ref, r_ref)
    rows, width = q_ref.shape
    lanes = width // LANE
    for c in range(lanes):
        cols = slice(c * LANE, (c + 1) * LANE)
        band = slice(c * rows, (c + 1) * rows)
        kf = k_ref[:, cols].astype(f32)
        vf = v_ref[:, cols].astype(f32)
        mix_ref[band, :] = (kf * vf).astype(jnp.bfloat16).astype(f32)
        up_ref[band, :] = g_ref[:, cols].astype(f32) * q_ref[:, cols].astype(f32)

    def body(t, carry):
        x, a = carry
        p = p_ref[...]
        r = r_ref[...]
        x = p * x + mix_ref[pl.ds(t, lanes, stride=rows), :][None]
        filt_ref[pl.ds(t, lanes, stride=rows), :] = jnp.sum(r * x, axis=0)
        tb = rows - 1 - t
        a = p * a + up_ref[pl.ds(tb, lanes, stride=rows), :][None]
        mg_ref[pl.ds(tb, lanes, stride=rows), :] = jnp.sum(r * a, axis=0)
        return x, a

    zero = jnp.zeros(p_ref.shape, f32)
    lax.fori_loop(0, rows, body, (zero, zero), unroll=4)
    for c in range(lanes):
        cols = slice(c * LANE, (c + 1) * LANE)
        band = slice(c * rows, (c + 1) * rows)
        filt_out[:, cols] = filt_ref[band, :]
        mg_out[:, cols] = mg_ref[band, :]


def correct_kernel(
    q_ref, k_ref, v_ref, g_ref, fl_ref, ml_ref, pw_ref, rw_ref, sw_ref, bw_ref,
    ho_ref, qg_ref, kg_ref, vg_ref,
    filt_ref, mg_ref, stage_ref, p_ref, r_ref, s_ref, b_ref,
):
    f32 = jnp.float32
    for src, dst in ((pw_ref, p_ref), (rw_ref, r_ref), (sw_ref, s_ref), (bw_ref, b_ref)):
        to_modes(src, stage_ref, dst)
    rows, width = q_ref.shape
    lanes = width // LANE

    def body(t, carry):
        z, w = carry
        p = p_ref[...]
        filt_ref[pl.ds(t, lanes, stride=rows), :] = jnp.sum(z, axis=0)
        tb = rows - 1 - t
        mg_ref[pl.ds(tb, lanes, stride=rows), :] = jnp.sum(w, axis=0)
        return z * p, w * p

    p = p_ref[...]
    r = r_ref[...]
    lax.fori_loop(0, rows, body, ((r * p) * s_ref[...], (r * p) * b_ref[...]), unroll=8)
    for c in range(lanes):
        cols = slice(c * LANE, (c + 1) * LANE)
        band = slice(c * rows, (c + 1) * rows)
        filt = fl_ref[:, cols] + filt_ref[band, :]
        mg = ml_ref[:, cols] + mg_ref[band, :]
        ho_ref[:, cols] = (q_ref[:, cols].astype(f32) * filt).astype(jnp.bfloat16)
        qg_ref[:, cols] = (g_ref[:, cols].astype(f32) * filt).astype(jnp.bfloat16)
        kg_ref[:, cols] = (mg * v_ref[:, cols].astype(f32)).astype(jnp.bfloat16)
        vg_ref[:, cols] = (mg * k_ref[:, cols].astype(f32)).astype(jnp.bfloat16)


def local_carries(query_proj, key_proj, value_proj, out_grad, group_row, params):
    rows, width = query_proj.shape
    modes = params.shape[0] // 2
    big = pl.BlockSpec((rows, BLOCK), lambda i: (0, i))
    small = pl.BlockSpec((modes, BLOCK), lambda i: (0, i))
    row = pl.BlockSpec((1, BLOCK), lambda i: (0, i))
    whole = pl.BlockSpec(params.shape, lambda i: (0, 0))
    return pl.pallas_call(
        carry_kernel,
        grid=(width // BLOCK,),
        in_specs=[big, big, big, big, row, whole],
        out_specs=[small] * 6,
        out_shape=[jax.ShapeDtypeStruct((modes, width), jnp.float32)] * 6,
        scratch_shapes=[pltpu.VMEM((rows, BLOCK), jnp.float32)] * 2,
    )(query_proj, key_proj, value_proj, out_grad, group_row, params)


def local_scans(query_proj, key_proj, value_proj, out_grad, factor, weight, first, previous):
    rows, width = query_proj.shape
    modes = factor.shape[0]
    lanes = BLOCK // LANE
    big = pl.BlockSpec((rows, BLOCK), lambda i: (0, i + first))
    small = pl.BlockSpec((modes, BLOCK), lambda i: (0, i + first))
    operands = [query_proj, key_proj, value_proj, out_grad, factor, weight]
    specs = [big, big, big, big, small, small]
    aliases = {}
    if previous is not None:
        operands += list(previous)
        specs += [pl.BlockSpec(memory_space=pl.ANY)] * 2
        aliases = {6: 0, 7: 1}
    return pl.pallas_call(
        local_kernel,
        grid=(1,),
        in_specs=specs,
        out_specs=[big, big],
        out_shape=[jax.ShapeDtypeStruct((rows, width), jnp.float32)] * 2,
        scratch_shapes=[pltpu.VMEM((lanes * rows, LANE), jnp.float32)] * 4
        + [pltpu.VMEM((lanes * modes, LANE), jnp.float32)]
        + [pltpu.VMEM((modes, lanes, LANE), jnp.float32)] * 2,
        input_output_aliases=aliases,
    )(*operands)


def corrected(query_proj, key_proj, value_proj, out_grad, local, factor, weight, state_in, adjoint_in):
    rows, width = query_proj.shape
    modes = factor.shape[0]
    lanes = BLOCK // LANE
    big = pl.BlockSpec((rows, BLOCK), lambda i: (0, i))
    small = pl.BlockSpec((modes, BLOCK), lambda i: (0, i))
    out_big = jax.ShapeDtypeStruct((rows, width), jnp.bfloat16)
    return pl.pallas_call(
        correct_kernel,
        grid=(width // BLOCK,),
        in_specs=[big] * 6 + [small] * 4,
        out_specs=[big, big, big, big],
        out_shape=[out_big] * 4,
        scratch_shapes=[pltpu.VMEM((lanes * rows, LANE), jnp.float32)] * 2
        + [pltpu.VMEM((lanes * modes, LANE), jnp.float32)]
        + [pltpu.VMEM((modes, lanes, LANE), jnp.float32)] * 4,
    )(query_proj, key_proj, value_proj, out_grad, *local, factor, weight, state_in, adjoint_in)


def split_dot(a, member):
    bf16 = jnp.bfloat16
    top = lax.reduce_precision(a, exponent_bits=8, mantissa_bits=7)
    rest = a - top
    middle = lax.reduce_precision(rest, exponent_bits=8, mantissa_bits=7)
    hi = top.astype(bf16)
    mid = middle.astype(bf16)
    lo = (rest - middle).astype(bf16)
    rows = a.shape[0]
    out = jnp.dot(jnp.concatenate([hi, mid, lo], axis=0), member, preferred_element_type=jnp.float32)
    return (out[:rows] + out[rows : 2 * rows]) + out[2 * rows :]


def make_on_device(count):
    def on_device(query_proj, key_proj, value_proj, out_grad, decay_rate, residue, group_of):
        rows = query_proj.shape[0]
        group_count = decay_rate.shape[0]
        member = (group_of[None, :] == jnp.arange(group_count, dtype=jnp.int32)[:, None]).astype(
            jnp.bfloat16
        )
        params = jnp.concatenate([decay_rate.T, residue.T], axis=0)
        end_state, head_adjoint, local_total, rate, factor, weight = local_carries(
            query_proj, key_proj, value_proj, out_grad, group_of.reshape(1, -1), params
        )
        width = query_proj.shape[1]
        modes = factor.shape[0]
        pieces = width // BLOCK
        local = None
        made = 0

        def span(blocks):
            return jnp.exp(-rate * (blocks * float(rows)))

        member_t = member.T

        def grouped(a):
            return split_dot(a, member_t)

        place = lax.axis_index("ctx")
        fwd_cube = end_state
        bwd_cube = head_adjoint
        grad_cube = grouped(local_total)
        state_in = jnp.zeros_like(end_state)
        adjoint_in = jnp.zeros_like(head_adjoint)
        bit = 1
        level = 0
        while bit < count:
            pairs = [(i, i ^ bit) for i in range(count)]
            packed = jnp.concatenate([fwd_cube, bwd_cube, grad_cube], axis=1)
            need = pieces if bit * 2 >= count else min(pieces, level)
            level += 1
            if bit == 1:
                got = lax.ppermute(packed, "ctx", pairs)
            else:
                half = packed.shape[1] // 2
                core = place % 2
                mine = lax.dynamic_slice_in_dim(packed, core * half, half, axis=1)
                got_mine = lax.ppermute(mine, "ctx", pairs)
                if need > made:
                    while made < need:
                        local = local_scans(
                            query_proj, key_proj, value_proj, out_grad, factor, weight, made,
                            local,
                        )
                        made += 1
                    got_mine, local = lax.optimization_barrier((got_mine, local))
                got_other = lax.ppermute(got_mine, "ctx", [(i, i ^ 1) for i in range(count)])
                first = jnp.where(core == 0, got_mine, got_other)
                second = jnp.where(core == 0, got_other, got_mine)
                got = jnp.concatenate([first, second], axis=1)
            got_fwd = got[:, :width]
            got_bwd = got[:, width : 2 * width]
            got_grad = got[:, 2 * width :]
            upper = (place & bit) != 0
            offset = (place % bit).astype(jnp.float32)
            low_fwd = jnp.where(upper, got_fwd, fwd_cube)
            high_fwd = jnp.where(upper, fwd_cube, got_fwd)
            low_bwd = jnp.where(upper, got_bwd, bwd_cube)
            high_bwd = jnp.where(upper, bwd_cube, got_bwd)
            low_grad = jnp.where(upper, got_grad, grad_cube)
            high_grad = jnp.where(upper, grad_cube, got_grad)
            state_in = state_in + jnp.where(upper, span(offset) * got_fwd, 0.0)
            adjoint_in = adjoint_in + jnp.where(upper, 0.0, span(bit - 1 - offset) * got_bwd)
            whole = span(bit)
            grad_cube = (low_grad + high_grad) + grouped((factor * low_fwd) * high_bwd)
            fwd_cube = high_fwd + whole * low_fwd
            bwd_cube = low_bwd + whole * high_bwd
            bit *= 2

        while made < pieces:
            local = local_scans(
                query_proj, key_proj, value_proj, out_grad, factor, weight, made, local
            )
            made += 1
        hyena_out, query_grad, key_grad, value_grad = corrected(
            query_proj, key_proj, value_proj, out_grad, local, factor, weight, state_in, adjoint_in
        )
        filter_grad = grad_cube.T
        filter_update = filter_grad / jnp.sqrt(jnp.mean(filter_grad * filter_grad) + 1e-06)
        return (hyena_out, query_grad, key_grad, value_grad, filter_update)

    return on_device


def solution(mesh):
    placed = (
        P(("groups", "ctx"), None),
        P(("groups", "ctx"), None),
        P(("groups", "ctx"), None),
        P(("groups", "ctx"), None),
        P(),
        P(),
        P(),
    )
    return jax.shard_map(
        make_on_device(mesh.shape["ctx"]),
        mesh=mesh,
        in_specs=placed,
        out_specs=(
            P(("groups", "ctx"), None),
            P(("groups", "ctx"), None),
            P(("groups", "ctx"), None),
            P(("groups", "ctx"), None),
            P("groups", None),
        ),
        check_vma=False,
    )
```
